512 devices in a mesh: band: 256 (over x_hi, y, z, core), pair: 2 (over x_lo).
Axes of the slice: x: 4 (x_hi: 2, x_lo: 2; x = x_hi * 2 + x_lo), y: 4, z: 16, core: 2. Of those that a mesh axis runs over, the one named last changes fastest.
Arguments:
- frame1: bfloat16 [256, 768, 256], P('band', 'pair'), parts along dimension 1, may hold values from -6 to 6, as said below
- frame2: bfloat16 [256, 768, 256], P('band', 'pair'), parts along dimension 1, may hold values from -6 to 6, as said below
- context: bfloat16 [256, 768, 128], P('band', 'pair'), parts along dimension 1, may hold values from -6 to 6
- hidden_init: bfloat16 [256, 768, 128], P('band', 'pair'), parts along dimension 1, may hold values from -1 to 1
- offsets: int32 [2, 256, 768], P(None, 'band', 'pair'), parts along dimension 2, may hold values from -4 to 4
- w_motion: float32 [3, 128], replicated, may hold values from -3.5 to 3.5
- w_row: bfloat16 [5, 384, 384], replicated, may hold values from -0.125 to 0.125
- w_col: bfloat16 [5, 384, 384], replicated, may hold values from -0.125 to 0.125
Outputs:
- hidden: float32 [256, 768, 128], P('band', 'pair'), parts along dimension 1
- flow: float32 [2, 256, 768], P(None, 'band', 'pair'), parts along dimension 2
The draws below stay inside these ranges and needn't reach their ends.
There are 2 independent parts, one for each index of `pair`. The reference program is written for one: setup_inputs(seed, part) draws one part's arguments, and reference() takes and returns one part's arrays. A program takes and returns all parts, laid end to end along the dimension named above; an argument that names none is the same for every part. Nothing has to cross between parts.
Inputs may be any that keep to these rules, and one draw needn't show every extreme that they name: `frame1`: feature vectors. `frame2`: feature vectors. offsets[0] and offsets[1] are each pixel's teacher lookup offsets, in rows and in strips.
All inputs are finite; a program needn't handle non-finite values.
Results may differ from the reference program's by a relative error of at most 0.0041.
Values may be sent and summed in bfloat16 or wider, within the bound.
No kernel may reach another device: no remote copies, remote signals or barrier semaphores. Data moves between devices by JAX's collectives and lax.ppermute only.
A program may use at most 64 MiB of HBM per device.

```python
import math
import jax
import jax.numpy as jnp
from jax import lax

C = 256
HID = 128
CTX = 128
MOTION = 128
WIDTH = 384
ITERS = 2
NROWS = 256


def base_field(key, spread):
    return jnp.clip(spread * jax.random.normal(key, (NROWS, WIDTH, C), jnp.float32), -6.0, 6.0)


def displacement(key):
    key_pair = jax.random.split(jax.random.fold_in(key, 3), 2)
    row_move = jax.random.randint(key_pair[0], (), -4, 5).astype(jnp.int32)
    col_move = jax.random.randint(key_pair[1], (), -12, 13).astype(jnp.int32)
    return (row_move, col_move)


def draw_frame1(key, part):
    feature_field = base_field(jax.random.fold_in(key, 1), 1.5)
    return feature_field.astype(jnp.bfloat16)


def draw_frame2(key, part):
    source_field = base_field(jax.random.fold_in(key, 1), 1.5)
    row_move, col_move = displacement(key)
    row_index = ((jnp.arange(NROWS, dtype=jnp.int32) - row_move) % NROWS).astype(jnp.int32)
    col_index = ((jnp.arange(WIDTH, dtype=jnp.int32) - col_move) % WIDTH).astype(jnp.int32)
    moved_field = jnp.take(jnp.take(source_field, row_index, axis=0), col_index, axis=1)
    noise_field = base_field(jax.random.fold_in(key, 2), 0.4)
    feature_field = jnp.clip(moved_field + noise_field, -6.0, 6.0)
    return feature_field.astype(jnp.bfloat16)


def place_ends(entries, own_key, low, top_value):
    longest = entries.shape.index(max(entries.shape))
    spots = []
    for shift in (0, 1):
        where = [jax.random.randint(jax.random.fold_in(own_key, axis), (), 0, length) for axis, length in enumerate(entries.shape)]
        where[longest] = (where[longest] + shift) % entries.shape[longest]
        spots.append(tuple(where))
    return entries.at[spots[0]].set(low).at[spots[1]].set(top_value)


def shard_levels(stream_key, dims, pieces, smallest, high):
    def one(dim, blocks):
        draws = jax.random.uniform(jax.random.fold_in(jax.random.fold_in(stream_key, 6), dim), (blocks,), jnp.float32, smallest / len(pieces), high / len(pieces))
        return jnp.repeat(jnp.exp(draws), dims[dim] // blocks).reshape((-1,) + (1,) * (len(dims) - dim - 1))

    gain = one(*pieces[0])
    for cut in pieces[1:]:
        gain = gain * one(*cut)
    return gain


def noise(key, extent, scale, bound, cuts=(), kind=jnp.bfloat16):
    result = scale * jax.random.normal(key, extent, jnp.float32)
    if cuts:
        result = result * shard_levels(key, extent, cuts, -0.22, 0.18)
    return jnp.clip(result, -bound, bound).astype(kind)


def setup_inputs(seed: int = 0, part: int = 0) -> dict:
    seeds = jax.random.split(jax.random.key(seed), 9)
    own_keys = jax.random.split(jax.random.fold_in(seeds[8], part), 9)
    frame1 = draw_frame1(jax.random.fold_in(jax.random.fold_in(seeds[8], part), 71), part)
    frame2 = draw_frame2(jax.random.fold_in(jax.random.fold_in(seeds[8], part), 71), part)
    context = noise(own_keys[2], (NROWS, WIDTH, CTX), 1.0, 6.0, ((0, 256),))
    hidden_init = jnp.clip(jax.random.uniform(own_keys[3], (NROWS, WIDTH, HID), jnp.float32, -1.0, 1.0) * shard_levels(own_keys[3], (NROWS, WIDTH, HID), ((0, 256),), -0.4, 0.0), -1.0, 1.0).astype(jnp.bfloat16)
    offsets = place_ends(jax.random.randint(own_keys[4], (2, NROWS, WIDTH), -4, 5), jax.random.fold_in(own_keys[4], 1), -4, 4).astype(jnp.int32)
    w_motion = noise(seeds[5], (3, MOTION), 3 ** -0.5, 3.5, (), jnp.float32)
    w_row = noise(seeds[6], (5, HID + CTX + MOTION, 3 * HID), (5 * (HID + CTX + MOTION)) ** -0.5, 0.125)
    w_col = noise(seeds[7], (5, HID + CTX + MOTION, 3 * HID), (5 * (HID + CTX + MOTION)) ** -0.5, 0.125)
    return {"frame1": frame1, "frame2": frame2, "context": context, "hidden_init": hidden_init, "offsets": offsets, "w_motion": w_motion, "w_row": w_row, "w_col": w_col}


def pool_strips(frame2):
    band_rows, image_width, channels = frame2.shape
    blocks = frame2.astype(jnp.float32).reshape(band_rows, image_width // 8, 8, channels)
    return (lax.optimization_barrier(jnp.sum(blocks, axis=2)) / 2.0).astype(jnp.bfloat16)

def lookup_targets(offsets, row_first, total_rows, image_width):
    band_rows = offsets.shape[1]
    pixel_row = row_first + jnp.arange(band_rows, dtype=jnp.int32)[:, None] + jnp.zeros((1, image_width), jnp.int32)
    pixel_col = jnp.zeros((band_rows, 1), jnp.int32) + jnp.arange(image_width, dtype=jnp.int32)[None, :]
    target_row = pixel_row + offsets[0]
    target_col = pixel_col // 8 + offsets[1]
    inside = (target_row >= 0) & (target_row < total_rows) & (target_col >= 0) & (target_col < image_width // 8)
    target_row = jnp.where(inside, target_row, -1).astype(jnp.int32)
    target_col = jnp.where(inside, target_col, -1).astype(jnp.int32)
    return (target_row, target_col, pixel_row, pixel_col)

def strip_step(state, feature_rows, strip_block, row_zero, total_rows, image_width, target_row, target_col):
    block_rows, grid_cols, channels = strip_block.shape
    scores = jnp.dot(feature_rows, strip_block.reshape(block_rows * grid_cols, channels).T, preferred_element_type=jnp.float32) / math.sqrt(channels)
    running_max, denominator, acc_row, acc_col, lookup = state
    new_max = jnp.maximum(running_max, lax.optimization_barrier(jnp.max(scores, axis=1)))
    shrink = jnp.exp(running_max - new_max)
    exponent = jnp.exp(scores - new_max[:, None]).reshape(-1, block_rows, grid_cols)
    strip_row = (row_zero + jnp.arange(block_rows, dtype=jnp.int32)).astype(jnp.int32)
    column_ids = jnp.arange(grid_cols, dtype=jnp.int32)
    row_centre = strip_row.astype(jnp.float32) / total_rows
    col_centre = ((8 * column_ids).astype(jnp.float32) + 3.5) / image_width
    row_weight = lax.optimization_barrier(jnp.sum(exponent, axis=2))
    col_weight = lax.optimization_barrier(jnp.sum(exponent, axis=1))
    scores_grid = scores.reshape(-1, block_rows, grid_cols)
    hit = (strip_row[None, :, None] == target_row[:, None, None]) & (column_ids[None, None, :] == target_col[:, None, None])
    found = lax.optimization_barrier(jnp.sum(jnp.where(hit, scores_grid, 0.0), axis=(1, 2)))
    return (new_max, denominator * shrink + lax.optimization_barrier(jnp.sum(row_weight, axis=1)), acc_row * shrink + lax.optimization_barrier(jnp.sum(row_weight * row_centre[None, :], axis=1)), acc_col * shrink + lax.optimization_barrier(jnp.sum(col_weight * col_centre[None, :], axis=1)), lookup + found)

def conv_valid(source, weight, conv_axis):
    out_count = source.shape[conv_axis] - 4
    summed = None
    for kernel_tap in range(5):
        tap_slice = lax.slice_in_dim(source, kernel_tap, kernel_tap + out_count, axis=conv_axis)
        tap_term = jnp.dot(tap_slice.reshape(-1, tap_slice.shape[-1]), weight[kernel_tap], preferred_element_type=jnp.float32)
        summed = tap_term if summed is None else summed + tap_term
    out_shape = tuple(tap_slice.shape[:-1]) + (weight.shape[-1],)
    return summed.reshape(out_shape)

def conv_padded(source, weight, conv_axis):
    widths = [(0, 0), (0, 0), (0, 0)]
    widths[conv_axis] = (2, 2)
    return conv_valid(jnp.pad(source, widths), weight, conv_axis)

def gru_pass(hidden, inputs, weight, conv_axis):
    width_h = hidden.shape[-1]
    from_inputs = conv_padded(inputs, weight[:, width_h:, :], conv_axis)
    hidden_half = lax.optimization_barrier(hidden.astype(jnp.bfloat16))
    gate_pair = jax.nn.sigmoid(conv_padded(hidden_half, weight[:, :width_h, :2 * width_h], conv_axis) + from_inputs[..., :2 * width_h])
    update_gate = gate_pair[..., :width_h]
    reset_gate = gate_pair[..., width_h:]
    gated = (reset_gate * hidden_half.astype(jnp.float32)).astype(jnp.bfloat16)
    candidate = jnp.tanh(conv_padded(gated, weight[:, :width_h, 2 * width_h:], conv_axis) + from_inputs[..., 2 * width_h:])
    return (1.0 - update_gate) * hidden + update_gate * candidate

def reference(frame1, frame2, context, hidden_init, offsets, w_motion, w_row, w_col):
    strips = pool_strips(frame2)
    target_row, target_col, pixel_row, pixel_col = lookup_targets(offsets, jnp.zeros((), jnp.int32), NROWS, WIDTH)

    def match_row(args):
        feature_rows, rows_target, cols_target = args
        begin = jnp.full((WIDTH,), -jnp.inf, jnp.float32)
        empty = jnp.zeros((WIDTH,), jnp.float32)
        state = (begin, empty, empty, empty, empty)
        final = strip_step(state, feature_rows, strips, jnp.zeros((), jnp.int32), NROWS, WIDTH, rows_target, cols_target)
        return (final[2] / final[1], final[3] / final[1], final[4])
    moved_row, moved_col, lookup = lax.map(match_row, (frame1, target_row, target_col))
    flow_row = moved_row - pixel_row.astype(jnp.float32) / NROWS
    flow_col = moved_col - pixel_col.astype(jnp.float32) / WIDTH
    motion = jax.nn.relu(flow_row[..., None] * w_motion[0] + flow_col[..., None] * w_motion[1] + lookup[..., None] * w_motion[2]).astype(jnp.bfloat16)
    inputs = jnp.concatenate([context, motion], axis=-1)
    hidden = hidden_init.astype(jnp.float32)
    for iteration in range(ITERS):
        hidden = gru_pass(hidden, inputs, w_row, 1)
        hidden = gru_pass(hidden, inputs, w_col, 0)
    return (hidden, jnp.stack([flow_row, flow_col]))
```

```python
import math

import numpy as np

import jax
import jax.numpy as jnp
from jax import lax
from jax.experimental import pallas as pl
from jax.sharding import PartitionSpec as P

ITERS = 2


def passed_along(array, axis, by):
    count = lax.axis_size(axis)
    pairs = [(i, i + by) for i in range(count) if 0 <= i + by < count]
    return lax.ppermute(array, axis, pairs)


def pool_strips(frame2):
    band_rows, image_width, channels = frame2.shape
    blocks = frame2.astype(jnp.float32).reshape(band_rows, image_width // 8, 8, channels)
    return (jnp.sum(blocks, axis=2) / 2.0).astype(jnp.bfloat16)


def lookup_targets(offsets, row_first, total_rows, image_width):
    band_rows = offsets.shape[1]
    pixel_row = (
        row_first
        + jnp.arange(band_rows, dtype=jnp.int32)[:, None]
        + jnp.zeros((1, image_width), jnp.int32)
    )
    pixel_col = jnp.arange(image_width, dtype=jnp.int32)[None, :]
    target_row = pixel_row + offsets[0]
    target_col = pixel_col // 8 + offsets[1]
    inside = (
        (target_row >= 0)
        & (target_row < total_rows)
        & (target_col >= 0)
        & (target_col < image_width // 8)
    )
    target_row = jnp.where(inside, target_row, -1)
    target_col = jnp.where(inside, target_col, -1)
    return (target_row, target_col, pixel_row, pixel_col)


def strip_step(
    state, feature_rows, strip_block, row_zero, total_rows, image_width, target_row, target_col
):
    block_rows, grid_cols, channels = strip_block.shape
    scores = jnp.dot(
        feature_rows,
        strip_block.reshape(block_rows * grid_cols, channels).T,
        preferred_element_type=jnp.float32,
    ) / math.sqrt(channels)
    running_max, denominator, acc_row, acc_col, lookup = state
    new_max = jnp.maximum(running_max, jnp.max(scores, axis=1))
    shrink = jnp.exp(running_max - new_max)
    exponent = jnp.exp(scores - new_max[:, None]).reshape(-1, block_rows, grid_cols)
    strip_row = row_zero + jnp.arange(block_rows, dtype=jnp.int32)
    column_ids = jnp.arange(grid_cols, dtype=jnp.int32)
    row_centre = strip_row.astype(jnp.float32) / total_rows
    col_centre = ((8 * column_ids).astype(jnp.float32) + 3.5) / image_width
    row_weight = jnp.sum(exponent, axis=2)
    col_weight = jnp.sum(exponent, axis=1)
    scores_grid = scores.reshape(-1, block_rows, grid_cols)
    hit = (strip_row[None, :, None] == target_row[:, None, None]) & (
        column_ids[None, None, :] == target_col[:, None, None]
    )
    found = jnp.sum(jnp.where(hit, scores_grid, 0.0), axis=(1, 2))
    return (
        new_max,
        denominator * shrink + jnp.sum(row_weight, axis=1),
        acc_row * shrink + jnp.sum(row_weight * row_centre[None, :], axis=1),
        acc_col * shrink + jnp.sum(col_weight * col_centre[None, :], axis=1),
        lookup + found,
    )


def conv_valid(source, weight, conv_axis):
    out_count = source.shape[conv_axis] - 4
    summed = None
    for kernel_tap in range(5):
        tap_slice = lax.slice_in_dim(source, kernel_tap, kernel_tap + out_count, axis=conv_axis)
        tap_term = jnp.dot(
            tap_slice.reshape(-1, tap_slice.shape[-1]),
            weight[kernel_tap],
            preferred_element_type=jnp.float32,
        )
        summed = tap_term if summed is None else summed + tap_term
    out_shape = tuple(tap_slice.shape[:-1]) + (weight.shape[-1],)
    return summed.reshape(out_shape)


def pad_columns(source):
    return jnp.pad(source, ((0, 0), (2, 2), (0, 0)))


def rows_around(source, depth, mover):
    above = [
        mover(source, offset)
        for offset in list(range(depth, 0, -1)) + list(range(-1, -depth - 1, -1))
    ]
    return jnp.concatenate(above[:depth] + [source] + above[depth:], axis=0)


def row_pass(hidden, from_inputs, weight):
    width_h = hidden.shape[-1]
    hidden_half = lax.optimization_barrier(hidden.astype(jnp.bfloat16))
    gate_pair = jax.nn.sigmoid(
        conv_valid(pad_columns(hidden_half), weight[:, :width_h, : 2 * width_h], 1)
        + from_inputs[..., : 2 * width_h]
    )
    update_gate = gate_pair[..., :width_h]
    reset_gate = gate_pair[..., width_h:]
    gated = (reset_gate * hidden_half.astype(jnp.float32)).astype(jnp.bfloat16)
    candidate = jnp.tanh(
        conv_valid(pad_columns(gated), weight[:, :width_h, 2 * width_h :], 1)
        + from_inputs[..., 2 * width_h :]
    )
    return (1.0 - update_gate) * hidden + update_gate * candidate


def column_pass_each(hidden, from_inputs, weight):
    width_h = hidden.shape[-1]
    hidden_half = lax.optimization_barrier(hidden.astype(jnp.bfloat16))
    hidden_ext = rows_around(
        hidden_half, 2, lambda source, offset: passed_along(source, "band", offset)
    )
    gate_pair = jax.nn.sigmoid(
        conv_valid(hidden_ext, weight[:, :width_h, : 2 * width_h], 0)
        + from_inputs[..., : 2 * width_h]
    )
    update_gate = gate_pair[..., :width_h]
    reset_gate = gate_pair[..., width_h:]
    gated = (reset_gate * hidden_half.astype(jnp.float32)).astype(jnp.bfloat16)
    gated_ext = rows_around(gated, 2, lambda source, offset: passed_along(source, "band", offset))
    candidate = jnp.tanh(
        conv_valid(gated_ext, weight[:, :width_h, 2 * width_h :], 0)
        + from_inputs[..., 2 * width_h :]
    )
    return (1.0 - update_gate) * hidden + update_gate * candidate


GATHER_BITS = (4, 3, 2, 7, 6, 5, 1, 0)


def match_kernel(f1_ref, s_ref, w_ref, m_in, a_in, m_out, a_out):
    @pl.when(pl.program_id(0) == 0)
    def _():
        m_out[...] = m_in[...]
        a_out[...] = a_in[...]

    scores = lax.dot_general(
        f1_ref[...], s_ref[...], (((1,), (1,)), ((), ())), preferred_element_type=jnp.float32
    ) / 16.0
    m_old = m_out[:, 0:1]
    m_new = jnp.maximum(m_old, jnp.max(scores, axis=1, keepdims=True))
    p = jnp.exp(scores - m_new)
    shrink = jnp.exp(m_old - m_new)
    p_hi = p.astype(jnp.bfloat16)
    p_lo = (p - p_hi.astype(jnp.float32)).astype(jnp.bfloat16)
    w = w_ref[...]
    part = jnp.dot(p_hi, w, preferred_element_type=jnp.float32) + jnp.dot(
        p_lo, w, preferred_element_type=jnp.float32
    )
    a_out[...] = a_out[...] * shrink + part
    m_out[...] = jnp.broadcast_to(m_new, m_out.shape)


def match_block(state, features, block, block_rows, grid_cols):
    count, channels = block.shape
    pixels = features.shape[0]
    tile = min(count, 768)
    strip_row = jnp.repeat(block_rows, grid_cols).astype(jnp.float32)
    strip_col = (jnp.arange(count, dtype=jnp.int32) % grid_cols).astype(jnp.float32)
    weights = jnp.concatenate(
        [
            jnp.ones((count, 1), jnp.float32),
            strip_row[:, None],
            strip_col[:, None],
            jnp.zeros((count, 125), jnp.float32),
        ],
        axis=1,
    ).astype(jnp.bfloat16)
    running_max, acc = state
    return pl.pallas_call(
        match_kernel,
        grid=(count // tile,),
        in_specs=[
            pl.BlockSpec((pixels, channels), lambda i: (0, 0)),
            pl.BlockSpec((tile, channels), lambda i: (i, 0)),
            pl.BlockSpec((tile, 128), lambda i: (i, 0)),
            pl.BlockSpec((pixels, 128), lambda i: (0, 0)),
            pl.BlockSpec((pixels, 128), lambda i: (0, 0)),
        ],
        out_specs=[
            pl.BlockSpec((pixels, 128), lambda i: (0, 0)),
            pl.BlockSpec((pixels, 128), lambda i: (0, 0)),
        ],
        out_shape=[
            jax.ShapeDtypeStruct((pixels, 128), jnp.float32),
            jax.ShapeDtypeStruct((pixels, 128), jnp.float32),
        ],
    )(features, block, weights, running_max, acc)


def deposit_table(bits):
    table = np.zeros((1 << len(bits),), np.int32)
    for q in range(table.shape[0]):
        table[q] = sum(((q >> i) & 1) << b for i, b in enumerate(bits))
    return table


def per_device(frame1, frame2, context, hidden_init, offsets, w_motion, w_row, w_col):
    band_rows, image_width, channels = frame1.shape
    bands = lax.axis_size("band")
    total_rows = band_rows * bands
    band = lax.axis_index("band")
    row_first = band * band_rows
    strips = pool_strips(frame2)
    grid_cols = strips.shape[1]
    target_row, target_col, pixel_row, pixel_col = lookup_targets(
        offsets, row_first, total_rows, image_width
    )
    pixel_count = band_rows * image_width
    features = frame1.reshape(pixel_count, channels)
    deposit = deposit_table(GATHER_BITS)
    state = (
        jnp.full((pixel_count, 128), -jnp.inf, jnp.float32),
        jnp.zeros((pixel_count, 128), jnp.float32),
    )
    held = strips.reshape(band_rows * grid_cols, channels)
    state = match_block(state, features, held, band[None], grid_cols)
    for step, bit in enumerate(GATHER_BITS):
        flip = 1 << bit
        pairs = [(i, i ^ flip) for i in range(bands)]
        got = lax.ppermute(held, "band", pairs)
        got_rows = (band ^ flip) ^ jnp.asarray(deposit[: 1 << step])
        state = match_block(state, features, got, got_rows, grid_cols)
        if step + 1 < len(GATHER_BITS):
            held = jnp.concatenate([held, got], axis=0)
    running_max, acc = state
    denominator = acc[:, 0]
    flow_row = (acc[:, 1] / denominator / total_rows).reshape(
        band_rows, image_width
    ) - pixel_row.astype(jnp.float32) / total_rows
    flow_col = (
        (8.0 * (acc[:, 2] / denominator) + 3.5) / image_width
    ).reshape(band_rows, image_width) - pixel_col.astype(jnp.float32) / image_width
    inverse = np.argsort(deposit).astype(np.int32)
    t_row = target_row.reshape(pixel_count)
    t_col = target_col.reshape(pixel_count)
    valid = t_row >= 0
    place = jnp.asarray(inverse)[jnp.where(valid, t_row ^ band, 0)] * grid_cols + jnp.where(
        valid, t_col, 0
    )
    half = held.shape[0]
    picked = jnp.where(
        (place < half)[:, None],
        jnp.take(held, jnp.minimum(place, half - 1), axis=0),
        jnp.take(got, jnp.maximum(place - half, 0), axis=0),
    )
    found = jnp.sum(
        features.astype(jnp.float32) * picked.astype(jnp.float32), axis=1
    ) / math.sqrt(channels)
    lookup = jnp.where(valid, found, 0.0)
    lookup = lookup.reshape(band_rows, image_width)
    motion = jax.nn.relu(
        flow_row[..., None] * w_motion[0]
        + flow_col[..., None] * w_motion[1]
        + lookup[..., None] * w_motion[2]
    ).astype(jnp.bfloat16)
    inputs = jnp.concatenate([context, motion], axis=-1)
    width_h = hidden_init.shape[-1]
    from_row = conv_valid(pad_columns(inputs), w_row[:, width_h:, :], 1)
    hidden = hidden_init.astype(jnp.float32)
    inputs_ext = rows_around(inputs, 2, lambda source, offset: passed_along(source, "band", offset))
    from_col = conv_valid(inputs_ext, w_col[:, width_h:, :], 0)
    for iteration in range(ITERS):
        hidden = row_pass(hidden, from_row, w_row)
        hidden = column_pass_each(hidden, from_col, w_col)
    return (hidden, jnp.stack([flow_row, flow_col]))


def solution(mesh):
    return jax.shard_map(
        per_device,
        mesh=mesh,
        in_specs=(
            P("band", "pair", None),
            P("band", "pair", None),
            P("band", "pair", None),
            P("band", "pair", None),
            P(None, "band", "pair"),
            P(),
            P(),
            P(),
        ),
        out_specs=(P("band", "pair", None), P(None, "band", "pair")),
        check_vma=False,
    )
```

```python
import math

import numpy as np

import jax
import jax.numpy as jnp
from jax import lax
from jax.experimental import pallas as pl
from jax.sharding import PartitionSpec as P

ITERS = 2


def passed_along(array, axis, by):
    count = lax.axis_size(axis)
    pairs = [(i, i + by) for i in range(count) if 0 <= i + by < count]
    return lax.ppermute(array, axis, pairs)


def pool_strips(frame2):
    band_rows, image_width, channels = frame2.shape
    blocks = frame2.astype(jnp.float32).reshape(band_rows, image_width // 8, 8, channels)
    return (jnp.sum(blocks, axis=2) / 2.0).astype(jnp.bfloat16)


def scaled_strips(frame2, scale):
    band_rows, image_width, channels = frame2.shape
    blocks = frame2.astype(jnp.float32).reshape(band_rows, image_width // 8, 8, channels)
    return (jnp.sum(blocks, axis=2) / (2.0 * scale)).astype(jnp.bfloat16)


def lookup_targets(offsets, row_first, total_rows, image_width):
    band_rows = offsets.shape[1]
    pixel_row = (
        row_first
        + jnp.arange(band_rows, dtype=jnp.int32)[:, None]
        + jnp.zeros((1, image_width), jnp.int32)
    )
    pixel_col = jnp.arange(image_width, dtype=jnp.int32)[None, :]
    target_row = pixel_row + offsets[0]
    target_col = pixel_col // 8 + offsets[1]
    inside = (
        (target_row >= 0)
        & (target_row < total_rows)
        & (target_col >= 0)
        & (target_col < image_width // 8)
    )
    target_row = jnp.where(inside, target_row, -1)
    target_col = jnp.where(inside, target_col, -1)
    return (target_row, target_col, pixel_row, pixel_col)


def strip_step(
    state, feature_rows, strip_block, row_zero, total_rows, image_width, target_row, target_col
):
    block_rows, grid_cols, channels = strip_block.shape
    scores = jnp.dot(
        feature_rows,
        strip_block.reshape(block_rows * grid_cols, channels).T,
        preferred_element_type=jnp.float32,
    ) / math.sqrt(channels)
    running_max, denominator, acc_row, acc_col, lookup = state
    new_max = jnp.maximum(running_max, jnp.max(scores, axis=1))
    shrink = jnp.exp(running_max - new_max)
    exponent = jnp.exp(scores - new_max[:, None]).reshape(-1, block_rows, grid_cols)
    strip_row = row_zero + jnp.arange(block_rows, dtype=jnp.int32)
    column_ids = jnp.arange(grid_cols, dtype=jnp.int32)
    row_centre = strip_row.astype(jnp.float32) / total_rows
    col_centre = ((8 * column_ids).astype(jnp.float32) + 3.5) / image_width
    row_weight = jnp.sum(exponent, axis=2)
    col_weight = jnp.sum(exponent, axis=1)
    scores_grid = scores.reshape(-1, block_rows, grid_cols)
    hit = (strip_row[None, :, None] == target_row[:, None, None]) & (
        column_ids[None, None, :] == target_col[:, None, None]
    )
    found = jnp.sum(jnp.where(hit, scores_grid, 0.0), axis=(1, 2))
    return (
        new_max,
        denominator * shrink + jnp.sum(row_weight, axis=1),
        acc_row * shrink + jnp.sum(row_weight * row_centre[None, :], axis=1),
        acc_col * shrink + jnp.sum(col_weight * col_centre[None, :], axis=1),
        lookup + found,
    )


def conv_valid(source, weight, conv_axis):
    out_count = source.shape[conv_axis] - 4
    summed = None
    for kernel_tap in range(5):
        tap_slice = lax.slice_in_dim(source, kernel_tap, kernel_tap + out_count, axis=conv_axis)
        tap_term = jnp.dot(
            tap_slice.reshape(-1, tap_slice.shape[-1]),
            weight[kernel_tap],
            preferred_element_type=jnp.float32,
        )
        summed = tap_term if summed is None else summed + tap_term
    out_shape = tuple(tap_slice.shape[:-1]) + (weight.shape[-1],)
    return summed.reshape(out_shape)


def pad_columns(source):
    return jnp.pad(source, ((0, 0), (2, 2), (0, 0)))


def rows_around(source, depth, mover):
    above = [
        mover(source, offset)
        for offset in list(range(depth, 0, -1)) + list(range(-1, -depth - 1, -1))
    ]
    return jnp.concatenate(above[:depth] + [source] + above[depth:], axis=0)


def row_pass(hidden, from_inputs, weight):
    width_h = hidden.shape[-1]
    hidden_half = lax.optimization_barrier(hidden.astype(jnp.bfloat16))
    gate_pair = jax.nn.sigmoid(
        conv_valid(pad_columns(hidden_half), weight[:, :width_h, : 2 * width_h], 1)
        + from_inputs[..., : 2 * width_h]
    )
    update_gate = gate_pair[..., :width_h]
    reset_gate = gate_pair[..., width_h:]
    gated = (reset_gate * hidden_half.astype(jnp.float32)).astype(jnp.bfloat16)
    candidate = jnp.tanh(
        conv_valid(pad_columns(gated), weight[:, :width_h, 2 * width_h :], 1)
        + from_inputs[..., 2 * width_h :]
    )
    return (1.0 - update_gate) * hidden + update_gate * candidate


def column_pass_each(hidden, from_inputs, weight):
    width_h = hidden.shape[-1]
    hidden_half = lax.optimization_barrier(hidden.astype(jnp.bfloat16))
    hidden_ext = rows_around(
        hidden_half, 2, lambda source, offset: passed_along(source, "band", offset)
    )
    gate_pair = jax.nn.sigmoid(
        conv_valid(hidden_ext, weight[:, :width_h, : 2 * width_h], 0)
        + from_inputs[..., : 2 * width_h]
    )
    update_gate = gate_pair[..., :width_h]
    reset_gate = gate_pair[..., width_h:]
    gated = (reset_gate * hidden_half.astype(jnp.float32)).astype(jnp.bfloat16)
    gated_ext = rows_around(gated, 2, lambda source, offset: passed_along(source, "band", offset))
    candidate = jnp.tanh(
        conv_valid(gated_ext, weight[:, :width_h, 2 * width_h :], 0)
        + from_inputs[..., 2 * width_h :]
    )
    return (1.0 - update_gate) * hidden + update_gate * candidate


GATHER_BITS = (4, 3, 2, 7, 6, 5, 1, 0)


def match_kernel(f1_ref, s_ref, w_ref, m_in, a_in, m_out, a_out):
    @pl.when(pl.program_id(0) == 0)
    def _():
        m_out[...] = m_in[...]
        a_out[...] = a_in[...]

    scores = lax.dot_general(
        f1_ref[...], s_ref[...], (((1,), (1,)), ((), ())), preferred_element_type=jnp.float32
    )
    m_old = m_out[:, 0:1]
    m_new = jnp.maximum(m_old, jnp.max(scores, axis=1, keepdims=True))
    p = jnp.exp(scores - m_new)
    shrink = jnp.exp(m_old - m_new)
    p_hi = p.astype(jnp.bfloat16)
    p_lo = (p - p_hi.astype(jnp.float32)).astype(jnp.bfloat16)
    w = w_ref[...]
    part = jnp.dot(p_hi, w, preferred_element_type=jnp.float32) + jnp.dot(
        p_lo, w, preferred_element_type=jnp.float32
    )
    a_out[...] = a_out[...] * shrink + part
    m_out[...] = jnp.broadcast_to(m_new, m_out.shape)


def match_block(state, features, block, block_rows, grid_cols):
    count, channels = block.shape
    pixels = features.shape[0]
    tile = min(count, 768)
    strip_row = jnp.repeat(block_rows, grid_cols).astype(jnp.float32)
    strip_col = (jnp.arange(count, dtype=jnp.int32) % grid_cols).astype(jnp.float32)
    weights = jnp.concatenate(
        [
            jnp.ones((count, 1), jnp.float32),
            strip_row[:, None],
            strip_col[:, None],
            jnp.zeros((count, 125), jnp.float32),
        ],
        axis=1,
    ).astype(jnp.bfloat16)
    running_max, acc = state
    return pl.pallas_call(
        match_kernel,
        grid=(count // tile,),
        in_specs=[
            pl.BlockSpec((pixels, channels), lambda i: (0, 0)),
            pl.BlockSpec((tile, channels), lambda i: (i, 0)),
            pl.BlockSpec((tile, 128), lambda i: (i, 0)),
            pl.BlockSpec((pixels, 128), lambda i: (0, 0)),
            pl.BlockSpec((pixels, 128), lambda i: (0, 0)),
        ],
        out_specs=[
            pl.BlockSpec((pixels, 128), lambda i: (0, 0)),
            pl.BlockSpec((pixels, 128), lambda i: (0, 0)),
        ],
        out_shape=[
            jax.ShapeDtypeStruct((pixels, 128), jnp.float32),
            jax.ShapeDtypeStruct((pixels, 128), jnp.float32),
        ],
        cost_estimate=pl.CostEstimate(
            flops=2 * pixels * count * (channels + 256),
            transcendentals=pixels * count,
            bytes_accessed=2 * count * (channels + 128) + 2 * pixels * channels + 16 * pixels * 128,
        ),
    )(features, block, weights, running_max, acc)


def deposit_table(bits):
    table = np.zeros((1 << len(bits),), np.int32)
    for q in range(table.shape[0]):
        table[q] = sum(((q >> i) & 1) << b for i, b in enumerate(bits))
    return table


def per_device(frame1, frame2, context, hidden_init, offsets, w_motion, w_row, w_col):
    band_rows, image_width, channels = frame1.shape
    bands = lax.axis_size("band")
    total_rows = band_rows * bands
    band = lax.axis_index("band")
    row_first = band * band_rows
    strips = scaled_strips(frame2, math.sqrt(channels))
    grid_cols = strips.shape[1]
    target_row, target_col, pixel_row, pixel_col = lookup_targets(
        offsets, row_first, total_rows, image_width
    )
    pixel_count = band_rows * image_width
    features = frame1.reshape(pixel_count, channels)
    deposit = deposit_table(GATHER_BITS)
    state = (
        jnp.full((pixel_count, 128), -jnp.inf, jnp.float32),
        jnp.zeros((pixel_count, 128), jnp.float32),
    )
    held = strips.reshape(band_rows * grid_cols, channels)
    state = match_block(state, features, held, band[None], grid_cols)
    for step, bit in enumerate(GATHER_BITS):
        flip = 1 << bit
        pairs = [(i, i ^ flip) for i in range(bands)]
        got = lax.ppermute(held, "band", pairs)
        got_rows = (band ^ flip) ^ jnp.asarray(deposit[: 1 << step])
        settled = state
        state = match_block(state, features, got, got_rows, grid_cols)
        if step + 1 < len(GATHER_BITS):
            held = jnp.concatenate([held, got], axis=0)
            held, settled = lax.optimization_barrier((held, settled))
    running_max, acc = state
    denominator = acc[:, 0]
    flow_row = (acc[:, 1] / denominator / total_rows).reshape(
        band_rows, image_width
    ) - pixel_row.astype(jnp.float32) / total_rows
    flow_col = (
        (8.0 * (acc[:, 2] / denominator) + 3.5) / image_width
    ).reshape(band_rows, image_width) - pixel_col.astype(jnp.float32) / image_width
    inverse = np.argsort(deposit).astype(np.int32)
    t_row = target_row.reshape(pixel_count)
    t_col = target_col.reshape(pixel_count)
    valid = t_row >= 0
    place = jnp.asarray(inverse)[jnp.where(valid, t_row ^ band, 0)] * grid_cols + jnp.where(
        valid, t_col, 0
    )
    half = held.shape[0]
    picked = jnp.where(
        (place < half)[:, None],
        jnp.take(held, jnp.minimum(place, half - 1), axis=0),
        jnp.take(got, jnp.maximum(place - half, 0), axis=0),
    )
    found = jnp.sum(features.astype(jnp.float32) * picked.astype(jnp.float32), axis=1)
    lookup = jnp.where(valid, found, 0.0)
    lookup = lookup.reshape(band_rows, image_width)
    motion = jax.nn.relu(
        flow_row[..., None] * w_motion[0]
        + flow_col[..., None] * w_motion[1]
        + lookup[..., None] * w_motion[2]
    ).astype(jnp.bfloat16)
    inputs = jnp.concatenate([context, motion], axis=-1)
    width_h = hidden_init.shape[-1]
    from_row = conv_valid(pad_columns(inputs), w_row[:, width_h:, :], 1)
    hidden = hidden_init.astype(jnp.float32)
    inputs_ext = rows_around(inputs, 2, lambda source, offset: passed_along(source, "band", offset))
    from_col = conv_valid(inputs_ext, w_col[:, width_h:, :], 0)
    for iteration in range(ITERS):
        hidden = row_pass(hidden, from_row, w_row)
        hidden = column_pass_each(hidden, from_col, w_col)
    return (hidden, jnp.stack([flow_row, flow_col]))


def solution(mesh):
    return jax.shard_map(
        per_device,
        mesh=mesh,
        in_specs=(
            P("band", "pair", None),
            P("band", "pair", None),
            P("band", "pair", None),
            P("band", "pair", None),
            P(None, "band", "pair"),
            P(),
            P(),
            P(),
        ),
        out_specs=(P("band", "pair", None), P(None, "band", "pair")),
        check_vma=False,
    )
```

```python
import math

import numpy as np

import jax
import jax.numpy as jnp
from jax import lax
from jax.experimental import pallas as pl
from jax.sharding import PartitionSpec as P

ITERS = 2


def passed_along(array, axis, by):
    count = lax.axis_size(axis)
    pairs = [(i, i + by) for i in range(count) if 0 <= i + by < count]
    return lax.ppermute(array, axis, pairs)


def pool_strips(frame2):
    band_rows, image_width, channels = frame2.shape
    blocks = frame2.astype(jnp.float32).reshape(band_rows, image_width // 8, 8, channels)
    return (jnp.sum(blocks, axis=2) / 2.0).astype(jnp.bfloat16)


def scaled_strips(frame2, scale):
    band_rows, image_width, channels = frame2.shape
    blocks = frame2.astype(jnp.float32).reshape(band_rows, image_width // 8, 8, channels)
    return (jnp.sum(blocks, axis=2) / (2.0 * scale)).astype(jnp.bfloat16)


def lookup_targets(offsets, row_first, total_rows, image_width):
    band_rows = offsets.shape[1]
    pixel_row = (
        row_first
        + jnp.arange(band_rows, dtype=jnp.int32)[:, None]
        + jnp.zeros((1, image_width), jnp.int32)
    )
    pixel_col = jnp.arange(image_width, dtype=jnp.int32)[None, :]
    target_row = pixel_row + offsets[0]
    target_col = pixel_col // 8 + offsets[1]
    inside = (
        (target_row >= 0)
        & (target_row < total_rows)
        & (target_col >= 0)
        & (target_col < image_width // 8)
    )
    target_row = jnp.where(inside, target_row, -1)
    target_col = jnp.where(inside, target_col, -1)
    return (target_row, target_col, pixel_row, pixel_col)


def strip_step(
    state, feature_rows, strip_block, row_zero, total_rows, image_width, target_row, target_col
):
    block_rows, grid_cols, channels = strip_block.shape
    scores = jnp.dot(
        feature_rows,
        strip_block.reshape(block_rows * grid_cols, channels).T,
        preferred_element_type=jnp.float32,
    ) / math.sqrt(channels)
    running_max, denominator, acc_row, acc_col, lookup = state
    new_max = jnp.maximum(running_max, jnp.max(scores, axis=1))
    shrink = jnp.exp(running_max - new_max)
    exponent = jnp.exp(scores - new_max[:, None]).reshape(-1, block_rows, grid_cols)
    strip_row = row_zero + jnp.arange(block_rows, dtype=jnp.int32)
    column_ids = jnp.arange(grid_cols, dtype=jnp.int32)
    row_centre = strip_row.astype(jnp.float32) / total_rows
    col_centre = ((8 * column_ids).astype(jnp.float32) + 3.5) / image_width
    row_weight = jnp.sum(exponent, axis=2)
    col_weight = jnp.sum(exponent, axis=1)
    scores_grid = scores.reshape(-1, block_rows, grid_cols)
    hit = (strip_row[None, :, None] == target_row[:, None, None]) & (
        column_ids[None, None, :] == target_col[:, None, None]
    )
    found = jnp.sum(jnp.where(hit, scores_grid, 0.0), axis=(1, 2))
    return (
        new_max,
        denominator * shrink + jnp.sum(row_weight, axis=1),
        acc_row * shrink + jnp.sum(row_weight * row_centre[None, :], axis=1),
        acc_col * shrink + jnp.sum(col_weight * col_centre[None, :], axis=1),
        lookup + found,
    )


def conv_valid(source, weight, conv_axis):
    window = (5, 1) if conv_axis == 0 else (1, 5)
    kernel = weight.reshape(window + weight.shape[1:])
    lhs = source[None] if source.ndim == 3 else source
    out = lax.conv_general_dilated(
        lhs,
        kernel,
        (1, 1),
        "VALID",
        dimension_numbers=("NHWC", "HWIO", "NHWC"),
        preferred_element_type=jnp.float32,
    )
    return out[0]


def pad_columns(source):
    return jnp.pad(source, ((0, 0), (2, 2), (0, 0)))


def rows_around(source, depth, mover):
    above = [
        mover(source, offset)
        for offset in list(range(depth, 0, -1)) + list(range(-1, -depth - 1, -1))
    ]
    return jnp.concatenate(above[:depth] + [source] + above[depth:], axis=0)


def row_pass(hidden, from_inputs, weight):
    width_h = hidden.shape[-1]
    hidden_half = lax.optimization_barrier(hidden.astype(jnp.bfloat16))
    gate_pair = jax.nn.sigmoid(
        conv_valid(pad_columns(hidden_half), weight[:, :width_h, : 2 * width_h], 1)
        + from_inputs[..., : 2 * width_h]
    )
    update_gate = gate_pair[..., :width_h]
    reset_gate = gate_pair[..., width_h:]
    gated = (reset_gate * hidden_half.astype(jnp.float32)).astype(jnp.bfloat16)
    candidate = jnp.tanh(
        conv_valid(pad_columns(gated), weight[:, :width_h, 2 * width_h :], 1)
        + from_inputs[..., 2 * width_h :]
    )
    return (1.0 - update_gate) * hidden + update_gate * candidate


def column_pass_each(hidden, from_inputs, weight):
    width_h = hidden.shape[-1]
    hidden_half = lax.optimization_barrier(hidden.astype(jnp.bfloat16))
    hidden_ext = rows_around(
        hidden_half, 2, lambda source, offset: passed_along(source, "band", offset)
    )
    gate_pair = jax.nn.sigmoid(
        conv_valid(hidden_ext, weight[:, :width_h, : 2 * width_h], 0)
        + from_inputs[..., : 2 * width_h]
    )
    update_gate = gate_pair[..., :width_h]
    reset_gate = gate_pair[..., width_h:]
    gated = (reset_gate * hidden_half.astype(jnp.float32)).astype(jnp.bfloat16)
    gated_ext = rows_around(gated, 2, lambda source, offset: passed_along(source, "band", offset))
    candidate = jnp.tanh(
        conv_valid(gated_ext, weight[:, :width_h, 2 * width_h :], 0)
        + from_inputs[..., 2 * width_h :]
    )
    return (1.0 - update_gate) * hidden + update_gate * candidate


GATHER_BITS = (4, 3, 2, 7, 6, 5, 1, 0)


def match_kernel(f1_ref, s_ref, w_ref, m_in, a_in, m_out, a_out):
    @pl.when(pl.program_id(0) == 0)
    def _():
        m_out[...] = m_in[...]
        a_out[...] = a_in[...]

    scores = lax.dot_general(
        f1_ref[...], s_ref[...], (((1,), (1,)), ((), ())), preferred_element_type=jnp.float32
    )
    m_old = m_out[:, 0:1]
    m_new = jnp.maximum(m_old, jnp.max(scores, axis=1, keepdims=True))
    p = jnp.exp(scores - m_new)
    shrink = jnp.exp(m_old - m_new)
    p_hi = p.astype(jnp.bfloat16)
    p_lo = (p - p_hi.astype(jnp.float32)).astype(jnp.bfloat16)
    w = w_ref[...]
    part = jnp.dot(p_hi, w, preferred_element_type=jnp.float32) + jnp.dot(
        p_lo, w, preferred_element_type=jnp.float32
    )
    a_out[...] = a_out[...] * shrink + part
    m_out[...] = jnp.broadcast_to(m_new, m_out.shape)


def match_block(state, features, block, block_rows, grid_cols):
    count, channels = block.shape
    pixels = features.shape[0]
    tile = min(count, 768)
    strip_row = jnp.repeat(block_rows, grid_cols).astype(jnp.float32)
    strip_col = (jnp.arange(count, dtype=jnp.int32) % grid_cols).astype(jnp.float32)
    weights = jnp.concatenate(
        [
            jnp.ones((count, 1), jnp.float32),
            strip_row[:, None],
            strip_col[:, None],
            jnp.zeros((count, 125), jnp.float32),
        ],
        axis=1,
    ).astype(jnp.bfloat16)
    running_max, acc = state
    return pl.pallas_call(
        match_kernel,
        grid=(count // tile,),
        in_specs=[
            pl.BlockSpec((pixels, channels), lambda i: (0, 0)),
            pl.BlockSpec((tile, channels), lambda i: (i, 0)),
            pl.BlockSpec((tile, 128), lambda i: (i, 0)),
            pl.BlockSpec((pixels, 128), lambda i: (0, 0)),
            pl.BlockSpec((pixels, 128), lambda i: (0, 0)),
        ],
        out_specs=[
            pl.BlockSpec((pixels, 128), lambda i: (0, 0)),
            pl.BlockSpec((pixels, 128), lambda i: (0, 0)),
        ],
        out_shape=[
            jax.ShapeDtypeStruct((pixels, 128), jnp.float32),
            jax.ShapeDtypeStruct((pixels, 128), jnp.float32),
        ],
        cost_estimate=pl.CostEstimate(
            flops=2 * pixels * count * (channels + 256),
            transcendentals=pixels * count,
            bytes_accessed=2 * count * (channels + 128) + 2 * pixels * channels + 16 * pixels * 128,
        ),
    )(features, block, weights, running_max, acc)


def deposit_table(bits):
    table = np.zeros((1 << len(bits),), np.int32)
    for q in range(table.shape[0]):
        table[q] = sum(((q >> i) & 1) << b for i, b in enumerate(bits))
    return table


def row_pass_joined(hidden, inputs, weight):
    width_h = hidden.shape[-1]
    hidden_half = lax.optimization_barrier(hidden.astype(jnp.bfloat16))
    joined = jnp.concatenate([hidden_half, inputs], axis=-1)
    gate_pair = jax.nn.sigmoid(conv_valid(pad_columns(joined), weight[:, :, : 2 * width_h], 1))
    update_gate = gate_pair[..., :width_h]
    reset_gate = gate_pair[..., width_h:]
    gated = (reset_gate * hidden_half.astype(jnp.float32)).astype(jnp.bfloat16)
    joined = jnp.concatenate([gated, inputs], axis=-1)
    candidate = jnp.tanh(conv_valid(pad_columns(joined), weight[:, :, 2 * width_h :], 1))
    return (1.0 - update_gate) * hidden + update_gate * candidate


def column_pass_joined(hidden, inputs, weight):
    width_h = hidden.shape[-1]
    rows = hidden.shape[0]
    hidden_half = lax.optimization_barrier(hidden.astype(jnp.bfloat16))
    joined = jnp.concatenate([hidden_half, inputs], axis=-1)
    gate_pair = jax.nn.sigmoid(conv_valid(joined, weight[:, :, : 2 * width_h], 0))
    update_gate = gate_pair[2 : rows - 6, :, :width_h]
    reset_gate = gate_pair[..., width_h:]
    gated = (reset_gate * hidden_half[2 : rows - 2].astype(jnp.float32)).astype(jnp.bfloat16)
    joined = jnp.concatenate([gated, inputs[2 : rows - 2]], axis=-1)
    candidate = jnp.tanh(conv_valid(joined, weight[:, :, 2 * width_h :], 0))
    return (1.0 - update_gate) * hidden[4 : rows - 4] + update_gate * candidate


def per_device(frame1, frame2, context, hidden_init, offsets, w_motion, w_row, w_col):
    band_rows, image_width, channels = frame1.shape
    bands = lax.axis_size("band")
    total_rows = band_rows * bands
    band = lax.axis_index("band")
    row_first = band * band_rows
    strips = scaled_strips(frame2, math.sqrt(channels))
    grid_cols = strips.shape[1]
    target_row, target_col, pixel_row, pixel_col = lookup_targets(
        offsets, row_first, total_rows, image_width
    )
    pixel_count = band_rows * image_width
    features = frame1.reshape(pixel_count, channels)
    deposit = deposit_table(GATHER_BITS)
    state = (
        jnp.full((pixel_count, 128), -jnp.inf, jnp.float32),
        jnp.zeros((pixel_count, 128), jnp.float32),
    )
    held = strips.reshape(band_rows * grid_cols, channels)
    state = match_block(state, features, held, band[None], grid_cols)
    for step, bit in enumerate(GATHER_BITS):
        flip = 1 << bit
        pairs = [(i, i ^ flip) for i in range(bands)]
        got = lax.ppermute(held, "band", pairs)
        got_rows = (band ^ flip) ^ jnp.asarray(deposit[: 1 << step])
        settled = state
        state = match_block(state, features, got, got_rows, grid_cols)
        if step + 1 < len(GATHER_BITS):
            held = jnp.concatenate([held, got], axis=0)
            held, settled = lax.optimization_barrier((held, settled))
    running_max, acc = state
    denominator = acc[:, 0]
    flow_row = (acc[:, 1] / denominator / total_rows).reshape(
        band_rows, image_width
    ) - pixel_row.astype(jnp.float32) / total_rows
    flow_col = (
        (8.0 * (acc[:, 2] / denominator) + 3.5) / image_width
    ).reshape(band_rows, image_width) - pixel_col.astype(jnp.float32) / image_width
    inverse = np.argsort(deposit).astype(np.int32)
    t_row = target_row.reshape(pixel_count)
    t_col = target_col.reshape(pixel_count)
    valid = t_row >= 0
    place = jnp.asarray(inverse)[jnp.where(valid, t_row ^ band, 0)] * grid_cols + jnp.where(
        valid, t_col, 0
    )
    half = held.shape[0]
    picked = jnp.where(
        (place < half)[:, None],
        jnp.take(held, jnp.minimum(place, half - 1), axis=0),
        jnp.take(got, jnp.maximum(place - half, 0), axis=0),
    )
    found = jnp.sum(features.astype(jnp.float32) * picked.astype(jnp.float32), axis=1)
    lookup = jnp.where(valid, found, 0.0)
    lookup = lookup.reshape(band_rows, image_width)
    motion = jax.nn.relu(
        flow_row[..., None] * w_motion[0]
        + flow_col[..., None] * w_motion[1]
        + lookup[..., None] * w_motion[2]
    ).astype(jnp.bfloat16)
    depth = 4 * ITERS
    width_h = hidden_init.shape[-1]
    early = rows_around(
        jnp.concatenate([hidden_init, context], axis=-1),
        depth,
        lambda source, offset: passed_along(source, "band", offset),
    )
    moved = rows_around(motion, depth, lambda source, offset: passed_along(source, "band", offset))
    window_rows = band + jnp.arange(-depth, depth + 1, dtype=jnp.int32)
    inside_rows = ((window_rows >= 0) & (window_rows < total_rows)).astype(jnp.float32)[:, None, None]
    inputs = jnp.concatenate([early[..., width_h:], moved], axis=-1)
    hidden = early[..., :width_h].astype(jnp.float32)
    for iteration in range(ITERS):
        trim = 4 * iteration
        rows = 2 * (depth - trim) + 1
        window = inputs[trim : trim + rows]
        hidden = row_pass_joined(hidden, window, w_row) * inside_rows[trim : trim + rows]
        hidden = column_pass_joined(hidden, window, w_col)
        hidden = hidden * inside_rows[trim + 4 : trim + rows - 4]
    return (hidden, jnp.stack([flow_row, flow_col]))


def solution(mesh):
    return jax.shard_map(
        per_device,
        mesh=mesh,
        in_specs=(
            P("band", "pair", None),
            P("band", "pair", None),
            P("band", "pair", None),
            P("band", "pair", None),
            P(None, "band", "pair"),
            P(),
            P(),
            P(),
        ),
        out_specs=(P("band", "pair", None), P(None, "band", "pair")),
        check_vma=False,
    )
```

```python
import math

import numpy as np

import jax
import jax.numpy as jnp
from jax import lax
from jax.experimental import pallas as pl
from jax.sharding import PartitionSpec as P

ITERS = 2


def passed_along(array, axis, by):
    count = lax.axis_size(axis)
    pairs = [(i, i + by) for i in range(count) if 0 <= i + by < count]
    return lax.ppermute(array, axis, pairs)


def pool_strips(frame2):
    band_rows, image_width, channels = frame2.shape
    blocks = frame2.astype(jnp.float32).reshape(band_rows, image_width // 8, 8, channels)
    return (jnp.sum(blocks, axis=2) / 2.0).astype(jnp.bfloat16)


def scaled_strips(frame2, scale):
    band_rows, image_width, channels = frame2.shape
    blocks = frame2.astype(jnp.float32).reshape(band_rows, image_width // 8, 8, channels)
    return (jnp.sum(blocks, axis=2) / (2.0 * scale)).astype(jnp.bfloat16)


def lookup_targets(offsets, row_first, total_rows, image_width):
    band_rows = offsets.shape[1]
    pixel_row = (
        row_first
        + jnp.arange(band_rows, dtype=jnp.int32)[:, None]
        + jnp.zeros((1, image_width), jnp.int32)
    )
    pixel_col = jnp.arange(image_width, dtype=jnp.int32)[None, :]
    target_row = pixel_row + offsets[0]
    target_col = pixel_col // 8 + offsets[1]
    inside = (
        (target_row >= 0)
        & (target_row < total_rows)
        & (target_col >= 0)
        & (target_col < image_width // 8)
    )
    target_row = jnp.where(inside, target_row, -1)
    target_col = jnp.where(inside, target_col, -1)
    return (target_row, target_col, pixel_row, pixel_col)


def strip_step(
    state, feature_rows, strip_block, row_zero, total_rows, image_width, target_row, target_col
):
    block_rows, grid_cols, channels = strip_block.shape
    scores = jnp.dot(
        feature_rows,
        strip_block.reshape(block_rows * grid_cols, channels).T,
        preferred_element_type=jnp.float32,
    ) / math.sqrt(channels)
    running_max, denominator, acc_row, acc_col, lookup = state
    new_max = jnp.maximum(running_max, jnp.max(scores, axis=1))
    shrink = jnp.exp(running_max - new_max)
    exponent = jnp.exp(scores - new_max[:, None]).reshape(-1, block_rows, grid_cols)
    strip_row = row_zero + jnp.arange(block_rows, dtype=jnp.int32)
    column_ids = jnp.arange(grid_cols, dtype=jnp.int32)
    row_centre = strip_row.astype(jnp.float32) / total_rows
    col_centre = ((8 * column_ids).astype(jnp.float32) + 3.5) / image_width
    row_weight = jnp.sum(exponent, axis=2)
    col_weight = jnp.sum(exponent, axis=1)
    scores_grid = scores.reshape(-1, block_rows, grid_cols)
    hit = (strip_row[None, :, None] == target_row[:, None, None]) & (
        column_ids[None, None, :] == target_col[:, None, None]
    )
    found = jnp.sum(jnp.where(hit, scores_grid, 0.0), axis=(1, 2))
    return (
        new_max,
        denominator * shrink + jnp.sum(row_weight, axis=1),
        acc_row * shrink + jnp.sum(row_weight * row_centre[None, :], axis=1),
        acc_col * shrink + jnp.sum(col_weight * col_centre[None, :], axis=1),
        lookup + found,
    )


def conv_valid(source, weight, conv_axis):
    out_count = source.shape[conv_axis] - 4
    summed = None
    for kernel_tap in range(5):
        tap_slice = lax.slice_in_dim(source, kernel_tap, kernel_tap + out_count, axis=conv_axis)
        tap_term = jnp.dot(
            tap_slice.reshape(-1, tap_slice.shape[-1]),
            weight[kernel_tap],
            preferred_element_type=jnp.float32,
        )
        summed = tap_term if summed is None else summed + tap_term
    out_shape = tuple(tap_slice.shape[:-1]) + (weight.shape[-1],)
    return summed.reshape(out_shape)


def pad_columns(source):
    return jnp.pad(source, ((0, 0), (2, 2), (0, 0)))


def rows_around(source, depth, mover):
    above = [
        mover(source, offset)
        for offset in list(range(depth, 0, -1)) + list(range(-1, -depth - 1, -1))
    ]
    return jnp.concatenate(above[:depth] + [source] + above[depth:], axis=0)


def row_pass(hidden, from_inputs, weight):
    width_h = hidden.shape[-1]
    hidden_half = lax.optimization_barrier(hidden.astype(jnp.bfloat16))
    gate_pair = jax.nn.sigmoid(
        conv_valid(pad_columns(hidden_half), weight[:, :width_h, : 2 * width_h], 1)
        + from_inputs[..., : 2 * width_h]
    )
    update_gate = gate_pair[..., :width_h]
    reset_gate = gate_pair[..., width_h:]
    gated = (reset_gate * hidden_half.astype(jnp.float32)).astype(jnp.bfloat16)
    candidate = jnp.tanh(
        conv_valid(pad_columns(gated), weight[:, :width_h, 2 * width_h :], 1)
        + from_inputs[..., 2 * width_h :]
    )
    return (1.0 - update_gate) * hidden + update_gate * candidate


def column_pass_each(hidden, from_inputs, weight, inputs=None):
    width_h = hidden.shape[-1]
    hidden_half = lax.optimization_barrier(hidden.astype(jnp.bfloat16))
    mover = lambda source, offset: passed_along(source, "band", offset)
    if inputs is None:
        hidden_ext = rows_around(hidden_half, 2, mover)
    else:
        joined_ext = rows_around(jnp.concatenate([hidden_half, inputs], axis=-1), 2, mover)
        hidden_ext = joined_ext[..., :width_h]
        from_inputs = conv_valid(joined_ext[..., width_h:], weight[:, width_h:, :], 0)
    gate_pair = jax.nn.sigmoid(
        conv_valid(hidden_ext, weight[:, :width_h, : 2 * width_h], 0)
        + from_inputs[..., : 2 * width_h]
    )
    update_gate = gate_pair[..., :width_h]
    reset_gate = gate_pair[..., width_h:]
    gated = (reset_gate * hidden_half.astype(jnp.float32)).astype(jnp.bfloat16)
    gated_ext = rows_around(gated, 2, mover)
    candidate = jnp.tanh(
        conv_valid(gated_ext, weight[:, :width_h, 2 * width_h :], 0)
        + from_inputs[..., 2 * width_h :]
    )
    return ((1.0 - update_gate) * hidden + update_gate * candidate, from_inputs)


GATHER_BITS = (4, 3, 2, 7, 6, 5, 1, 0)


def match_kernel(f1_ref, s_ref, w_ref, m_in, a_in, m_out, a_out):
    @pl.when(pl.program_id(0) == 0)
    def _():
        m_out[...] = m_in[...]
        a_out[...] = a_in[...]

    scores = lax.dot_general(
        f1_ref[...], s_ref[...], (((1,), (1,)), ((), ())), preferred_element_type=jnp.float32
    )
    m_old = m_out[:, 0:1]
    m_new = jnp.maximum(m_old, jnp.max(scores, axis=1, keepdims=True))
    p = jnp.exp(scores - m_new)
    shrink = jnp.exp(m_old - m_new)
    p_hi = p.astype(jnp.bfloat16)
    p_lo = (p - p_hi.astype(jnp.float32)).astype(jnp.bfloat16)
    w = w_ref[...]
    part = jnp.dot(p_hi, w, preferred_element_type=jnp.float32) + jnp.dot(
        p_lo, w, preferred_element_type=jnp.float32
    )
    a_out[...] = a_out[...] * shrink + part
    m_out[...] = jnp.broadcast_to(m_new, m_out.shape)


def match_block(state, features, block, block_rows, grid_cols):
    count, channels = block.shape
    pixels = features.shape[0]
    tile = min(count, 768)
    strip_row = jnp.repeat(block_rows, grid_cols).astype(jnp.float32)
    strip_col = (jnp.arange(count, dtype=jnp.int32) % grid_cols).astype(jnp.float32)
    weights = jnp.concatenate(
        [
            jnp.ones((count, 1), jnp.float32),
            strip_row[:, None],
            strip_col[:, None],
            jnp.zeros((count, 125), jnp.float32),
        ],
        axis=1,
    ).astype(jnp.bfloat16)
    running_max, acc = state
    return pl.pallas_call(
        match_kernel,
        grid=(count // tile,),
        in_specs=[
            pl.BlockSpec((pixels, channels), lambda i: (0, 0)),
            pl.BlockSpec((tile, channels), lambda i: (i, 0)),
            pl.BlockSpec((tile, 128), lambda i: (i, 0)),
            pl.BlockSpec((pixels, 128), lambda i: (0, 0)),
            pl.BlockSpec((pixels, 128), lambda i: (0, 0)),
        ],
        out_specs=[
            pl.BlockSpec((pixels, 128), lambda i: (0, 0)),
            pl.BlockSpec((pixels, 128), lambda i: (0, 0)),
        ],
        out_shape=[
            jax.ShapeDtypeStruct((pixels, 128), jnp.float32),
            jax.ShapeDtypeStruct((pixels, 128), jnp.float32),
        ],
        cost_estimate=pl.CostEstimate(
            flops=2 * pixels * count * (channels + 256),
            transcendentals=pixels * count,
            bytes_accessed=2 * count * (channels + 128) + 2 * pixels * channels + 16 * pixels * 128,
        ),
    )(features, block, weights, running_max, acc)


def deposit_table(bits):
    table = np.zeros((1 << len(bits),), np.int32)
    for q in range(table.shape[0]):
        table[q] = sum(((q >> i) & 1) << b for i, b in enumerate(bits))
    return table


def per_device(frame1, frame2, context, hidden_init, offsets, w_motion, w_row, w_col):
    band_rows, image_width, channels = frame1.shape
    bands = lax.axis_size("band")
    total_rows = band_rows * bands
    band = lax.axis_index("band")
    row_first = band * band_rows
    strips = scaled_strips(frame2, math.sqrt(channels))
    grid_cols = strips.shape[1]
    target_row, target_col, pixel_row, pixel_col = lookup_targets(
        offsets, row_first, total_rows, image_width
    )
    pixel_count = band_rows * image_width
    features = frame1.reshape(pixel_count, channels)
    deposit = deposit_table(GATHER_BITS)
    state = (
        jnp.full((pixel_count, 128), -jnp.inf, jnp.float32),
        jnp.zeros((pixel_count, 128), jnp.float32),
    )
    held = strips.reshape(band_rows * grid_cols, channels)
    state = match_block(state, features, held, band[None], grid_cols)
    for step, bit in enumerate(GATHER_BITS):
        flip = 1 << bit
        pairs = [(i, i ^ flip) for i in range(bands)]
        got = lax.ppermute(held, "band", pairs)
        got_rows = (band ^ flip) ^ jnp.asarray(deposit[: 1 << step])
        settled = state
        state = match_block(state, features, got, got_rows, grid_cols)
        if step + 1 < len(GATHER_BITS):
            held = jnp.concatenate([held, got], axis=0)
            held, settled = lax.optimization_barrier((held, settled))
    running_max, acc = state
    denominator = acc[:, 0]
    flow_row = (acc[:, 1] / denominator / total_rows).reshape(
        band_rows, image_width
    ) - pixel_row.astype(jnp.float32) / total_rows
    flow_col = (
        (8.0 * (acc[:, 2] / denominator) + 3.5) / image_width
    ).reshape(band_rows, image_width) - pixel_col.astype(jnp.float32) / image_width
    inverse = np.argsort(deposit).astype(np.int32)
    t_row = target_row.reshape(pixel_count)
    t_col = target_col.reshape(pixel_count)
    valid = t_row >= 0
    place = jnp.asarray(inverse)[jnp.where(valid, t_row ^ band, 0)] * grid_cols + jnp.where(
        valid, t_col, 0
    )
    half = held.shape[0]
    picked = jnp.where(
        (place < half)[:, None],
        jnp.take(held, jnp.minimum(place, half - 1), axis=0),
        jnp.take(got, jnp.maximum(place - half, 0), axis=0),
    )
    found = jnp.sum(features.astype(jnp.float32) * picked.astype(jnp.float32), axis=1)
    lookup = jnp.where(valid, found, 0.0)
    lookup = lookup.reshape(band_rows, image_width)
    motion = jax.nn.relu(
        flow_row[..., None] * w_motion[0]
        + flow_col[..., None] * w_motion[1]
        + lookup[..., None] * w_motion[2]
    ).astype(jnp.bfloat16)
    inputs = jnp.concatenate([context, motion], axis=-1)
    width_h = hidden_init.shape[-1]
    from_row = conv_valid(pad_columns(inputs), w_row[:, width_h:, :], 1)
    hidden = hidden_init.astype(jnp.float32)
    from_col = None
    for iteration in range(ITERS):
        hidden = row_pass(hidden, from_row, w_row)
        hidden, from_col = column_pass_each(
            hidden, from_col, w_col, inputs if iteration == 0 else None
        )
    return (hidden, jnp.stack([flow_row, flow_col]))


def solution(mesh):
    return jax.shard_map(
        per_device,
        mesh=mesh,
        in_specs=(
            P("band", "pair", None),
            P("band", "pair", None),
            P("band", "pair", None),
            P("band", "pair", None),
            P(None, "band", "pair"),
            P(),
            P(),
            P(),
        ),
        out_specs=(P("band", "pair", None), P(None, "band", "pair")),
        check_vma=False,
    )
```

```python
import math

import numpy as np

import jax
import jax.numpy as jnp
from jax import lax
from jax.experimental import pallas as pl
from jax.sharding import PartitionSpec as P

ITERS = 2


def passed_along(array, axis, by):
    count = lax.axis_size(axis)
    pairs = [(i, i + by) for i in range(count) if 0 <= i + by < count]
    return lax.ppermute(array, axis, pairs)


def pool_strips(frame2):
    band_rows, image_width, channels = frame2.shape
    blocks = frame2.astype(jnp.float32).reshape(band_rows, image_width // 8, 8, channels)
    return (jnp.sum(blocks, axis=2) / 2.0).astype(jnp.bfloat16)


def scaled_strips(frame2, scale):
    band_rows, image_width, channels = frame2.shape
    blocks = frame2.astype(jnp.float32).reshape(band_rows, image_width // 8, 8, channels)
    return (jnp.sum(blocks, axis=2) / (2.0 * scale)).astype(jnp.bfloat16)


def lookup_targets(offsets, row_first, total_rows, image_width):
    band_rows = offsets.shape[1]
    pixel_row = (
        row_first
        + jnp.arange(band_rows, dtype=jnp.int32)[:, None]
        + jnp.zeros((1, image_width), jnp.int32)
    )
    pixel_col = jnp.arange(image_width, dtype=jnp.int32)[None, :]
    target_row = pixel_row + offsets[0]
    target_col = pixel_col // 8 + offsets[1]
    inside = (
        (target_row >= 0)
        & (target_row < total_rows)
        & (target_col >= 0)
        & (target_col < image_width // 8)
    )
    target_row = jnp.where(inside, target_row, -1)
    target_col = jnp.where(inside, target_col, -1)
    return (target_row, target_col, pixel_row, pixel_col)


def strip_step(
    state, feature_rows, strip_block, row_zero, total_rows, image_width, target_row, target_col
):
    block_rows, grid_cols, channels = strip_block.shape
    scores = jnp.dot(
        feature_rows,
        strip_block.reshape(block_rows * grid_cols, channels).T,
        preferred_element_type=jnp.float32,
    ) / math.sqrt(channels)
    running_max, denominator, acc_row, acc_col, lookup = state
    new_max = jnp.maximum(running_max, jnp.max(scores, axis=1))
    shrink = jnp.exp(running_max - new_max)
    exponent = jnp.exp(scores - new_max[:, None]).reshape(-1, block_rows, grid_cols)
    strip_row = row_zero + jnp.arange(block_rows, dtype=jnp.int32)
    column_ids = jnp.arange(grid_cols, dtype=jnp.int32)
    row_centre = strip_row.astype(jnp.float32) / total_rows
    col_centre = ((8 * column_ids).astype(jnp.float32) + 3.5) / image_width
    row_weight = jnp.sum(exponent, axis=2)
    col_weight = jnp.sum(exponent, axis=1)
    scores_grid = scores.reshape(-1, block_rows, grid_cols)
    hit = (strip_row[None, :, None] == target_row[:, None, None]) & (
        column_ids[None, None, :] == target_col[:, None, None]
    )
    found = jnp.sum(jnp.where(hit, scores_grid, 0.0), axis=(1, 2))
    return (
        new_max,
        denominator * shrink + jnp.sum(row_weight, axis=1),
        acc_row * shrink + jnp.sum(row_weight * row_centre[None, :], axis=1),
        acc_col * shrink + jnp.sum(col_weight * col_centre[None, :], axis=1),
        lookup + found,
    )


def conv_valid(source, weight, conv_axis):
    out_count = source.shape[conv_axis] - 4
    summed = None
    for kernel_tap in range(5):
        tap_slice = lax.slice_in_dim(source, kernel_tap, kernel_tap + out_count, axis=conv_axis)
        tap_term = jnp.dot(
            tap_slice.reshape(-1, tap_slice.shape[-1]),
            weight[kernel_tap],
            preferred_element_type=jnp.float32,
        )
        summed = tap_term if summed is None else summed + tap_term
    out_shape = tuple(tap_slice.shape[:-1]) + (weight.shape[-1],)
    return summed.reshape(out_shape)


def pad_columns(source):
    return jnp.pad(source, ((0, 0), (2, 2), (0, 0)))


def rows_around(source, depth, mover):
    above = [
        mover(source, offset)
        for offset in list(range(depth, 0, -1)) + list(range(-1, -depth - 1, -1))
    ]
    return jnp.concatenate(above[:depth] + [source] + above[depth:], axis=0)


def row_pass(hidden, from_inputs, weight):
    width_h = hidden.shape[-1]
    hidden_half = lax.optimization_barrier(hidden.astype(jnp.bfloat16))
    gate_pair = jax.nn.sigmoid(
        conv_valid(pad_columns(hidden_half), weight[:, :width_h, : 2 * width_h], 1)
        + from_inputs[..., : 2 * width_h]
    )
    update_gate = gate_pair[..., :width_h]
    reset_gate = gate_pair[..., width_h:]
    gated = (reset_gate * hidden_half.astype(jnp.float32)).astype(jnp.bfloat16)
    candidate = jnp.tanh(
        conv_valid(pad_columns(gated), weight[:, :width_h, 2 * width_h :], 1)
        + from_inputs[..., 2 * width_h :]
    )
    return (1.0 - update_gate) * hidden + update_gate * candidate


def column_pass_each(hidden, from_inputs, weight, inputs=None):
    width_h = hidden.shape[-1]
    hidden_half = lax.optimization_barrier(hidden.astype(jnp.bfloat16))
    mover = lambda source, offset: passed_along(source, "band", offset)
    if inputs is None:
        hidden_ext = rows_around(hidden_half, 2, mover)
    else:
        joined_ext = rows_around(jnp.concatenate([hidden_half, inputs], axis=-1), 2, mover)
        hidden_ext = joined_ext[..., :width_h]
        from_inputs = conv_valid(joined_ext[..., width_h:], weight[:, width_h:, :], 0)
    gate_pair = jax.nn.sigmoid(
        conv_valid(hidden_ext, weight[:, :width_h, : 2 * width_h], 0)
        + from_inputs[..., : 2 * width_h]
    )
    update_gate = gate_pair[..., :width_h]
    reset_gate = gate_pair[..., width_h:]
    gated = (reset_gate * hidden_half.astype(jnp.float32)).astype(jnp.bfloat16)
    gated_ext = rows_around(gated, 2, mover)
    candidate = jnp.tanh(
        conv_valid(gated_ext, weight[:, :width_h, 2 * width_h :], 0)
        + from_inputs[..., 2 * width_h :]
    )
    return ((1.0 - update_gate) * hidden + update_gate * candidate, from_inputs)


GATHER_BITS = (4, 3, 2, 7, 6, 1, 5, 0)


def match_kernel(f1_ref, s_ref, w_ref, m_in, a_in, m_out, a_out):
    @pl.when(pl.program_id(0) == 0)
    def _():
        m_out[...] = m_in[...]
        a_out[...] = a_in[...]

    scores = lax.dot_general(
        f1_ref[...], s_ref[...], (((1,), (1,)), ((), ())), preferred_element_type=jnp.float32
    )
    m_old = m_out[:, 0:1]
    m_new = jnp.maximum(m_old, jnp.max(scores, axis=1, keepdims=True))
    p = jnp.exp(scores - m_new)
    shrink = jnp.exp(m_old - m_new)
    p_hi = p.astype(jnp.bfloat16)
    p_lo = (p - p_hi.astype(jnp.float32)).astype(jnp.bfloat16)
    w = w_ref[...]
    part = jnp.dot(p_hi, w, preferred_element_type=jnp.float32) + jnp.dot(
        p_lo, w, preferred_element_type=jnp.float32
    )
    a_out[...] = a_out[...] * shrink + part
    m_out[...] = jnp.broadcast_to(m_new, m_out.shape)


def match_block(state, features, block, block_rows, grid_cols):
    count, channels = block.shape
    pixels = features.shape[0]
    tile = min(count, 768)
    strip_row = jnp.repeat(block_rows, grid_cols).astype(jnp.float32)
    strip_col = (jnp.arange(count, dtype=jnp.int32) % grid_cols).astype(jnp.float32)
    weights = jnp.concatenate(
        [
            jnp.ones((count, 1), jnp.float32),
            strip_row[:, None],
            strip_col[:, None],
            jnp.zeros((count, 125), jnp.float32),
        ],
        axis=1,
    ).astype(jnp.bfloat16)
    running_max, acc = state
    return pl.pallas_call(
        match_kernel,
        grid=(count // tile,),
        in_specs=[
            pl.BlockSpec((pixels, channels), lambda i: (0, 0)),
            pl.BlockSpec((tile, channels), lambda i: (i, 0)),
            pl.BlockSpec((tile, 128), lambda i: (i, 0)),
            pl.BlockSpec((pixels, 128), lambda i: (0, 0)),
            pl.BlockSpec((pixels, 128), lambda i: (0, 0)),
        ],
        out_specs=[
            pl.BlockSpec((pixels, 128), lambda i: (0, 0)),
            pl.BlockSpec((pixels, 128), lambda i: (0, 0)),
        ],
        out_shape=[
            jax.ShapeDtypeStruct((pixels, 128), jnp.float32),
            jax.ShapeDtypeStruct((pixels, 128), jnp.float32),
        ],
        cost_estimate=pl.CostEstimate(
            flops=2 * pixels * count * (channels + 256),
            transcendentals=pixels * count,
            bytes_accessed=2 * count * (channels + 128) + 2 * pixels * channels + 16 * pixels * 128,
        ),
    )(features, block, weights, running_max, acc)


def deposit_table(bits):
    table = np.zeros((1 << len(bits),), np.int32)
    for q in range(table.shape[0]):
        table[q] = sum(((q >> i) & 1) << b for i, b in enumerate(bits))
    return table


def per_device(frame1, frame2, context, hidden_init, offsets, w_motion, w_row, w_col):
    band_rows, image_width, channels = frame1.shape
    bands = lax.axis_size("band")
    total_rows = band_rows * bands
    band = lax.axis_index("band")
    row_first = band * band_rows
    strips = scaled_strips(frame2, math.sqrt(channels))
    grid_cols = strips.shape[1]
    target_row, target_col, pixel_row, pixel_col = lookup_targets(
        offsets, row_first, total_rows, image_width
    )
    pixel_count = band_rows * image_width
    features = frame1.reshape(pixel_count, channels)
    deposit = deposit_table(GATHER_BITS)
    state = (
        jnp.full((pixel_count, 128), -jnp.inf, jnp.float32),
        jnp.zeros((pixel_count, 128), jnp.float32),
    )
    held = strips.reshape(band_rows * grid_cols, channels)
    state = match_block(state, features, held, band[None], grid_cols)
    last = len(GATHER_BITS) - 1
    for step, bit in enumerate(GATHER_BITS):
        flip = 1 << bit
        pairs = [(i, i ^ flip) for i in range(bands)]
        got_rows = (band ^ flip) ^ jnp.asarray(deposit[: 1 << step])
        if step < last:
            got = lax.ppermute(held, "band", pairs)
            settled = state
            state = match_block(state, features, got, got_rows, grid_cols)
            held = jnp.concatenate([held, got], axis=0)
            held, settled = lax.optimization_barrier((held, settled))
        else:
            split = held.shape[0] // 2
            first = lax.ppermute(held[:split], "band", pairs)
            second = lax.ppermute(held[split:], "band", pairs)
            half_rows = got_rows.shape[0] // 2
            state = match_block(state, features, first, got_rows[:half_rows], grid_cols)
            state = match_block(state, features, second, got_rows[half_rows:], grid_cols)
    pieces = [held, first, second]
    running_max, acc = state
    denominator = acc[:, 0]
    flow_row = (acc[:, 1] / denominator / total_rows).reshape(
        band_rows, image_width
    ) - pixel_row.astype(jnp.float32) / total_rows
    flow_col = (
        (8.0 * (acc[:, 2] / denominator) + 3.5) / image_width
    ).reshape(band_rows, image_width) - pixel_col.astype(jnp.float32) / image_width
    inverse = jnp.asarray(np.argsort(deposit).astype(np.int32))
    reach = 4
    window = []
    for shift in range(-reach, reach + 1):
        block = inverse[jnp.clip(band + shift, 0, total_rows - 1) ^ band]
        chosen = None
        first_block = 0
        for piece in pieces:
            count = piece.shape[0] // grid_cols
            local = jnp.clip(block - first_block, 0, count - 1)
            part = lax.dynamic_slice_in_dim(piece, local * grid_cols, grid_cols, 0)
            chosen = part if chosen is None else jnp.where(block >= first_block, part, chosen)
            first_block += count
        window.append(chosen)
    window = jnp.concatenate(window, axis=0)
    near = lax.dot_general(
        features, window, (((1,), (1,)), ((), ())), preferred_element_type=jnp.float32
    )
    t_row = target_row.reshape(pixel_count)
    t_col = target_col.reshape(pixel_count)
    valid = t_row >= 0
    slot = (t_row - band + reach) * grid_cols + t_col
    hit = jnp.arange(near.shape[1], dtype=jnp.int32)[None, :] == slot[:, None]
    found = jnp.sum(jnp.where(hit, near, 0.0), axis=1)
    lookup = jnp.where(valid, found, 0.0)
    lookup = lookup.reshape(band_rows, image_width)
    motion = jax.nn.relu(
        flow_row[..., None] * w_motion[0]
        + flow_col[..., None] * w_motion[1]
        + lookup[..., None] * w_motion[2]
    ).astype(jnp.bfloat16)
    inputs = jnp.concatenate([context, motion], axis=-1)
    width_h = hidden_init.shape[-1]
    from_row = conv_valid(pad_columns(inputs), w_row[:, width_h:, :], 1)
    hidden = hidden_init.astype(jnp.float32)
    from_col = None
    for iteration in range(ITERS):
        hidden = row_pass(hidden, from_row, w_row)
        hidden, from_col = column_pass_each(
            hidden, from_col, w_col, inputs if iteration == 0 else None
        )
    return (hidden, jnp.stack([flow_row, flow_col]))


def solution(mesh):
    return jax.shard_map(
        per_device,
        mesh=mesh,
        in_specs=(
            P("band", "pair", None),
            P("band", "pair", None),
            P("band", "pair", None),
            P("band", "pair", None),
            P(None, "band", "pair"),
            P(),
            P(),
            P(),
        ),
        out_specs=(P("band", "pair", None), P(None, "band", "pair")),
        check_vma=False,
    )
```

```python
import math

import numpy as np

import jax
import jax.numpy as jnp
from jax import lax
from jax.experimental import pallas as pl
from jax.sharding import PartitionSpec as P

ITERS = 2


def passed_along(array, axis, by):
    count = lax.axis_size(axis)
    pairs = [(i, i + by) for i in range(count) if 0 <= i + by < count]
    return lax.ppermute(array, axis, pairs)


def pool_strips(frame2):
    band_rows, image_width, channels = frame2.shape
    blocks = frame2.astype(jnp.float32).reshape(band_rows, image_width // 8, 8, channels)
    return (jnp.sum(blocks, axis=2) / 2.0).astype(jnp.bfloat16)


def scaled_strips(frame2, scale):
    band_rows, image_width, channels = frame2.shape
    blocks = frame2.astype(jnp.float32).reshape(band_rows, image_width // 8, 8, channels)
    return (jnp.sum(blocks, axis=2) / (2.0 * scale)).astype(jnp.bfloat16)


def lookup_targets(offsets, row_first, total_rows, image_width):
    band_rows = offsets.shape[1]
    pixel_row = (
        row_first
        + jnp.arange(band_rows, dtype=jnp.int32)[:, None]
        + jnp.zeros((1, image_width), jnp.int32)
    )
    pixel_col = jnp.arange(image_width, dtype=jnp.int32)[None, :]
    target_row = pixel_row + offsets[0]
    target_col = pixel_col // 8 + offsets[1]
    inside = (
        (target_row >= 0)
        & (target_row < total_rows)
        & (target_col >= 0)
        & (target_col < image_width // 8)
    )
    target_row = jnp.where(inside, target_row, -1)
    target_col = jnp.where(inside, target_col, -1)
    return (target_row, target_col, pixel_row, pixel_col)


def strip_step(
    state, feature_rows, strip_block, row_zero, total_rows, image_width, target_row, target_col
):
    block_rows, grid_cols, channels = strip_block.shape
    scores = jnp.dot(
        feature_rows,
        strip_block.reshape(block_rows * grid_cols, channels).T,
        preferred_element_type=jnp.float32,
    ) / math.sqrt(channels)
    running_max, denominator, acc_row, acc_col, lookup = state
    new_max = jnp.maximum(running_max, jnp.max(scores, axis=1))
    shrink = jnp.exp(running_max - new_max)
    exponent = jnp.exp(scores - new_max[:, None]).reshape(-1, block_rows, grid_cols)
    strip_row = row_zero + jnp.arange(block_rows, dtype=jnp.int32)
    column_ids = jnp.arange(grid_cols, dtype=jnp.int32)
    row_centre = strip_row.astype(jnp.float32) / total_rows
    col_centre = ((8 * column_ids).astype(jnp.float32) + 3.5) / image_width
    row_weight = jnp.sum(exponent, axis=2)
    col_weight = jnp.sum(exponent, axis=1)
    scores_grid = scores.reshape(-1, block_rows, grid_cols)
    hit = (strip_row[None, :, None] == target_row[:, None, None]) & (
        column_ids[None, None, :] == target_col[:, None, None]
    )
    found = jnp.sum(jnp.where(hit, scores_grid, 0.0), axis=(1, 2))
    return (
        new_max,
        denominator * shrink + jnp.sum(row_weight, axis=1),
        acc_row * shrink + jnp.sum(row_weight * row_centre[None, :], axis=1),
        acc_col * shrink + jnp.sum(col_weight * col_centre[None, :], axis=1),
        lookup + found,
    )


def conv_valid(source, weight, conv_axis):
    out_count = source.shape[conv_axis] - 4
    summed = None
    for kernel_tap in range(5):
        tap_slice = lax.slice_in_dim(source, kernel_tap, kernel_tap + out_count, axis=conv_axis)
        tap_term = jnp.dot(
            tap_slice.reshape(-1, tap_slice.shape[-1]),
            weight[kernel_tap],
            preferred_element_type=jnp.float32,
        )
        summed = tap_term if summed is None else summed + tap_term
    out_shape = tuple(tap_slice.shape[:-1]) + (weight.shape[-1],)
    return summed.reshape(out_shape)


def pad_columns(source):
    return jnp.pad(source, ((0, 0), (2, 2), (0, 0)))


def rows_around(source, depth, mover):
    above = [
        mover(source, offset)
        for offset in list(range(depth, 0, -1)) + list(range(-1, -depth - 1, -1))
    ]
    return jnp.concatenate(above[:depth] + [source] + above[depth:], axis=0)


def row_pass(hidden, from_inputs, weight):
    width_h = hidden.shape[-1]
    hidden_half = lax.optimization_barrier(hidden.astype(jnp.bfloat16))
    gate_pair = jax.nn.sigmoid(
        conv_valid(pad_columns(hidden_half), weight[:, :width_h, : 2 * width_h], 1)
        + from_inputs[..., : 2 * width_h]
    )
    update_gate = gate_pair[..., :width_h]
    reset_gate = gate_pair[..., width_h:]
    gated = (reset_gate * hidden_half.astype(jnp.float32)).astype(jnp.bfloat16)
    candidate = jnp.tanh(
        conv_valid(pad_columns(gated), weight[:, :width_h, 2 * width_h :], 1)
        + from_inputs[..., 2 * width_h :]
    )
    return (1.0 - update_gate) * hidden + update_gate * candidate


def column_pass_each(hidden, from_inputs, weight, inputs=None):
    width_h = hidden.shape[-1]
    hidden_half = lax.optimization_barrier(hidden.astype(jnp.bfloat16))
    mover = lambda source, offset: passed_along(source, "band", offset)
    if inputs is None:
        hidden_ext = rows_around(hidden_half, 2, mover)
    else:
        joined_ext = rows_around(jnp.concatenate([hidden_half, inputs], axis=-1), 2, mover)
        hidden_ext = joined_ext[..., :width_h]
        from_inputs = conv_valid(joined_ext[..., width_h:], weight[:, width_h:, :], 0)
    gate_pair = jax.nn.sigmoid(
        conv_valid(hidden_ext, weight[:, :width_h, : 2 * width_h], 0)
        + from_inputs[..., : 2 * width_h]
    )
    update_gate = gate_pair[..., :width_h]
    reset_gate = gate_pair[..., width_h:]
    gated = (reset_gate * hidden_half.astype(jnp.float32)).astype(jnp.bfloat16)
    gated_ext = rows_around(gated, 2, mover)
    candidate = jnp.tanh(
        conv_valid(gated_ext, weight[:, :width_h, 2 * width_h :], 0)
        + from_inputs[..., 2 * width_h :]
    )
    return ((1.0 - update_gate) * hidden + update_gate * candidate, from_inputs)


GATHER_BITS = (4, 3, 2, 7, 6, 1, 5, 0)


def match_kernel(f1_ref, s_ref, w_ref, m_in, a_in, m_out, a_out):
    @pl.when(pl.program_id(0) == 0)
    def _():
        m_out[...] = m_in[...]
        a_out[...] = a_in[...]

    scores = lax.dot_general(
        f1_ref[...], s_ref[...], (((1,), (1,)), ((), ())), preferred_element_type=jnp.float32
    )
    m_old = m_out[:, 0:1]
    m_new = jnp.maximum(m_old, jnp.max(scores, axis=1, keepdims=True))
    p = jnp.exp(scores - m_new)
    shrink = jnp.exp(m_old - m_new)
    part = jnp.dot(p.astype(jnp.bfloat16), w_ref[...], preferred_element_type=jnp.float32)
    a_out[...] = a_out[...] * shrink + part
    m_out[...] = jnp.broadcast_to(m_new, m_out.shape)


def match_block(state, features, block, block_rows, grid_cols):
    count, channels = block.shape
    pixels = features.shape[0]
    tile = min(count, 768)
    strip_row = jnp.repeat(block_rows, grid_cols).astype(jnp.float32)
    strip_col = (jnp.arange(count, dtype=jnp.int32) % grid_cols).astype(jnp.float32)
    weights = jnp.concatenate(
        [
            jnp.ones((count, 1), jnp.float32),
            strip_row[:, None],
            strip_col[:, None],
            jnp.zeros((count, 125), jnp.float32),
        ],
        axis=1,
    ).astype(jnp.bfloat16)
    running_max, acc = state
    return pl.pallas_call(
        match_kernel,
        grid=(count // tile,),
        in_specs=[
            pl.BlockSpec((pixels, channels), lambda i: (0, 0)),
            pl.BlockSpec((tile, channels), lambda i: (i, 0)),
            pl.BlockSpec((tile, 128), lambda i: (i, 0)),
            pl.BlockSpec((pixels, 128), lambda i: (0, 0)),
            pl.BlockSpec((pixels, 128), lambda i: (0, 0)),
        ],
        out_specs=[
            pl.BlockSpec((pixels, 128), lambda i: (0, 0)),
            pl.BlockSpec((pixels, 128), lambda i: (0, 0)),
        ],
        out_shape=[
            jax.ShapeDtypeStruct((pixels, 128), jnp.float32),
            jax.ShapeDtypeStruct((pixels, 128), jnp.float32),
        ],
        cost_estimate=pl.CostEstimate(
            flops=2 * pixels * count * (channels + 256),
            transcendentals=pixels * count,
            bytes_accessed=2 * count * (channels + 128) + 2 * pixels * channels + 16 * pixels * 128,
        ),
    )(features, block, weights, running_max, acc)


def deposit_table(bits):
    table = np.zeros((1 << len(bits),), np.int32)
    for q in range(table.shape[0]):
        table[q] = sum(((q >> i) & 1) << b for i, b in enumerate(bits))
    return table


def per_device(frame1, frame2, context, hidden_init, offsets, w_motion, w_row, w_col):
    band_rows, image_width, channels = frame1.shape
    bands = lax.axis_size("band")
    total_rows = band_rows * bands
    band = lax.axis_index("band")
    row_first = band * band_rows
    strips = scaled_strips(frame2, math.sqrt(channels))
    grid_cols = strips.shape[1]
    target_row, target_col, pixel_row, pixel_col = lookup_targets(
        offsets, row_first, total_rows, image_width
    )
    pixel_count = band_rows * image_width
    features = frame1.reshape(pixel_count, channels)
    deposit = deposit_table(GATHER_BITS)
    state = (
        jnp.full((pixel_count, 128), -jnp.inf, jnp.float32),
        jnp.zeros((pixel_count, 128), jnp.float32),
    )
    held = strips.reshape(band_rows * grid_cols, channels)
    state = match_block(state, features, held, band[None], grid_cols)
    for step, bit in enumerate(GATHER_BITS):
        flip = 1 << bit
        pairs = [(i, i ^ flip) for i in range(bands)]
        got = lax.ppermute(held, "band", pairs)
        got_rows = (band ^ flip) ^ jnp.asarray(deposit[: 1 << step])
        settled = state
        state = match_block(state, features, got, got_rows, grid_cols)
        if step + 1 < len(GATHER_BITS):
            held = jnp.concatenate([held, got], axis=0)
            held, settled = lax.optimization_barrier((held, settled))
    running_max, acc = state
    denominator = acc[:, 0]
    flow_row = (acc[:, 1] / denominator / total_rows).reshape(
        band_rows, image_width
    ) - pixel_row.astype(jnp.float32) / total_rows
    flow_col = (
        (8.0 * (acc[:, 2] / denominator) + 3.5) / image_width
    ).reshape(band_rows, image_width) - pixel_col.astype(jnp.float32) / image_width
    pieces = [held, got]
    inverse = jnp.asarray(np.argsort(deposit).astype(np.int32))
    reach = 4
    window = []
    for shift in range(-reach, reach + 1):
        block = inverse[jnp.clip(band + shift, 0, total_rows - 1) ^ band]
        chosen = None
        first_block = 0
        for piece in pieces:
            count = piece.shape[0] // grid_cols
            local = jnp.clip(block - first_block, 0, count - 1)
            part = lax.dynamic_slice_in_dim(piece, local * grid_cols, grid_cols, 0)
            chosen = part if chosen is None else jnp.where(block >= first_block, part, chosen)
            first_block += count
        window.append(chosen)
    window = jnp.concatenate(window, axis=0)
    near = lax.dot_general(
        features, window, (((1,), (1,)), ((), ())), preferred_element_type=jnp.float32
    )
    t_row = target_row.reshape(pixel_count)
    t_col = target_col.reshape(pixel_count)
    valid = t_row >= 0
    slot = (t_row - band + reach) * grid_cols + t_col
    hit = jnp.arange(near.shape[1], dtype=jnp.int32)[None, :] == slot[:, None]
    found = jnp.sum(jnp.where(hit, near, 0.0), axis=1)
    lookup = jnp.where(valid, found, 0.0)
    lookup = lookup.reshape(band_rows, image_width)
    motion = jax.nn.relu(
        flow_row[..., None] * w_motion[0]
        + flow_col[..., None] * w_motion[1]
        + lookup[..., None] * w_motion[2]
    ).astype(jnp.bfloat16)
    inputs = jnp.concatenate([context, motion], axis=-1)
    width_h = hidden_init.shape[-1]
    from_row = conv_valid(pad_columns(inputs), w_row[:, width_h:, :], 1)
    hidden = hidden_init.astype(jnp.float32)
    from_col = None
    for iteration in range(ITERS):
        hidden = row_pass(hidden, from_row, w_row)
        hidden, from_col = column_pass_each(
            hidden, from_col, w_col, inputs if iteration == 0 else None
        )
    return (hidden, jnp.stack([flow_row, flow_col]))


def solution(mesh):
    return jax.shard_map(
        per_device,
        mesh=mesh,
        in_specs=(
            P("band", "pair", None),
            P("band", "pair", None),
            P("band", "pair", None),
            P("band", "pair", None),
            P(None, "band", "pair"),
            P(),
            P(),
            P(),
        ),
        out_specs=(P("band", "pair", None), P(None, "band", "pair")),
        check_vma=False,
    )
```

```python
import math

import numpy as np

import jax
import jax.numpy as jnp
from jax import lax
from jax.experimental import pallas as pl
from jax.sharding import PartitionSpec as P

ITERS = 2


def passed_along(array, axis, by):
    count = lax.axis_size(axis)
    pairs = [(i, i + by) for i in range(count) if 0 <= i + by < count]
    return lax.ppermute(array, axis, pairs)


def pool_strips(frame2):
    band_rows, image_width, channels = frame2.shape
    blocks = frame2.astype(jnp.float32).reshape(band_rows, image_width // 8, 8, channels)
    return (jnp.sum(blocks, axis=2) / 2.0).astype(jnp.bfloat16)


def scaled_strips(frame2, scale):
    band_rows, image_width, channels = frame2.shape
    blocks = frame2.astype(jnp.float32).reshape(band_rows, image_width // 8, 8, channels)
    return (jnp.sum(blocks, axis=2) / (2.0 * scale)).astype(jnp.bfloat16)


def lookup_targets(offsets, row_first, total_rows, image_width):
    band_rows = offsets.shape[1]
    pixel_row = (
        row_first
        + jnp.arange(band_rows, dtype=jnp.int32)[:, None]
        + jnp.zeros((1, image_width), jnp.int32)
    )
    pixel_col = jnp.arange(image_width, dtype=jnp.int32)[None, :]
    target_row = pixel_row + offsets[0]
    target_col = pixel_col // 8 + offsets[1]
    inside = (
        (target_row >= 0)
        & (target_row < total_rows)
        & (target_col >= 0)
        & (target_col < image_width // 8)
    )
    target_row = jnp.where(inside, target_row, -1)
    target_col = jnp.where(inside, target_col, -1)
    return (target_row, target_col, pixel_row, pixel_col)


def strip_step(
    state, feature_rows, strip_block, row_zero, total_rows, image_width, target_row, target_col
):
    block_rows, grid_cols, channels = strip_block.shape
    scores = jnp.dot(
        feature_rows,
        strip_block.reshape(block_rows * grid_cols, channels).T,
        preferred_element_type=jnp.float32,
    ) / math.sqrt(channels)
    running_max, denominator, acc_row, acc_col, lookup = state
    new_max = jnp.maximum(running_max, jnp.max(scores, axis=1))
    shrink = jnp.exp(running_max - new_max)
    exponent = jnp.exp(scores - new_max[:, None]).reshape(-1, block_rows, grid_cols)
    strip_row = row_zero + jnp.arange(block_rows, dtype=jnp.int32)
    column_ids = jnp.arange(grid_cols, dtype=jnp.int32)
    row_centre = strip_row.astype(jnp.float32) / total_rows
    col_centre = ((8 * column_ids).astype(jnp.float32) + 3.5) / image_width
    row_weight = jnp.sum(exponent, axis=2)
    col_weight = jnp.sum(exponent, axis=1)
    scores_grid = scores.reshape(-1, block_rows, grid_cols)
    hit = (strip_row[None, :, None] == target_row[:, None, None]) & (
        column_ids[None, None, :] == target_col[:, None, None]
    )
    found = jnp.sum(jnp.where(hit, scores_grid, 0.0), axis=(1, 2))
    return (
        new_max,
        denominator * shrink + jnp.sum(row_weight, axis=1),
        acc_row * shrink + jnp.sum(row_weight * row_centre[None, :], axis=1),
        acc_col * shrink + jnp.sum(col_weight * col_centre[None, :], axis=1),
        lookup + found,
    )


def conv_valid(source, weight, conv_axis):
    out_count = source.shape[conv_axis] - 4
    summed = None
    for kernel_tap in range(5):
        tap_slice = lax.slice_in_dim(source, kernel_tap, kernel_tap + out_count, axis=conv_axis)
        tap_term = jnp.dot(
            tap_slice.reshape(-1, tap_slice.shape[-1]),
            weight[kernel_tap],
            preferred_element_type=jnp.float32,
        )
        summed = tap_term if summed is None else summed + tap_term
    out_shape = tuple(tap_slice.shape[:-1]) + (weight.shape[-1],)
    return summed.reshape(out_shape)


def pad_columns(source):
    return jnp.pad(source, ((0, 0), (2, 2), (0, 0)))


def rows_around(source, depth, mover):
    above = [
        mover(source, offset)
        for offset in list(range(depth, 0, -1)) + list(range(-1, -depth - 1, -1))
    ]
    return jnp.concatenate(above[:depth] + [source] + above[depth:], axis=0)


def row_pass(hidden, from_inputs, weight):
    width_h = hidden.shape[-1]
    hidden_half = lax.optimization_barrier(hidden.astype(jnp.bfloat16))
    gate_pair = jax.nn.sigmoid(
        conv_valid(pad_columns(hidden_half), weight[:, :width_h, : 2 * width_h], 1)
        + from_inputs[..., : 2 * width_h]
    )
    update_gate = gate_pair[..., :width_h]
    reset_gate = gate_pair[..., width_h:]
    gated = (reset_gate * hidden_half.astype(jnp.float32)).astype(jnp.bfloat16)
    candidate = jnp.tanh(
        conv_valid(pad_columns(gated), weight[:, :width_h, 2 * width_h :], 1)
        + from_inputs[..., 2 * width_h :]
    )
    return (1.0 - update_gate) * hidden + update_gate * candidate


def column_pass_each(hidden, from_inputs, weight, inputs=None):
    width_h = hidden.shape[-1]
    hidden_half = lax.optimization_barrier(hidden.astype(jnp.bfloat16))
    mover = lambda source, offset: passed_along(source, "band", offset)
    if inputs is None:
        hidden_ext = rows_around(hidden_half, 2, mover)
    else:
        joined_ext = rows_around(jnp.concatenate([hidden_half, inputs], axis=-1), 2, mover)
        hidden_ext = joined_ext[..., :width_h]
        from_inputs = conv_valid(joined_ext[..., width_h:], weight[:, width_h:, :], 0)
    gate_pair = jax.nn.sigmoid(
        conv_valid(hidden_ext, weight[:, :width_h, : 2 * width_h], 0)
        + from_inputs[..., : 2 * width_h]
    )
    update_gate = gate_pair[..., :width_h]
    reset_gate = gate_pair[..., width_h:]
    gated = (reset_gate * hidden_half.astype(jnp.float32)).astype(jnp.bfloat16)
    gated_ext = rows_around(gated, 2, mover)
    candidate = jnp.tanh(
        conv_valid(gated_ext, weight[:, :width_h, 2 * width_h :], 0)
        + from_inputs[..., 2 * width_h :]
    )
    return ((1.0 - update_gate) * hidden + update_gate * candidate, from_inputs)


GATHER_BITS = (4, 3, 2, 7, 6, 5, 1, 0)


def match_kernel(f1_ref, s_ref, w_ref, m_in, a_in, m_out, a_out):
    @pl.when(pl.program_id(0) == 0)
    def _():
        m_out[...] = m_in[...]
        a_out[...] = a_in[...]

    scores = lax.dot_general(
        f1_ref[...], s_ref[...], (((1,), (1,)), ((), ())), preferred_element_type=jnp.float32
    )
    m_old = m_out[:, 0:1]
    m_new = jnp.maximum(m_old, jnp.max(scores, axis=1, keepdims=True))
    p = jnp.exp(scores - m_new)
    shrink = jnp.exp(m_old - m_new)
    p_hi = p.astype(jnp.bfloat16)
    p_lo = (p - p_hi.astype(jnp.float32)).astype(jnp.bfloat16)
    w = w_ref[...]
    part = jnp.dot(p_hi, w, preferred_element_type=jnp.float32) + jnp.dot(
        p_lo, w, preferred_element_type=jnp.float32
    )
    a_out[...] = a_out[...] * shrink + part
    m_out[...] = jnp.broadcast_to(m_new, m_out.shape)


def match_block(state, features, block, block_rows, grid_cols):
    count, channels = block.shape
    pixels = features.shape[0]
    tile = min(count, 768)
    strip_row = jnp.repeat(block_rows, grid_cols).astype(jnp.float32)
    strip_col = (jnp.arange(count, dtype=jnp.int32) % grid_cols).astype(jnp.float32)
    weights = jnp.concatenate(
        [
            jnp.ones((count, 1), jnp.float32),
            strip_row[:, None],
            strip_col[:, None],
            jnp.zeros((count, 125), jnp.float32),
        ],
        axis=1,
    ).astype(jnp.bfloat16)
    running_max, acc = state
    return pl.pallas_call(
        match_kernel,
        grid=(count // tile,),
        in_specs=[
            pl.BlockSpec((pixels, channels), lambda i: (0, 0)),
            pl.BlockSpec((tile, channels), lambda i: (i, 0)),
            pl.BlockSpec((tile, 128), lambda i: (i, 0)),
            pl.BlockSpec((pixels, 128), lambda i: (0, 0)),
            pl.BlockSpec((pixels, 128), lambda i: (0, 0)),
        ],
        out_specs=[
            pl.BlockSpec((pixels, 128), lambda i: (0, 0)),
            pl.BlockSpec((pixels, 128), lambda i: (0, 0)),
        ],
        out_shape=[
            jax.ShapeDtypeStruct((pixels, 128), jnp.float32),
            jax.ShapeDtypeStruct((pixels, 128), jnp.float32),
        ],
        cost_estimate=pl.CostEstimate(
            flops=2 * pixels * count * (channels + 256),
            transcendentals=pixels * count,
            bytes_accessed=2 * count * (channels + 128) + 2 * pixels * channels + 16 * pixels * 128,
        ),
    )(features, block, weights, running_max, acc)


def gather_partner(device, step, where):
    bit = GATHER_BITS[step]
    if bit != 1:
        return device ^ (1 << bit)
    z = (device >> 1) & 15
    shifted = ((((z + 15) % 16) ^ 1) + 1) % 16
    partner_z = where((device & 1) == 0, z ^ 1, shifted)
    return device - (z << 1) + (partner_z << 1)


def gather_tables(bands):
    devices = np.arange(bands, dtype=np.int64)
    rows = devices[:, None]
    for step in range(len(GATHER_BITS)):
        rows = np.concatenate([rows, rows[gather_partner(devices, step, np.where)]], axis=1)
    places = np.zeros_like(rows)
    for device in range(bands):
        places[device, rows[device]] = np.arange(rows.shape[1])
    return rows.astype(np.int16), places.astype(np.int16)


def per_device(frame1, frame2, context, hidden_init, offsets, w_motion, w_row, w_col):
    band_rows, image_width, channels = frame1.shape
    bands = lax.axis_size("band")
    total_rows = band_rows * bands
    band = lax.axis_index("band")
    row_first = band * band_rows
    strips = scaled_strips(frame2, math.sqrt(channels))
    grid_cols = strips.shape[1]
    target_row, target_col, pixel_row, pixel_col = lookup_targets(
        offsets, row_first, total_rows, image_width
    )
    pixel_count = band_rows * image_width
    features = frame1.reshape(pixel_count, channels)
    row_table, place_table = gather_tables(bands)
    state = (
        jnp.full((pixel_count, 128), -jnp.inf, jnp.float32),
        jnp.zeros((pixel_count, 128), jnp.float32),
    )
    held = strips.reshape(band_rows * grid_cols, channels)
    state = match_block(state, features, held, band[None], grid_cols)
    for step, bit in enumerate(GATHER_BITS):
        pairs = [(i, int(gather_partner(i, step, np.where))) for i in range(bands)]
        got = lax.ppermute(held, "band", pairs)
        partner = gather_partner(band, step, jnp.where)
        got_rows = lax.dynamic_index_in_dim(
            jnp.asarray(row_table[:, : 1 << step]), partner, 0, keepdims=False
        ).astype(jnp.int32)
        settled = state
        state = match_block(state, features, got, got_rows, grid_cols)
        if step + 1 < len(GATHER_BITS):
            held = jnp.concatenate([held, got], axis=0)
            held, settled = lax.optimization_barrier((held, settled))
    running_max, acc = state
    denominator = acc[:, 0]
    flow_row = (acc[:, 1] / denominator / total_rows).reshape(
        band_rows, image_width
    ) - pixel_row.astype(jnp.float32) / total_rows
    flow_col = (
        (8.0 * (acc[:, 2] / denominator) + 3.5) / image_width
    ).reshape(band_rows, image_width) - pixel_col.astype(jnp.float32) / image_width
    places = lax.dynamic_index_in_dim(jnp.asarray(place_table), band, 0, keepdims=False)
    t_row = target_row.reshape(pixel_count)
    t_col = target_col.reshape(pixel_count)
    valid = t_row >= 0
    place = places.astype(jnp.int32)[jnp.where(valid, t_row, 0)] * grid_cols + jnp.where(
        valid, t_col, 0
    )
    half = held.shape[0]
    picked = jnp.where(
        (place < half)[:, None],
        jnp.take(held, jnp.minimum(place, half - 1), axis=0),
        jnp.take(got, jnp.maximum(place - half, 0), axis=0),
    )
    found = jnp.sum(features.astype(jnp.float32) * picked.astype(jnp.float32), axis=1)
    lookup = jnp.where(valid, found, 0.0)
    lookup = lookup.reshape(band_rows, image_width)
    motion = jax.nn.relu(
        flow_row[..., None] * w_motion[0]
        + flow_col[..., None] * w_motion[1]
        + lookup[..., None] * w_motion[2]
    ).astype(jnp.bfloat16)
    inputs = jnp.concatenate([context, motion], axis=-1)
    width_h = hidden_init.shape[-1]
    from_row = conv_valid(pad_columns(inputs), w_row[:, width_h:, :], 1)
    hidden = hidden_init.astype(jnp.float32)
    from_col = None
    for iteration in range(ITERS):
        hidden = row_pass(hidden, from_row, w_row)
        hidden, from_col = column_pass_each(
            hidden, from_col, w_col, inputs if iteration == 0 else None
        )
    return (hidden, jnp.stack([flow_row, flow_col]))


def solution(mesh):
    return jax.shard_map(
        per_device,
        mesh=mesh,
        in_specs=(
            P("band", "pair", None),
            P("band", "pair", None),
            P("band", "pair", None),
            P("band", "pair", None),
            P(None, "band", "pair"),
            P(),
            P(),
            P(),
        ),
        out_specs=(P("band", "pair", None), P(None, "band", "pair")),
        check_vma=False,
    )
```

```python
import math

import numpy as np

import jax
import jax.numpy as jnp
from jax import lax
from jax.experimental import pallas as pl
from jax.sharding import PartitionSpec as P

ITERS = 2


def passed_along(array, axis, by):
    count = lax.axis_size(axis)
    pairs = [(i, i + by) for i in range(count) if 0 <= i + by < count]
    return lax.ppermute(array, axis, pairs)


def pool_strips(frame2):
    band_rows, image_width, channels = frame2.shape
    blocks = frame2.astype(jnp.float32).reshape(band_rows, image_width // 8, 8, channels)
    return (jnp.sum(blocks, axis=2) / 2.0).astype(jnp.bfloat16)


def scaled_strips(frame2, scale):
    band_rows, image_width, channels = frame2.shape
    blocks = frame2.astype(jnp.float32).reshape(band_rows, image_width // 8, 8, channels)
    return (jnp.sum(blocks, axis=2) / (2.0 * scale)).astype(jnp.bfloat16)


def lookup_targets(offsets, row_first, total_rows, image_width):
    band_rows = offsets.shape[1]
    pixel_row = (
        row_first
        + jnp.arange(band_rows, dtype=jnp.int32)[:, None]
        + jnp.zeros((1, image_width), jnp.int32)
    )
    pixel_col = jnp.arange(image_width, dtype=jnp.int32)[None, :]
    target_row = pixel_row + offsets[0]
    target_col = pixel_col // 8 + offsets[1]
    inside = (
        (target_row >= 0)
        & (target_row < total_rows)
        & (target_col >= 0)
        & (target_col < image_width // 8)
    )
    target_row = jnp.where(inside, target_row, -1)
    target_col = jnp.where(inside, target_col, -1)
    return (target_row, target_col, pixel_row, pixel_col)


def strip_step(
    state, feature_rows, strip_block, row_zero, total_rows, image_width, target_row, target_col
):
    block_rows, grid_cols, channels = strip_block.shape
    scores = jnp.dot(
        feature_rows,
        strip_block.reshape(block_rows * grid_cols, channels).T,
        preferred_element_type=jnp.float32,
    ) / math.sqrt(channels)
    running_max, denominator, acc_row, acc_col, lookup = state
    new_max = jnp.maximum(running_max, jnp.max(scores, axis=1))
    shrink = jnp.exp(running_max - new_max)
    exponent = jnp.exp(scores - new_max[:, None]).reshape(-1, block_rows, grid_cols)
    strip_row = row_zero + jnp.arange(block_rows, dtype=jnp.int32)
    column_ids = jnp.arange(grid_cols, dtype=jnp.int32)
    row_centre = strip_row.astype(jnp.float32) / total_rows
    col_centre = ((8 * column_ids).astype(jnp.float32) + 3.5) / image_width
    row_weight = jnp.sum(exponent, axis=2)
    col_weight = jnp.sum(exponent, axis=1)
    scores_grid = scores.reshape(-1, block_rows, grid_cols)
    hit = (strip_row[None, :, None] == target_row[:, None, None]) & (
        column_ids[None, None, :] == target_col[:, None, None]
    )
    found = jnp.sum(jnp.where(hit, scores_grid, 0.0), axis=(1, 2))
    return (
        new_max,
        denominator * shrink + jnp.sum(row_weight, axis=1),
        acc_row * shrink + jnp.sum(row_weight * row_centre[None, :], axis=1),
        acc_col * shrink + jnp.sum(col_weight * col_centre[None, :], axis=1),
        lookup + found,
    )


def conv_valid(source, weight, conv_axis):
    out_count = source.shape[conv_axis] - 4
    summed = None
    for kernel_tap in range(5):
        tap_slice = lax.slice_in_dim(source, kernel_tap, kernel_tap + out_count, axis=conv_axis)
        tap_term = jnp.dot(
            tap_slice.reshape(-1, tap_slice.shape[-1]),
            weight[kernel_tap],
            preferred_element_type=jnp.float32,
        )
        summed = tap_term if summed is None else summed + tap_term
    out_shape = tuple(tap_slice.shape[:-1]) + (weight.shape[-1],)
    return summed.reshape(out_shape)


def pad_columns(source):
    return jnp.pad(source, ((0, 0), (2, 2), (0, 0)))


def rows_around(source, depth, mover):
    above = [
        mover(source, offset)
        for offset in list(range(depth, 0, -1)) + list(range(-1, -depth - 1, -1))
    ]
    return jnp.concatenate(above[:depth] + [source] + above[depth:], axis=0)


def row_pass(hidden, from_inputs, weight):
    width_h = hidden.shape[-1]
    hidden_half = lax.optimization_barrier(hidden.astype(jnp.bfloat16))
    gate_pair = jax.nn.sigmoid(
        conv_valid(pad_columns(hidden_half), weight[:, :width_h, : 2 * width_h], 1)
        + from_inputs[..., : 2 * width_h]
    )
    update_gate = gate_pair[..., :width_h]
    reset_gate = gate_pair[..., width_h:]
    gated = (reset_gate * hidden_half.astype(jnp.float32)).astype(jnp.bfloat16)
    candidate = jnp.tanh(
        conv_valid(pad_columns(gated), weight[:, :width_h, 2 * width_h :], 1)
        + from_inputs[..., 2 * width_h :]
    )
    return (1.0 - update_gate) * hidden + update_gate * candidate


def column_pass_each(hidden, from_inputs, weight, inputs=None):
    width_h = hidden.shape[-1]
    hidden_half = lax.optimization_barrier(hidden.astype(jnp.bfloat16))
    mover = lambda source, offset: passed_along(source, "band", offset)
    if inputs is None:
        hidden_ext = rows_around(hidden_half, 2, mover)
    else:
        joined_ext = rows_around(jnp.concatenate([hidden_half, inputs], axis=-1), 2, mover)
        hidden_ext = joined_ext[..., :width_h]
        from_inputs = conv_valid(joined_ext[..., width_h:], weight[:, width_h:, :], 0)
    gate_pair = jax.nn.sigmoid(
        conv_valid(hidden_ext, weight[:, :width_h, : 2 * width_h], 0)
        + from_inputs[..., : 2 * width_h]
    )
    update_gate = gate_pair[..., :width_h]
    reset_gate = gate_pair[..., width_h:]
    gated = (reset_gate * hidden_half.astype(jnp.float32)).astype(jnp.bfloat16)
    gated_ext = rows_around(gated, 2, mover)
    candidate = jnp.tanh(
        conv_valid(gated_ext, weight[:, :width_h, 2 * width_h :], 0)
        + from_inputs[..., 2 * width_h :]
    )
    return ((1.0 - update_gate) * hidden + update_gate * candidate, from_inputs)


GATHER_BITS = (4, 3, 2, 7, 6, 5, 1, 0)


def match_kernel(f1_ref, s_ref, w_ref, m_in, a_in, m_out, a_out):
    @pl.when(pl.program_id(0) == 0)
    def _():
        m_out[...] = m_in[...]
        a_out[...] = a_in[...]

    scores = lax.dot_general(
        f1_ref[...], s_ref[...], (((1,), (1,)), ((), ())), preferred_element_type=jnp.float32
    )
    m_old = m_out[:, 0:1]
    m_new = jnp.maximum(m_old, jnp.max(scores, axis=1, keepdims=True))
    p = jnp.exp(scores - m_new)
    shrink = jnp.exp(m_old - m_new)
    p_hi = p.astype(jnp.bfloat16)
    p_lo = (p - p_hi.astype(jnp.float32)).astype(jnp.bfloat16)
    w = w_ref[...]
    part = jnp.dot(p_hi, w, preferred_element_type=jnp.float32) + jnp.dot(
        p_lo, w, preferred_element_type=jnp.float32
    )
    a_out[...] = a_out[...] * shrink + part
    m_out[...] = jnp.broadcast_to(m_new, m_out.shape)


def match_block(state, features, block, block_rows, grid_cols):
    count, channels = block.shape
    pixels = features.shape[0]
    tile = min(count, 1536)
    strip_row = jnp.repeat(block_rows, grid_cols).astype(jnp.float32)
    strip_col = (jnp.arange(count, dtype=jnp.int32) % grid_cols).astype(jnp.float32)
    weights = jnp.concatenate(
        [
            jnp.ones((count, 1), jnp.float32),
            strip_row[:, None],
            strip_col[:, None],
            jnp.zeros((count, 125), jnp.float32),
        ],
        axis=1,
    ).astype(jnp.bfloat16)
    running_max, acc = state
    return pl.pallas_call(
        match_kernel,
        grid=(count // tile,),
        in_specs=[
            pl.BlockSpec((pixels, channels), lambda i: (0, 0)),
            pl.BlockSpec((tile, channels), lambda i: (i, 0)),
            pl.BlockSpec((tile, 128), lambda i: (i, 0)),
            pl.BlockSpec((pixels, 128), lambda i: (0, 0)),
            pl.BlockSpec((pixels, 128), lambda i: (0, 0)),
        ],
        out_specs=[
            pl.BlockSpec((pixels, 128), lambda i: (0, 0)),
            pl.BlockSpec((pixels, 128), lambda i: (0, 0)),
        ],
        out_shape=[
            jax.ShapeDtypeStruct((pixels, 128), jnp.float32),
            jax.ShapeDtypeStruct((pixels, 128), jnp.float32),
        ],
        cost_estimate=pl.CostEstimate(
            flops=2 * pixels * count * (channels + 256),
            transcendentals=pixels * count,
            bytes_accessed=2 * count * (channels + 128) + 2 * pixels * channels + 16 * pixels * 128,
        ),
    )(features, block, weights, running_max, acc)


def gather_partner(device, step, where):
    bit = GATHER_BITS[step]
    if bit != 1:
        return device ^ (1 << bit)
    z = (device >> 1) & 15
    shifted = ((((z + 15) % 16) ^ 1) + 1) % 16
    partner_z = where((device & 1) == 0, z ^ 1, shifted)
    return device - (z << 1) + (partner_z << 1)


def gather_tables(bands):
    devices = np.arange(bands, dtype=np.int64)
    rows = devices[:, None]
    for step in range(len(GATHER_BITS)):
        rows = np.concatenate([rows, rows[gather_partner(devices, step, np.where)]], axis=1)
    places = np.zeros_like(rows)
    for device in range(bands):
        places[device, rows[device]] = np.arange(rows.shape[1])
    return rows.astype(np.int16), places.astype(np.int16)


def per_device(frame1, frame2, context, hidden_init, offsets, w_motion, w_row, w_col):
    band_rows, image_width, channels = frame1.shape
    bands = lax.axis_size("band")
    total_rows = band_rows * bands
    band = lax.axis_index("band")
    row_first = band * band_rows
    strips = scaled_strips(frame2, math.sqrt(channels))
    grid_cols = strips.shape[1]
    target_row, target_col, pixel_row, pixel_col = lookup_targets(
        offsets, row_first, total_rows, image_width
    )
    pixel_count = band_rows * image_width
    features = frame1.reshape(pixel_count, channels)
    row_table, place_table = gather_tables(bands)
    state = (
        jnp.full((pixel_count, 128), -jnp.inf, jnp.float32),
        jnp.zeros((pixel_count, 128), jnp.float32),
    )
    held = strips.reshape(band_rows * grid_cols, channels)
    state = match_block(state, features, held, band[None], grid_cols)
    for step, bit in enumerate(GATHER_BITS):
        pairs = [(i, int(gather_partner(i, step, np.where))) for i in range(bands)]
        got = lax.ppermute(held, "band", pairs)
        partner = gather_partner(band, step, jnp.where)
        got_rows = lax.dynamic_index_in_dim(
            jnp.asarray(row_table[:, : 1 << step]), partner, 0, keepdims=False
        ).astype(jnp.int32)
        settled = state
        state = match_block(state, features, got, got_rows, grid_cols)
        if step + 1 < len(GATHER_BITS):
            held = jnp.concatenate([held, got], axis=0)
            held, settled = lax.optimization_barrier((held, settled))
    running_max, acc = state
    denominator = acc[:, 0]
    flow_row = (acc[:, 1] / denominator / total_rows).reshape(
        band_rows, image_width
    ) - pixel_row.astype(jnp.float32) / total_rows
    flow_col = (
        (8.0 * (acc[:, 2] / denominator) + 3.5) / image_width
    ).reshape(band_rows, image_width) - pixel_col.astype(jnp.float32) / image_width
    places = lax.dynamic_index_in_dim(jnp.asarray(place_table), band, 0, keepdims=False)
    t_row = target_row.reshape(pixel_count)
    t_col = target_col.reshape(pixel_count)
    valid = t_row >= 0
    place = places.astype(jnp.int32)[jnp.where(valid, t_row, 0)] * grid_cols + jnp.where(
        valid, t_col, 0
    )
    half = held.shape[0]
    picked = jnp.where(
        (place < half)[:, None],
        jnp.take(held, jnp.minimum(place, half - 1), axis=0),
        jnp.take(got, jnp.maximum(place - half, 0), axis=0),
    )
    found = jnp.sum(features.astype(jnp.float32) * picked.astype(jnp.float32), axis=1)
    lookup = jnp.where(valid, found, 0.0)
    lookup = lookup.reshape(band_rows, image_width)
    motion = jax.nn.relu(
        flow_row[..., None] * w_motion[0]
        + flow_col[..., None] * w_motion[1]
        + lookup[..., None] * w_motion[2]
    ).astype(jnp.bfloat16)
    inputs = jnp.concatenate([context, motion], axis=-1)
    width_h = hidden_init.shape[-1]
    from_row = conv_valid(pad_columns(inputs), w_row[:, width_h:, :], 1)
    hidden = hidden_init.astype(jnp.float32)
    from_col = None
    for iteration in range(ITERS):
        hidden = row_pass(hidden, from_row, w_row)
        hidden, from_col = column_pass_each(
            hidden, from_col, w_col, inputs if iteration == 0 else None
        )
    return (hidden, jnp.stack([flow_row, flow_col]))


def solution(mesh):
    return jax.shard_map(
        per_device,
        mesh=mesh,
        in_specs=(
            P("band", "pair", None),
            P("band", "pair", None),
            P("band", "pair", None),
            P("band", "pair", None),
            P(None, "band", "pair"),
            P(),
            P(),
            P(),
        ),
        out_specs=(P("band", "pair", None), P(None, "band", "pair")),
        check_vma=False,
    )
```

```python
import math

import numpy as np

import jax
import jax.numpy as jnp
from jax import lax
from jax.experimental import pallas as pl
from jax.sharding import PartitionSpec as P

ITERS = 2


def passed_along(array, axis, by):
    count = lax.axis_size(axis)
    pairs = [(i, i + by) for i in range(count) if 0 <= i + by < count]
    return lax.ppermute(array, axis, pairs)


def pool_strips(frame2):
    band_rows, image_width, channels = frame2.shape
    blocks = frame2.astype(jnp.float32).reshape(band_rows, image_width // 8, 8, channels)
    return (jnp.sum(blocks, axis=2) / 2.0).astype(jnp.bfloat16)


def scaled_strips(frame2, scale):
    band_rows, image_width, channels = frame2.shape
    blocks = frame2.astype(jnp.float32).reshape(band_rows, image_width // 8, 8, channels)
    return (jnp.sum(blocks, axis=2) / (2.0 * scale)).astype(jnp.bfloat16)


def lookup_targets(offsets, row_first, total_rows, image_width):
    band_rows = offsets.shape[1]
    pixel_row = (
        row_first
        + jnp.arange(band_rows, dtype=jnp.int32)[:, None]
        + jnp.zeros((1, image_width), jnp.int32)
    )
    pixel_col = jnp.arange(image_width, dtype=jnp.int32)[None, :]
    target_row = pixel_row + offsets[0]
    target_col = pixel_col // 8 + offsets[1]
    inside = (
        (target_row >= 0)
        & (target_row < total_rows)
        & (target_col >= 0)
        & (target_col < image_width // 8)
    )
    target_row = jnp.where(inside, target_row, -1)
    target_col = jnp.where(inside, target_col, -1)
    return (target_row, target_col, pixel_row, pixel_col)


def strip_step(
    state, feature_rows, strip_block, row_zero, total_rows, image_width, target_row, target_col
):
    block_rows, grid_cols, channels = strip_block.shape
    scores = jnp.dot(
        feature_rows,
        strip_block.reshape(block_rows * grid_cols, channels).T,
        preferred_element_type=jnp.float32,
    ) / math.sqrt(channels)
    running_max, denominator, acc_row, acc_col, lookup = state
    new_max = jnp.maximum(running_max, jnp.max(scores, axis=1))
    shrink = jnp.exp(running_max - new_max)
    exponent = jnp.exp(scores - new_max[:, None]).reshape(-1, block_rows, grid_cols)
    strip_row = row_zero + jnp.arange(block_rows, dtype=jnp.int32)
    column_ids = jnp.arange(grid_cols, dtype=jnp.int32)
    row_centre = strip_row.astype(jnp.float32) / total_rows
    col_centre = ((8 * column_ids).astype(jnp.float32) + 3.5) / image_width
    row_weight = jnp.sum(exponent, axis=2)
    col_weight = jnp.sum(exponent, axis=1)
    scores_grid = scores.reshape(-1, block_rows, grid_cols)
    hit = (strip_row[None, :, None] == target_row[:, None, None]) & (
        column_ids[None, None, :] == target_col[:, None, None]
    )
    found = jnp.sum(jnp.where(hit, scores_grid, 0.0), axis=(1, 2))
    return (
        new_max,
        denominator * shrink + jnp.sum(row_weight, axis=1),
        acc_row * shrink + jnp.sum(row_weight * row_centre[None, :], axis=1),
        acc_col * shrink + jnp.sum(col_weight * col_centre[None, :], axis=1),
        lookup + found,
    )


def conv_valid(source, weight, conv_axis):
    out_count = source.shape[conv_axis] - 4
    summed = None
    for kernel_tap in range(5):
        tap_slice = lax.slice_in_dim(source, kernel_tap, kernel_tap + out_count, axis=conv_axis)
        tap_term = jnp.dot(
            tap_slice.reshape(-1, tap_slice.shape[-1]),
            weight[kernel_tap],
            preferred_element_type=jnp.float32,
        )
        summed = tap_term if summed is None else summed + tap_term
    out_shape = tuple(tap_slice.shape[:-1]) + (weight.shape[-1],)
    return summed.reshape(out_shape)


def pad_columns(source):
    return jnp.pad(source, ((0, 0), (2, 2), (0, 0)))


def rows_around(source, depth, mover):
    above = [
        mover(source, offset)
        for offset in list(range(depth, 0, -1)) + list(range(-1, -depth - 1, -1))
    ]
    return jnp.concatenate(above[:depth] + [source] + above[depth:], axis=0)


def row_pass(hidden, from_inputs, weight):
    width_h = hidden.shape[-1]
    hidden_half = lax.optimization_barrier(hidden.astype(jnp.bfloat16))
    gate_pair = jax.nn.sigmoid(
        conv_valid(pad_columns(hidden_half), weight[:, :width_h, : 2 * width_h], 1)
        + from_inputs[..., : 2 * width_h]
    )
    update_gate = gate_pair[..., :width_h]
    reset_gate = gate_pair[..., width_h:]
    gated = (reset_gate * hidden_half.astype(jnp.float32)).astype(jnp.bfloat16)
    candidate = jnp.tanh(
        conv_valid(pad_columns(gated), weight[:, :width_h, 2 * width_h :], 1)
        + from_inputs[..., 2 * width_h :]
    )
    return (1.0 - update_gate) * hidden + update_gate * candidate


def column_pass_each(hidden, from_inputs, weight, inputs=None):
    width_h = hidden.shape[-1]
    hidden_half = lax.optimization_barrier(hidden.astype(jnp.bfloat16))
    mover = lambda source, offset: passed_along(source, "band", offset)
    if inputs is None:
        hidden_ext = rows_around(hidden_half, 2, mover)
    else:
        joined_ext = rows_around(jnp.concatenate([hidden_half, inputs], axis=-1), 2, mover)
        hidden_ext = joined_ext[..., :width_h]
        from_inputs = conv_valid(joined_ext[..., width_h:], weight[:, width_h:, :], 0)
    gate_pair = jax.nn.sigmoid(
        conv_valid(hidden_ext, weight[:, :width_h, : 2 * width_h], 0)
        + from_inputs[..., : 2 * width_h]
    )
    update_gate = gate_pair[..., :width_h]
    reset_gate = gate_pair[..., width_h:]
    gated = (reset_gate * hidden_half.astype(jnp.float32)).astype(jnp.bfloat16)
    gated_ext = rows_around(gated, 2, mover)
    candidate = jnp.tanh(
        conv_valid(gated_ext, weight[:, :width_h, 2 * width_h :], 0)
        + from_inputs[..., 2 * width_h :]
    )
    return ((1.0 - update_gate) * hidden + update_gate * candidate, from_inputs)


GATHER_BITS = (4, 3, 2, 7, 6, 5, 1, 0)


def match_kernel(f1_ref, s_ref, w_ref, m_in, a_in, m_out, a_out):
    @pl.when(pl.program_id(0) == 0)
    def _():
        m_out[...] = m_in[...]
        a_out[...] = a_in[...]

    scores = lax.dot_general(
        f1_ref[...], s_ref[...], (((1,), (1,)), ((), ())), preferred_element_type=jnp.float32
    )
    m_old = m_out[:, 0:1]
    m_new = jnp.maximum(m_old, jnp.max(scores, axis=1, keepdims=True))
    p = jnp.exp(scores - m_new)
    shrink = jnp.exp(m_old - m_new)
    p_hi = p.astype(jnp.bfloat16)
    p_lo = (p - p_hi.astype(jnp.float32)).astype(jnp.bfloat16)
    w = w_ref[...]
    part = jnp.dot(p_hi, w, preferred_element_type=jnp.float32) + jnp.dot(
        p_lo, w, preferred_element_type=jnp.float32
    )
    a_out[...] = a_out[...] * shrink + part
    m_out[...] = jnp.broadcast_to(m_new, m_out.shape)


def match_block(state, features, block, block_rows, grid_cols):
    count, channels = block.shape
    pixels = features.shape[0]
    tile = min(count, 1536)
    strip_row = jnp.repeat(block_rows, grid_cols).astype(jnp.float32)
    strip_col = (jnp.arange(count, dtype=jnp.int32) % grid_cols).astype(jnp.float32)
    weights = jnp.concatenate(
        [
            jnp.ones((count, 1), jnp.float32),
            strip_row[:, None],
            strip_col[:, None],
            jnp.zeros((count, 125), jnp.float32),
        ],
        axis=1,
    ).astype(jnp.bfloat16)
    running_max, acc = state
    return pl.pallas_call(
        match_kernel,
        grid=(count // tile,),
        in_specs=[
            pl.BlockSpec((pixels, channels), lambda i: (0, 0)),
            pl.BlockSpec((tile, channels), lambda i: (i, 0)),
            pl.BlockSpec((tile, 128), lambda i: (i, 0)),
            pl.BlockSpec((pixels, 128), lambda i: (0, 0)),
            pl.BlockSpec((pixels, 128), lambda i: (0, 0)),
        ],
        out_specs=[
            pl.BlockSpec((pixels, 128), lambda i: (0, 0)),
            pl.BlockSpec((pixels, 128), lambda i: (0, 0)),
        ],
        out_shape=[
            jax.ShapeDtypeStruct((pixels, 128), jnp.float32),
            jax.ShapeDtypeStruct((pixels, 128), jnp.float32),
        ],
        cost_estimate=pl.CostEstimate(
            flops=2 * pixels * count * (channels + 256),
            transcendentals=pixels * count,
            bytes_accessed=2 * count * (channels + 128) + 2 * pixels * channels + 16 * pixels * 128,
        ),
    )(features, block, weights, running_max, acc)


def gather_partner(device, step, where):
    bit = GATHER_BITS[step]
    if bit != 1:
        return device ^ (1 << bit)
    z = (device >> 1) & 15
    shifted = ((((z + 15) % 16) ^ 1) + 1) % 16
    partner_z = where((device & 1) == 0, z ^ 1, shifted)
    return device - (z << 1) + (partner_z << 1)


def gather_tables(bands):
    devices = np.arange(bands, dtype=np.int64)
    rows = devices[:, None]
    for step in range(len(GATHER_BITS)):
        rows = np.concatenate([rows, rows[gather_partner(devices, step, np.where)]], axis=1)
    places = np.zeros_like(rows)
    for device in range(bands):
        places[device, rows[device]] = np.arange(rows.shape[1])
    return rows.astype(np.int16), places.astype(np.int16)


def per_device(frame1, frame2, context, hidden_init, offsets, w_motion, w_row, w_col):
    band_rows, image_width, channels = frame1.shape
    bands = lax.axis_size("band")
    total_rows = band_rows * bands
    band = lax.axis_index("band")
    row_first = band * band_rows
    strips = scaled_strips(frame2, math.sqrt(channels))
    grid_cols = strips.shape[1]
    target_row, target_col, pixel_row, pixel_col = lookup_targets(
        offsets, row_first, total_rows, image_width
    )
    pixel_count = band_rows * image_width
    features = frame1.reshape(pixel_count, channels)
    row_table, place_table = gather_tables(bands)
    state = (
        jnp.full((pixel_count, 128), -jnp.inf, jnp.float32),
        jnp.zeros((pixel_count, 128), jnp.float32),
    )
    held = strips.reshape(band_rows * grid_cols, channels)
    merged = 3
    own_rows = lax.dynamic_index_in_dim(jnp.asarray(row_table), band, 0, keepdims=False)
    for step, bit in enumerate(GATHER_BITS):
        pairs = [(i, int(gather_partner(i, step, np.where))) for i in range(bands)]
        got = lax.ppermute(held, "band", pairs)
        if step < merged:
            held = jnp.concatenate([held, got], axis=0)
            if step == merged - 1:
                start_rows = own_rows[: 1 << merged].astype(jnp.int32)
                state = match_block(state, features, held, start_rows, grid_cols)
            continue
        partner = gather_partner(band, step, jnp.where)
        got_rows = lax.dynamic_index_in_dim(
            jnp.asarray(row_table[:, : 1 << step]), partner, 0, keepdims=False
        ).astype(jnp.int32)
        settled = state
        state = match_block(state, features, got, got_rows, grid_cols)
        if step + 1 < len(GATHER_BITS):
            held = jnp.concatenate([held, got], axis=0)
            held, settled = lax.optimization_barrier((held, settled))
    running_max, acc = state
    denominator = acc[:, 0]
    flow_row = (acc[:, 1] / denominator / total_rows).reshape(
        band_rows, image_width
    ) - pixel_row.astype(jnp.float32) / total_rows
    flow_col = (
        (8.0 * (acc[:, 2] / denominator) + 3.5) / image_width
    ).reshape(band_rows, image_width) - pixel_col.astype(jnp.float32) / image_width
    places = lax.dynamic_index_in_dim(jnp.asarray(place_table), band, 0, keepdims=False)
    t_row = target_row.reshape(pixel_count)
    t_col = target_col.reshape(pixel_count)
    valid = t_row >= 0
    place = places.astype(jnp.int32)[jnp.where(valid, t_row, 0)] * grid_cols + jnp.where(
        valid, t_col, 0
    )
    half = held.shape[0]
    picked = jnp.where(
        (place < half)[:, None],
        jnp.take(held, jnp.minimum(place, half - 1), axis=0),
        jnp.take(got, jnp.maximum(place - half, 0), axis=0),
    )
    found = jnp.sum(features.astype(jnp.float32) * picked.astype(jnp.float32), axis=1)
    lookup = jnp.where(valid, found, 0.0)
    lookup = lookup.reshape(band_rows, image_width)
    motion = jax.nn.relu(
        flow_row[..., None] * w_motion[0]
        + flow_col[..., None] * w_motion[1]
        + lookup[..., None] * w_motion[2]
    ).astype(jnp.bfloat16)
    inputs = jnp.concatenate([context, motion], axis=-1)
    width_h = hidden_init.shape[-1]
    from_row = conv_valid(pad_columns(inputs), w_row[:, width_h:, :], 1)
    hidden = hidden_init.astype(jnp.float32)
    from_col = None
    for iteration in range(ITERS):
        hidden = row_pass(hidden, from_row, w_row)
        hidden, from_col = column_pass_each(
            hidden, from_col, w_col, inputs if iteration == 0 else None
        )
    return (hidden, jnp.stack([flow_row, flow_col]))


def solution(mesh):
    return jax.shard_map(
        per_device,
        mesh=mesh,
        in_specs=(
            P("band", "pair", None),
            P("band", "pair", None),
            P("band", "pair", None),
            P("band", "pair", None),
            P(None, "band", "pair"),
            P(),
            P(),
            P(),
        ),
        out_specs=(P("band", "pair", None), P(None, "band", "pair")),
        check_vma=False,
    )
```

```python
import math

import numpy as np

import jax
import jax.numpy as jnp
from jax import lax
from jax.experimental import pallas as pl
from jax.sharding import PartitionSpec as P

ITERS = 2


def passed_along(array, axis, by):
    count = lax.axis_size(axis)
    pairs = [(i, i + by) for i in range(count) if 0 <= i + by < count]
    return lax.ppermute(array, axis, pairs)


def pool_strips(frame2):
    band_rows, image_width, channels = frame2.shape
    blocks = frame2.astype(jnp.float32).reshape(band_rows, image_width // 8, 8, channels)
    return (jnp.sum(blocks, axis=2) / 2.0).astype(jnp.bfloat16)


def scaled_strips(frame2, scale):
    band_rows, image_width, channels = frame2.shape
    blocks = frame2.astype(jnp.float32).reshape(band_rows, image_width // 8, 8, channels)
    return (jnp.sum(blocks, axis=2) / (2.0 * scale)).astype(jnp.bfloat16)


def lookup_targets(offsets, row_first, total_rows, image_width):
    band_rows = offsets.shape[1]
    pixel_row = (
        row_first
        + jnp.arange(band_rows, dtype=jnp.int32)[:, None]
        + jnp.zeros((1, image_width), jnp.int32)
    )
    pixel_col = jnp.arange(image_width, dtype=jnp.int32)[None, :]
    target_row = pixel_row + offsets[0]
    target_col = pixel_col // 8 + offsets[1]
    inside = (
        (target_row >= 0)
        & (target_row < total_rows)
        & (target_col >= 0)
        & (target_col < image_width // 8)
    )
    target_row = jnp.where(inside, target_row, -1)
    target_col = jnp.where(inside, target_col, -1)
    return (target_row, target_col, pixel_row, pixel_col)


def strip_step(
    state, feature_rows, strip_block, row_zero, total_rows, image_width, target_row, target_col
):
    block_rows, grid_cols, channels = strip_block.shape
    scores = jnp.dot(
        feature_rows,
        strip_block.reshape(block_rows * grid_cols, channels).T,
        preferred_element_type=jnp.float32,
    ) / math.sqrt(channels)
    running_max, denominator, acc_row, acc_col, lookup = state
    new_max = jnp.maximum(running_max, jnp.max(scores, axis=1))
    shrink = jnp.exp(running_max - new_max)
    exponent = jnp.exp(scores - new_max[:, None]).reshape(-1, block_rows, grid_cols)
    strip_row = row_zero + jnp.arange(block_rows, dtype=jnp.int32)
    column_ids = jnp.arange(grid_cols, dtype=jnp.int32)
    row_centre = strip_row.astype(jnp.float32) / total_rows
    col_centre = ((8 * column_ids).astype(jnp.float32) + 3.5) / image_width
    row_weight = jnp.sum(exponent, axis=2)
    col_weight = jnp.sum(exponent, axis=1)
    scores_grid = scores.reshape(-1, block_rows, grid_cols)
    hit = (strip_row[None, :, None] == target_row[:, None, None]) & (
        column_ids[None, None, :] == target_col[:, None, None]
    )
    found = jnp.sum(jnp.where(hit, scores_grid, 0.0), axis=(1, 2))
    return (
        new_max,
        denominator * shrink + jnp.sum(row_weight, axis=1),
        acc_row * shrink + jnp.sum(row_weight * row_centre[None, :], axis=1),
        acc_col * shrink + jnp.sum(col_weight * col_centre[None, :], axis=1),
        lookup + found,
    )


def conv_valid(source, weight, conv_axis):
    out_count = source.shape[conv_axis] - 4
    summed = None
    for kernel_tap in range(5):
        tap_slice = lax.slice_in_dim(source, kernel_tap, kernel_tap + out_count, axis=conv_axis)
        tap_term = jnp.dot(
            tap_slice.reshape(-1, tap_slice.shape[-1]),
            weight[kernel_tap],
            preferred_element_type=jnp.float32,
        )
        summed = tap_term if summed is None else summed + tap_term
    out_shape = tuple(tap_slice.shape[:-1]) + (weight.shape[-1],)
    return summed.reshape(out_shape)


def pad_columns(source):
    return jnp.pad(source, ((0, 0), (2, 2), (0, 0)))


def rows_around(source, depth, mover):
    above = [
        mover(source, offset)
        for offset in list(range(depth, 0, -1)) + list(range(-1, -depth - 1, -1))
    ]
    return jnp.concatenate(above[:depth] + [source] + above[depth:], axis=0)


def row_pass(hidden, from_inputs, weight):
    width_h = hidden.shape[-1]
    hidden_half = lax.optimization_barrier(hidden.astype(jnp.bfloat16))
    gate_pair = jax.nn.sigmoid(
        conv_valid(pad_columns(hidden_half), weight[:, :width_h, : 2 * width_h], 1)
        + from_inputs[..., : 2 * width_h]
    )
    update_gate = gate_pair[..., :width_h]
    reset_gate = gate_pair[..., width_h:]
    gated = (reset_gate * hidden_half.astype(jnp.float32)).astype(jnp.bfloat16)
    candidate = jnp.tanh(
        conv_valid(pad_columns(gated), weight[:, :width_h, 2 * width_h :], 1)
        + from_inputs[..., 2 * width_h :]
    )
    return (1.0 - update_gate) * hidden + update_gate * candidate


def column_pass_each(hidden, from_inputs, weight, inputs=None):
    width_h = hidden.shape[-1]
    hidden_half = lax.optimization_barrier(hidden.astype(jnp.bfloat16))
    mover = lambda source, offset: passed_along(source, "band", offset)
    if inputs is None:
        hidden_ext = rows_around(hidden_half, 2, mover)
    else:
        joined_ext = rows_around(jnp.concatenate([hidden_half, inputs], axis=-1), 2, mover)
        hidden_ext = joined_ext[..., :width_h]
        from_inputs = conv_valid(joined_ext[..., width_h:], weight[:, width_h:, :], 0)
    gate_pair = jax.nn.sigmoid(
        conv_valid(hidden_ext, weight[:, :width_h, : 2 * width_h], 0)
        + from_inputs[..., : 2 * width_h]
    )
    update_gate = gate_pair[..., :width_h]
    reset_gate = gate_pair[..., width_h:]
    gated = (reset_gate * hidden_half.astype(jnp.float32)).astype(jnp.bfloat16)
    gated_ext = rows_around(gated, 2, mover)
    candidate = jnp.tanh(
        conv_valid(gated_ext, weight[:, :width_h, 2 * width_h :], 0)
        + from_inputs[..., 2 * width_h :]
    )
    return ((1.0 - update_gate) * hidden + update_gate * candidate, from_inputs)


GATHER_BITS = (4, 3, 2, 7, 6, 5, 1, 0)


def match_kernel(f1_ref, s_ref, w_ref, m_in, a_in, m_out, a_out):
    @pl.when(pl.program_id(0) == 0)
    def _():
        m_out[...] = m_in[...]
        a_out[...] = a_in[...]

    scores = lax.dot_general(
        f1_ref[...], s_ref[...], (((1,), (1,)), ((), ())), preferred_element_type=jnp.float32
    )
    m_old = m_out[:, 0:1]
    m_new = jnp.maximum(m_old, jnp.max(scores, axis=1, keepdims=True))
    p = jnp.exp(scores - m_new)
    shrink = jnp.exp(m_old - m_new)
    p_hi = p.astype(jnp.bfloat16)
    p_lo = (p - p_hi.astype(jnp.float32)).astype(jnp.bfloat16)
    w = w_ref[...]
    part = jnp.dot(p_hi, w, preferred_element_type=jnp.float32) + jnp.dot(
        p_lo, w, preferred_element_type=jnp.float32
    )
    a_out[...] = a_out[...] * shrink + part
    m_out[...] = jnp.broadcast_to(m_new, m_out.shape)


def match_block(state, features, block, block_rows, grid_cols):
    count, channels = block.shape
    pixels = features.shape[0]
    tile = min(count, 1536)
    strip_row = jnp.repeat(block_rows, grid_cols).astype(jnp.float32)
    strip_col = (jnp.arange(count, dtype=jnp.int32) % grid_cols).astype(jnp.float32)
    weights = jnp.concatenate(
        [
            jnp.ones((count, 1), jnp.float32),
            strip_row[:, None],
            strip_col[:, None],
            jnp.zeros((count, 125), jnp.float32),
        ],
        axis=1,
    ).astype(jnp.bfloat16)
    running_max, acc = state
    return pl.pallas_call(
        match_kernel,
        grid=(count // tile,),
        in_specs=[
            pl.BlockSpec((pixels, channels), lambda i: (0, 0)),
            pl.BlockSpec((tile, channels), lambda i: (i, 0)),
            pl.BlockSpec((tile, 128), lambda i: (i, 0)),
            pl.BlockSpec((pixels, 128), lambda i: (0, 0)),
            pl.BlockSpec((pixels, 128), lambda i: (0, 0)),
        ],
        out_specs=[
            pl.BlockSpec((pixels, 128), lambda i: (0, 0)),
            pl.BlockSpec((pixels, 128), lambda i: (0, 0)),
        ],
        out_shape=[
            jax.ShapeDtypeStruct((pixels, 128), jnp.float32),
            jax.ShapeDtypeStruct((pixels, 128), jnp.float32),
        ],
        cost_estimate=pl.CostEstimate(
            flops=2 * pixels * count * (channels + 256),
            transcendentals=pixels * count,
            bytes_accessed=2 * count * (channels + 128) + 2 * pixels * channels + 16 * pixels * 128,
        ),
    )(features, block, weights, running_max, acc)


def gather_partner(device, step, where):
    bit = GATHER_BITS[step]
    if bit != 1:
        return device ^ (1 << bit)
    z = (device >> 1) & 15
    shifted = ((((z + 15) % 16) ^ 1) + 1) % 16
    partner_z = where((device & 1) == 0, z ^ 1, shifted)
    return device - (z << 1) + (partner_z << 1)


def gather_tables(bands):
    devices = np.arange(bands, dtype=np.int64)
    rows = devices[:, None]
    for step in range(len(GATHER_BITS)):
        rows = np.concatenate([rows, rows[gather_partner(devices, step, np.where)]], axis=1)
    places = np.zeros_like(rows)
    for device in range(bands):
        places[device, rows[device]] = np.arange(rows.shape[1])
    return rows.astype(np.int16), places.astype(np.int16)


def per_device(frame1, frame2, context, hidden_init, offsets, w_motion, w_row, w_col):
    band_rows, image_width, channels = frame1.shape
    bands = lax.axis_size("band")
    total_rows = band_rows * bands
    band = lax.axis_index("band")
    row_first = band * band_rows
    strips = scaled_strips(frame2, math.sqrt(channels))
    grid_cols = strips.shape[1]
    target_row, target_col, pixel_row, pixel_col = lookup_targets(
        offsets, row_first, total_rows, image_width
    )
    pixel_count = band_rows * image_width
    features = frame1.reshape(pixel_count, channels)
    row_table, place_table = gather_tables(bands)
    state = (
        jnp.full((pixel_count, 128), -jnp.inf, jnp.float32),
        jnp.zeros((pixel_count, 128), jnp.float32),
    )
    held = strips.reshape(band_rows * grid_cols, channels)
    merged = 5
    own_rows = lax.dynamic_index_in_dim(jnp.asarray(row_table), band, 0, keepdims=False)
    for step, bit in enumerate(GATHER_BITS):
        pairs = [(i, int(gather_partner(i, step, np.where))) for i in range(bands)]
        got = lax.ppermute(held, "band", pairs)
        if step < merged:
            held = jnp.concatenate([held, got], axis=0)
            if step == merged - 1:
                start_rows = own_rows[: 1 << merged].astype(jnp.int32)
                state = match_block(state, features, held, start_rows, grid_cols)
            continue
        partner = gather_partner(band, step, jnp.where)
        got_rows = lax.dynamic_index_in_dim(
            jnp.asarray(row_table[:, : 1 << step]), partner, 0, keepdims=False
        ).astype(jnp.int32)
        settled = state
        state = match_block(state, features, got, got_rows, grid_cols)
        if step + 1 < len(GATHER_BITS):
            held = jnp.concatenate([held, got], axis=0)
            held, settled = lax.optimization_barrier((held, settled))
    running_max, acc = state
    denominator = acc[:, 0]
    flow_row = (acc[:, 1] / denominator / total_rows).reshape(
        band_rows, image_width
    ) - pixel_row.astype(jnp.float32) / total_rows
    flow_col = (
        (8.0 * (acc[:, 2] / denominator) + 3.5) / image_width
    ).reshape(band_rows, image_width) - pixel_col.astype(jnp.float32) / image_width
    places = lax.dynamic_index_in_dim(jnp.asarray(place_table), band, 0, keepdims=False)
    t_row = target_row.reshape(pixel_count)
    t_col = target_col.reshape(pixel_count)
    valid = t_row >= 0
    place = places.astype(jnp.int32)[jnp.where(valid, t_row, 0)] * grid_cols + jnp.where(
        valid, t_col, 0
    )
    half = held.shape[0]
    picked = jnp.where(
        (place < half)[:, None],
        jnp.take(held, jnp.minimum(place, half - 1), axis=0),
        jnp.take(got, jnp.maximum(place - half, 0), axis=0),
    )
    found = jnp.sum(features.astype(jnp.float32) * picked.astype(jnp.float32), axis=1)
    lookup = jnp.where(valid, found, 0.0)
    lookup = lookup.reshape(band_rows, image_width)
    motion = jax.nn.relu(
        flow_row[..., None] * w_motion[0]
        + flow_col[..., None] * w_motion[1]
        + lookup[..., None] * w_motion[2]
    ).astype(jnp.bfloat16)
    inputs = jnp.concatenate([context, motion], axis=-1)
    width_h = hidden_init.shape[-1]
    from_row = conv_valid(pad_columns(inputs), w_row[:, width_h:, :], 1)
    hidden = hidden_init.astype(jnp.float32)
    from_col = None
    for iteration in range(ITERS):
        hidden = row_pass(hidden, from_row, w_row)
        hidden, from_col = column_pass_each(
            hidden, from_col, w_col, inputs if iteration == 0 else None
        )
    return (hidden, jnp.stack([flow_row, flow_col]))


def solution(mesh):
    return jax.shard_map(
        per_device,
        mesh=mesh,
        in_specs=(
            P("band", "pair", None),
            P("band", "pair", None),
            P("band", "pair", None),
            P("band", "pair", None),
            P(None, "band", "pair"),
            P(),
            P(),
            P(),
        ),
        out_specs=(P("band", "pair", None), P(None, "band", "pair")),
        check_vma=False,
    )
```

```python
import math

import numpy as np

import jax
import jax.numpy as jnp
from jax import lax
from jax.experimental import pallas as pl
from jax.sharding import PartitionSpec as P

ITERS = 2


def passed_along(array, axis, by):
    count = lax.axis_size(axis)
    pairs = [(i, i + by) for i in range(count) if 0 <= i + by < count]
    return lax.ppermute(array, axis, pairs)


def pool_strips(frame2):
    band_rows, image_width, channels = frame2.shape
    blocks = frame2.astype(jnp.float32).reshape(band_rows, image_width // 8, 8, channels)
    return (jnp.sum(blocks, axis=2) / 2.0).astype(jnp.bfloat16)


def scaled_strips(frame2, scale):
    band_rows, image_width, channels = frame2.shape
    blocks = frame2.astype(jnp.float32).reshape(band_rows, image_width // 8, 8, channels)
    return (jnp.sum(blocks, axis=2) / (2.0 * scale)).astype(jnp.bfloat16)


def lookup_targets(offsets, row_first, total_rows, image_width):
    band_rows = offsets.shape[1]
    pixel_row = (
        row_first
        + jnp.arange(band_rows, dtype=jnp.int32)[:, None]
        + jnp.zeros((1, image_width), jnp.int32)
    )
    pixel_col = jnp.arange(image_width, dtype=jnp.int32)[None, :]
    target_row = pixel_row + offsets[0]
    target_col = pixel_col // 8 + offsets[1]
    inside = (
        (target_row >= 0)
        & (target_row < total_rows)
        & (target_col >= 0)
        & (target_col < image_width // 8)
    )
    target_row = jnp.where(inside, target_row, -1)
    target_col = jnp.where(inside, target_col, -1)
    return (target_row, target_col, pixel_row, pixel_col)


def strip_step(
    state, feature_rows, strip_block, row_zero, total_rows, image_width, target_row, target_col
):
    block_rows, grid_cols, channels = strip_block.shape
    scores = jnp.dot(
        feature_rows,
        strip_block.reshape(block_rows * grid_cols, channels).T,
        preferred_element_type=jnp.float32,
    ) / math.sqrt(channels)
    running_max, denominator, acc_row, acc_col, lookup = state
    new_max = jnp.maximum(running_max, jnp.max(scores, axis=1))
    shrink = jnp.exp(running_max - new_max)
    exponent = jnp.exp(scores - new_max[:, None]).reshape(-1, block_rows, grid_cols)
    strip_row = row_zero + jnp.arange(block_rows, dtype=jnp.int32)
    column_ids = jnp.arange(grid_cols, dtype=jnp.int32)
    row_centre = strip_row.astype(jnp.float32) / total_rows
    col_centre = ((8 * column_ids).astype(jnp.float32) + 3.5) / image_width
    row_weight = jnp.sum(exponent, axis=2)
    col_weight = jnp.sum(exponent, axis=1)
    scores_grid = scores.reshape(-1, block_rows, grid_cols)
    hit = (strip_row[None, :, None] == target_row[:, None, None]) & (
        column_ids[None, None, :] == target_col[:, None, None]
    )
    found = jnp.sum(jnp.where(hit, scores_grid, 0.0), axis=(1, 2))
    return (
        new_max,
        denominator * shrink + jnp.sum(row_weight, axis=1),
        acc_row * shrink + jnp.sum(row_weight * row_centre[None, :], axis=1),
        acc_col * shrink + jnp.sum(col_weight * col_centre[None, :], axis=1),
        lookup + found,
    )


def conv_valid(source, weight, conv_axis):
    out_count = source.shape[conv_axis] - 4
    summed = None
    for kernel_tap in range(5):
        tap_slice = lax.slice_in_dim(source, kernel_tap, kernel_tap + out_count, axis=conv_axis)
        tap_term = jnp.dot(
            tap_slice.reshape(-1, tap_slice.shape[-1]),
            weight[kernel_tap],
            preferred_element_type=jnp.float32,
        )
        summed = tap_term if summed is None else summed + tap_term
    out_shape = tuple(tap_slice.shape[:-1]) + (weight.shape[-1],)
    return summed.reshape(out_shape)


def pad_columns(source):
    return jnp.pad(source, ((0, 0), (2, 2), (0, 0)))


def rows_around(source, depth, mover):
    above = [
        mover(source, offset)
        for offset in list(range(depth, 0, -1)) + list(range(-1, -depth - 1, -1))
    ]
    return jnp.concatenate(above[:depth] + [source] + above[depth:], axis=0)


def row_pass(hidden, from_inputs, weight):
    width_h = hidden.shape[-1]
    hidden_half = lax.optimization_barrier(hidden.astype(jnp.bfloat16))
    gate_pair = jax.nn.sigmoid(
        conv_valid(pad_columns(hidden_half), weight[:, :width_h, : 2 * width_h], 1)
        + from_inputs[..., : 2 * width_h]
    )
    update_gate = gate_pair[..., :width_h]
    reset_gate = gate_pair[..., width_h:]
    gated = (reset_gate * hidden_half.astype(jnp.float32)).astype(jnp.bfloat16)
    candidate = jnp.tanh(
        conv_valid(pad_columns(gated), weight[:, :width_h, 2 * width_h :], 1)
        + from_inputs[..., 2 * width_h :]
    )
    return (1.0 - update_gate) * hidden + update_gate * candidate


def column_pass_each(hidden, from_inputs, weight, inputs=None):
    width_h = hidden.shape[-1]
    hidden_half = lax.optimization_barrier(hidden.astype(jnp.bfloat16))
    mover = lambda source, offset: passed_along(source, "band", offset)
    if inputs is None:
        hidden_ext = rows_around(hidden_half, 2, mover)
    else:
        joined_ext = rows_around(jnp.concatenate([hidden_half, inputs], axis=-1), 2, mover)
        hidden_ext = joined_ext[..., :width_h]
        from_inputs = conv_valid(joined_ext[..., width_h:], weight[:, width_h:, :], 0)
    gate_pair = jax.nn.sigmoid(
        conv_valid(hidden_ext, weight[:, :width_h, : 2 * width_h], 0)
        + from_inputs[..., : 2 * width_h]
    )
    update_gate = gate_pair[..., :width_h]
    reset_gate = gate_pair[..., width_h:]
    gated = (reset_gate * hidden_half.astype(jnp.float32)).astype(jnp.bfloat16)
    gated_ext = rows_around(gated, 2, mover)
    candidate = jnp.tanh(
        conv_valid(gated_ext, weight[:, :width_h, 2 * width_h :], 0)
        + from_inputs[..., 2 * width_h :]
    )
    return ((1.0 - update_gate) * hidden + update_gate * candidate, from_inputs)


GATHER_BITS = (4, 3, 2, 7, 6, 5, 1, 0)


def match_kernel(f1_ref, s_ref, w_ref, m_in, a_in, m_out, a_out):
    @pl.when(pl.program_id(0) == 0)
    def _():
        m_out[...] = m_in[...]
        a_out[...] = a_in[...]

    scores = lax.dot_general(
        f1_ref[...], s_ref[...], (((1,), (1,)), ((), ())), preferred_element_type=jnp.float32
    )
    m_old = m_out[:, 0:1]
    m_new = jnp.maximum(m_old, jnp.max(scores, axis=1, keepdims=True))
    p = jnp.exp(scores - m_new)
    shrink = jnp.exp(m_old - m_new)
    p_hi = p.astype(jnp.bfloat16)
    p_lo = (p - p_hi.astype(jnp.float32)).astype(jnp.bfloat16)
    w = w_ref[...]
    part = jnp.dot(p_hi, w, preferred_element_type=jnp.float32) + jnp.dot(
        p_lo, w, preferred_element_type=jnp.float32
    )
    a_out[...] = a_out[...] * shrink + part
    m_out[...] = jnp.broadcast_to(m_new, m_out.shape)


def match_block(state, features, block, block_rows, grid_cols):
    count, channels = block.shape
    pixels = features.shape[0]
    tile = min(count, 3072)
    strip_row = jnp.repeat(block_rows, grid_cols).astype(jnp.float32)
    strip_col = (jnp.arange(count, dtype=jnp.int32) % grid_cols).astype(jnp.float32)
    weights = jnp.concatenate(
        [
            jnp.ones((count, 1), jnp.float32),
            strip_row[:, None],
            strip_col[:, None],
            jnp.zeros((count, 125), jnp.float32),
        ],
        axis=1,
    ).astype(jnp.bfloat16)
    running_max, acc = state
    return pl.pallas_call(
        match_kernel,
        grid=(count // tile,),
        in_specs=[
            pl.BlockSpec((pixels, channels), lambda i: (0, 0)),
            pl.BlockSpec((tile, channels), lambda i: (i, 0)),
            pl.BlockSpec((tile, 128), lambda i: (i, 0)),
            pl.BlockSpec((pixels, 128), lambda i: (0, 0)),
            pl.BlockSpec((pixels, 128), lambda i: (0, 0)),
        ],
        out_specs=[
            pl.BlockSpec((pixels, 128), lambda i: (0, 0)),
            pl.BlockSpec((pixels, 128), lambda i: (0, 0)),
        ],
        out_shape=[
            jax.ShapeDtypeStruct((pixels, 128), jnp.float32),
            jax.ShapeDtypeStruct((pixels, 128), jnp.float32),
        ],
        cost_estimate=pl.CostEstimate(
            flops=2 * pixels * count * (channels + 256),
            transcendentals=pixels * count,
            bytes_accessed=2 * count * (channels + 128) + 2 * pixels * channels + 16 * pixels * 128,
        ),
    )(features, block, weights, running_max, acc)


def gather_partner(device, step, where):
    bit = GATHER_BITS[step]
    if bit != 1:
        return device ^ (1 << bit)
    z = (device >> 1) & 15
    shifted = ((((z + 15) % 16) ^ 1) + 1) % 16
    partner_z = where((device & 1) == 0, z ^ 1, shifted)
    return device - (z << 1) + (partner_z << 1)


def gather_tables(bands):
    devices = np.arange(bands, dtype=np.int64)
    rows = devices[:, None]
    for step in range(len(GATHER_BITS)):
        rows = np.concatenate([rows, rows[gather_partner(devices, step, np.where)]], axis=1)
    places = np.zeros_like(rows)
    for device in range(bands):
        places[device, rows[device]] = np.arange(rows.shape[1])
    return rows.astype(np.int16), places.astype(np.int16)


def per_device(frame1, frame2, context, hidden_init, offsets, w_motion, w_row, w_col):
    band_rows, image_width, channels = frame1.shape
    bands = lax.axis_size("band")
    total_rows = band_rows * bands
    band = lax.axis_index("band")
    row_first = band * band_rows
    strips = scaled_strips(frame2, math.sqrt(channels))
    grid_cols = strips.shape[1]
    target_row, target_col, pixel_row, pixel_col = lookup_targets(
        offsets, row_first, total_rows, image_width
    )
    pixel_count = band_rows * image_width
    features = frame1.reshape(pixel_count, channels)
    row_table, place_table = gather_tables(bands)
    state = (
        jnp.full((pixel_count, 128), -jnp.inf, jnp.float32),
        jnp.zeros((pixel_count, 128), jnp.float32),
    )
    held = strips.reshape(band_rows * grid_cols, channels)
    merged = 5
    own_rows = lax.dynamic_index_in_dim(jnp.asarray(row_table), band, 0, keepdims=False)
    for step, bit in enumerate(GATHER_BITS):
        pairs = [(i, int(gather_partner(i, step, np.where))) for i in range(bands)]
        got = lax.ppermute(held, "band", pairs)
        if step < merged:
            held = jnp.concatenate([held, got], axis=0)
            if step == merged - 1:
                start_rows = own_rows[: 1 << merged].astype(jnp.int32)
                state = match_block(state, features, held, start_rows, grid_cols)
            continue
        partner = gather_partner(band, step, jnp.where)
        got_rows = lax.dynamic_index_in_dim(
            jnp.asarray(row_table[:, : 1 << step]), partner, 0, keepdims=False
        ).astype(jnp.int32)
        settled = state
        state = match_block(state, features, got, got_rows, grid_cols)
        if step + 1 < len(GATHER_BITS):
            held = jnp.concatenate([held, got], axis=0)
            held, settled = lax.optimization_barrier((held, settled))
    running_max, acc = state
    denominator = acc[:, 0]
    flow_row = (acc[:, 1] / denominator / total_rows).reshape(
        band_rows, image_width
    ) - pixel_row.astype(jnp.float32) / total_rows
    flow_col = (
        (8.0 * (acc[:, 2] / denominator) + 3.5) / image_width
    ).reshape(band_rows, image_width) - pixel_col.astype(jnp.float32) / image_width
    places = lax.dynamic_index_in_dim(jnp.asarray(place_table), band, 0, keepdims=False)
    t_row = target_row.reshape(pixel_count)
    t_col = target_col.reshape(pixel_count)
    valid = t_row >= 0
    place = places.astype(jnp.int32)[jnp.where(valid, t_row, 0)] * grid_cols + jnp.where(
        valid, t_col, 0
    )
    half = held.shape[0]
    picked = jnp.where(
        (place < half)[:, None],
        jnp.take(held, jnp.minimum(place, half - 1), axis=0),
        jnp.take(got, jnp.maximum(place - half, 0), axis=0),
    )
    found = jnp.sum(features.astype(jnp.float32) * picked.astype(jnp.float32), axis=1)
    lookup = jnp.where(valid, found, 0.0)
    lookup = lookup.reshape(band_rows, image_width)
    motion = jax.nn.relu(
        flow_row[..., None] * w_motion[0]
        + flow_col[..., None] * w_motion[1]
        + lookup[..., None] * w_motion[2]
    ).astype(jnp.bfloat16)
    inputs = jnp.concatenate([context, motion], axis=-1)
    width_h = hidden_init.shape[-1]
    from_row = conv_valid(pad_columns(inputs), w_row[:, width_h:, :], 1)
    hidden = hidden_init.astype(jnp.float32)
    from_col = None
    for iteration in range(ITERS):
        hidden = row_pass(hidden, from_row, w_row)
        hidden, from_col = column_pass_each(
            hidden, from_col, w_col, inputs if iteration == 0 else None
        )
    return (hidden, jnp.stack([flow_row, flow_col]))


def solution(mesh):
    return jax.shard_map(
        per_device,
        mesh=mesh,
        in_specs=(
            P("band", "pair", None),
            P("band", "pair", None),
            P("band", "pair", None),
            P("band", "pair", None),
            P(None, "band", "pair"),
            P(),
            P(),
            P(),
        ),
        out_specs=(P("band", "pair", None), P(None, "band", "pair")),
        check_vma=False,
    )
```

```python
import math

import numpy as np

import jax
import jax.numpy as jnp
from jax import lax
from jax.experimental import pallas as pl
from jax.sharding import PartitionSpec as P

ITERS = 2


def passed_along(array, axis, by):
    count = lax.axis_size(axis)
    pairs = [(i, i + by) for i in range(count) if 0 <= i + by < count]
    return lax.ppermute(array, axis, pairs)


def pool_strips(frame2):
    band_rows, image_width, channels = frame2.shape
    blocks = frame2.astype(jnp.float32).reshape(band_rows, image_width // 8, 8, channels)
    return (jnp.sum(blocks, axis=2) / 2.0).astype(jnp.bfloat16)


def scaled_strips(frame2, scale):
    band_rows, image_width, channels = frame2.shape
    blocks = frame2.astype(jnp.float32).reshape(band_rows, image_width // 8, 8, channels)
    return (jnp.sum(blocks, axis=2) / (2.0 * scale)).astype(jnp.bfloat16)


def lookup_targets(offsets, row_first, total_rows, image_width):
    band_rows = offsets.shape[1]
    pixel_row = (
        row_first
        + jnp.arange(band_rows, dtype=jnp.int32)[:, None]
        + jnp.zeros((1, image_width), jnp.int32)
    )
    pixel_col = jnp.arange(image_width, dtype=jnp.int32)[None, :]
    target_row = pixel_row + offsets[0]
    target_col = pixel_col // 8 + offsets[1]
    inside = (
        (target_row >= 0)
        & (target_row < total_rows)
        & (target_col >= 0)
        & (target_col < image_width // 8)
    )
    target_row = jnp.where(inside, target_row, -1)
    target_col = jnp.where(inside, target_col, -1)
    return (target_row, target_col, pixel_row, pixel_col)


def strip_step(
    state, feature_rows, strip_block, row_zero, total_rows, image_width, target_row, target_col
):
    block_rows, grid_cols, channels = strip_block.shape
    scores = jnp.dot(
        feature_rows,
        strip_block.reshape(block_rows * grid_cols, channels).T,
        preferred_element_type=jnp.float32,
    ) / math.sqrt(channels)
    running_max, denominator, acc_row, acc_col, lookup = state
    new_max = jnp.maximum(running_max, jnp.max(scores, axis=1))
    shrink = jnp.exp(running_max - new_max)
    exponent = jnp.exp(scores - new_max[:, None]).reshape(-1, block_rows, grid_cols)
    strip_row = row_zero + jnp.arange(block_rows, dtype=jnp.int32)
    column_ids = jnp.arange(grid_cols, dtype=jnp.int32)
    row_centre = strip_row.astype(jnp.float32) / total_rows
    col_centre = ((8 * column_ids).astype(jnp.float32) + 3.5) / image_width
    row_weight = jnp.sum(exponent, axis=2)
    col_weight = jnp.sum(exponent, axis=1)
    scores_grid = scores.reshape(-1, block_rows, grid_cols)
    hit = (strip_row[None, :, None] == target_row[:, None, None]) & (
        column_ids[None, None, :] == target_col[:, None, None]
    )
    found = jnp.sum(jnp.where(hit, scores_grid, 0.0), axis=(1, 2))
    return (
        new_max,
        denominator * shrink + jnp.sum(row_weight, axis=1),
        acc_row * shrink + jnp.sum(row_weight * row_centre[None, :], axis=1),
        acc_col * shrink + jnp.sum(col_weight * col_centre[None, :], axis=1),
        lookup + found,
    )


def conv_valid(source, weight, conv_axis):
    out_count = source.shape[conv_axis] - 4
    summed = None
    for kernel_tap in range(5):
        tap_slice = lax.slice_in_dim(source, kernel_tap, kernel_tap + out_count, axis=conv_axis)
        tap_term = jnp.dot(
            tap_slice.reshape(-1, tap_slice.shape[-1]),
            weight[kernel_tap],
            preferred_element_type=jnp.float32,
        )
        summed = tap_term if summed is None else summed + tap_term
    out_shape = tuple(tap_slice.shape[:-1]) + (weight.shape[-1],)
    return summed.reshape(out_shape)


def pad_columns(source):
    return jnp.pad(source, ((0, 0), (2, 2), (0, 0)))


def rows_around(source, depth, mover):
    above = [
        mover(source, offset)
        for offset in list(range(depth, 0, -1)) + list(range(-1, -depth - 1, -1))
    ]
    return jnp.concatenate(above[:depth] + [source] + above[depth:], axis=0)


def row_pass(hidden, from_inputs, weight):
    width_h = hidden.shape[-1]
    hidden_half = lax.optimization_barrier(hidden.astype(jnp.bfloat16))
    gate_pair = jax.nn.sigmoid(
        conv_valid(pad_columns(hidden_half), weight[:, :width_h, : 2 * width_h], 1)
        + from_inputs[..., : 2 * width_h]
    )
    update_gate = gate_pair[..., :width_h]
    reset_gate = gate_pair[..., width_h:]
    gated = (reset_gate * hidden_half.astype(jnp.float32)).astype(jnp.bfloat16)
    candidate = jnp.tanh(
        conv_valid(pad_columns(gated), weight[:, :width_h, 2 * width_h :], 1)
        + from_inputs[..., 2 * width_h :]
    )
    return (1.0 - update_gate) * hidden + update_gate * candidate


def column_pass_each(hidden, from_inputs, weight, inputs=None):
    width_h = hidden.shape[-1]
    hidden_half = lax.optimization_barrier(hidden.astype(jnp.bfloat16))
    mover = lambda source, offset: passed_along(source, "band", offset)
    if inputs is None:
        hidden_ext = rows_around(hidden_half, 2, mover)
    else:
        joined_ext = rows_around(jnp.concatenate([hidden_half, inputs], axis=-1), 2, mover)
        hidden_ext = joined_ext[..., :width_h]
        from_inputs = conv_valid(joined_ext[..., width_h:], weight[:, width_h:, :], 0)
    gate_pair = jax.nn.sigmoid(
        conv_valid(hidden_ext, weight[:, :width_h, : 2 * width_h], 0)
        + from_inputs[..., : 2 * width_h]
    )
    update_gate = gate_pair[..., :width_h]
    reset_gate = gate_pair[..., width_h:]
    gated = (reset_gate * hidden_half.astype(jnp.float32)).astype(jnp.bfloat16)
    gated_ext = rows_around(gated, 2, mover)
    candidate = jnp.tanh(
        conv_valid(gated_ext, weight[:, :width_h, 2 * width_h :], 0)
        + from_inputs[..., 2 * width_h :]
    )
    return ((1.0 - update_gate) * hidden + update_gate * candidate, from_inputs)


GATHER_BITS = (4, 3, 2, 7, 6, 5, 1, 0)


def match_kernel(f1_ref, s_ref, w_ref, m_in, a_in, m_out, a_out):
    @pl.when(pl.program_id(0) == 0)
    def _():
        m_out[...] = m_in[...]
        a_out[...] = a_in[...]

    scores = lax.dot_general(
        f1_ref[...], s_ref[...], (((1,), (1,)), ((), ())), preferred_element_type=jnp.float32
    )
    m_old = m_out[:, 0:1]
    m_new = jnp.maximum(m_old, jnp.max(scores, axis=1, keepdims=True))
    p = jnp.exp(scores - m_new)
    shrink = jnp.exp(m_old - m_new)
    p_hi = p.astype(jnp.bfloat16)
    p_lo = (p - p_hi.astype(jnp.float32)).astype(jnp.bfloat16)
    w = w_ref[...]
    part = jnp.dot(p_hi, w, preferred_element_type=jnp.float32) + jnp.dot(
        p_lo, w, preferred_element_type=jnp.float32
    )
    a_out[...] = a_out[...] * shrink + part
    m_out[...] = jnp.broadcast_to(m_new, m_out.shape)


def match_block(state, features, block, block_rows, grid_cols):
    count, channels = block.shape
    pixels = features.shape[0]
    tile = min(count, 3072)
    strip_row = jnp.repeat(block_rows, grid_cols).astype(jnp.float32)
    strip_col = (jnp.arange(count, dtype=jnp.int32) % grid_cols).astype(jnp.float32)
    weights = jnp.concatenate(
        [
            jnp.ones((count, 1), jnp.float32),
            strip_row[:, None],
            strip_col[:, None],
            jnp.zeros((count, 125), jnp.float32),
        ],
        axis=1,
    ).astype(jnp.bfloat16)
    running_max, acc = state
    return pl.pallas_call(
        match_kernel,
        grid=(count // tile,),
        in_specs=[
            pl.BlockSpec((pixels, channels), lambda i: (0, 0)),
            pl.BlockSpec((tile, channels), lambda i: (i, 0)),
            pl.BlockSpec((tile, 128), lambda i: (i, 0)),
            pl.BlockSpec((pixels, 128), lambda i: (0, 0)),
            pl.BlockSpec((pixels, 128), lambda i: (0, 0)),
        ],
        out_specs=[
            pl.BlockSpec((pixels, 128), lambda i: (0, 0)),
            pl.BlockSpec((pixels, 128), lambda i: (0, 0)),
        ],
        out_shape=[
            jax.ShapeDtypeStruct((pixels, 128), jnp.float32),
            jax.ShapeDtypeStruct((pixels, 128), jnp.float32),
        ],
        cost_estimate=pl.CostEstimate(
            flops=2 * pixels * count * (channels + 256),
            transcendentals=pixels * count,
            bytes_accessed=2 * count * (channels + 128) + 2 * pixels * channels + 16 * pixels * 128,
        ),
    )(features, block, weights, running_max, acc)


def gather_partner(device, step, where):
    bit = GATHER_BITS[step]
    if bit != 1:
        return device ^ (1 << bit)
    z = (device >> 1) & 15
    shifted = ((((z + 15) % 16) ^ 1) + 1) % 16
    partner_z = where((device & 1) == 0, z ^ 1, shifted)
    return device - (z << 1) + (partner_z << 1)


def gather_tables(bands):
    devices = np.arange(bands, dtype=np.int64)
    rows = devices[:, None]
    for step in range(len(GATHER_BITS)):
        rows = np.concatenate([rows, rows[gather_partner(devices, step, np.where)]], axis=1)
    places = np.zeros_like(rows)
    for device in range(bands):
        places[device, rows[device]] = np.arange(rows.shape[1])
    return rows.astype(np.int16), places.astype(np.int16)


def per_device(frame1, frame2, context, hidden_init, offsets, w_motion, w_row, w_col):
    band_rows, image_width, channels = frame1.shape
    bands = lax.axis_size("band")
    total_rows = band_rows * bands
    band = lax.axis_index("band")
    row_first = band * band_rows
    strips = scaled_strips(frame2, math.sqrt(channels))
    grid_cols = strips.shape[1]
    target_row, target_col, pixel_row, pixel_col = lookup_targets(
        offsets, row_first, total_rows, image_width
    )
    pixel_count = band_rows * image_width
    features = frame1.reshape(pixel_count, channels)
    row_table, place_table = gather_tables(bands)
    state = (
        jnp.full((pixel_count, 128), -jnp.inf, jnp.float32),
        jnp.zeros((pixel_count, 128), jnp.float32),
    )
    held = strips.reshape(band_rows * grid_cols, channels)
    merged = 6
    own_rows = lax.dynamic_index_in_dim(jnp.asarray(row_table), band, 0, keepdims=False)
    for step, bit in enumerate(GATHER_BITS):
        pairs = [(i, int(gather_partner(i, step, np.where))) for i in range(bands)]
        got = lax.ppermute(held, "band", pairs)
        if step < merged:
            held = jnp.concatenate([held, got], axis=0)
            if step == merged - 1:
                start_rows = own_rows[: 1 << merged].astype(jnp.int32)
                state = match_block(state, features, held, start_rows, grid_cols)
            continue
        partner = gather_partner(band, step, jnp.where)
        got_rows = lax.dynamic_index_in_dim(
            jnp.asarray(row_table[:, : 1 << step]), partner, 0, keepdims=False
        ).astype(jnp.int32)
        settled = state
        state = match_block(state, features, got, got_rows, grid_cols)
        if step + 1 < len(GATHER_BITS):
            held = jnp.concatenate([held, got], axis=0)
            held, settled = lax.optimization_barrier((held, settled))
    running_max, acc = state
    denominator = acc[:, 0]
    flow_row = (acc[:, 1] / denominator / total_rows).reshape(
        band_rows, image_width
    ) - pixel_row.astype(jnp.float32) / total_rows
    flow_col = (
        (8.0 * (acc[:, 2] / denominator) + 3.5) / image_width
    ).reshape(band_rows, image_width) - pixel_col.astype(jnp.float32) / image_width
    places = lax.dynamic_index_in_dim(jnp.asarray(place_table), band, 0, keepdims=False)
    t_row = target_row.reshape(pixel_count)
    t_col = target_col.reshape(pixel_count)
    valid = t_row >= 0
    place = places.astype(jnp.int32)[jnp.where(valid, t_row, 0)] * grid_cols + jnp.where(
        valid, t_col, 0
    )
    half = held.shape[0]
    picked = jnp.where(
        (place < half)[:, None],
        jnp.take(held, jnp.minimum(place, half - 1), axis=0),
        jnp.take(got, jnp.maximum(place - half, 0), axis=0),
    )
    found = jnp.sum(features.astype(jnp.float32) * picked.astype(jnp.float32), axis=1)
    lookup = jnp.where(valid, found, 0.0)
    lookup = lookup.reshape(band_rows, image_width)
    motion = jax.nn.relu(
        flow_row[..., None] * w_motion[0]
        + flow_col[..., None] * w_motion[1]
        + lookup[..., None] * w_motion[2]
    ).astype(jnp.bfloat16)
    inputs = jnp.concatenate([context, motion], axis=-1)
    width_h = hidden_init.shape[-1]
    from_row = conv_valid(pad_columns(inputs), w_row[:, width_h:, :], 1)
    hidden = hidden_init.astype(jnp.float32)
    from_col = None
    for iteration in range(ITERS):
        hidden = row_pass(hidden, from_row, w_row)
        hidden, from_col = column_pass_each(
            hidden, from_col, w_col, inputs if iteration == 0 else None
        )
    return (hidden, jnp.stack([flow_row, flow_col]))


def solution(mesh):
    return jax.shard_map(
        per_device,
        mesh=mesh,
        in_specs=(
            P("band", "pair", None),
            P("band", "pair", None),
            P("band", "pair", None),
            P("band", "pair", None),
            P(None, "band", "pair"),
            P(),
            P(),
            P(),
        ),
        out_specs=(P("band", "pair", None), P(None, "band", "pair")),
        check_vma=False,
    )
```

```python
import math

import numpy as np

import jax
import jax.numpy as jnp
from jax import lax
from jax.experimental import pallas as pl
from jax.sharding import PartitionSpec as P

ITERS = 2


def passed_along(array, axis, by):
    count = lax.axis_size(axis)
    pairs = [(i, i + by) for i in range(count) if 0 <= i + by < count]
    return lax.ppermute(array, axis, pairs)


def pool_strips(frame2):
    band_rows, image_width, channels = frame2.shape
    blocks = frame2.astype(jnp.float32).reshape(band_rows, image_width // 8, 8, channels)
    return (jnp.sum(blocks, axis=2) / 2.0).astype(jnp.bfloat16)


def scaled_strips(frame2, scale):
    band_rows, image_width, channels = frame2.shape
    blocks = frame2.astype(jnp.float32).reshape(band_rows, image_width // 8, 8, channels)
    return (jnp.sum(blocks, axis=2) / (2.0 * scale)).astype(jnp.bfloat16)


def lookup_targets(offsets, row_first, total_rows, image_width):
    band_rows = offsets.shape[1]
    pixel_row = (
        row_first
        + jnp.arange(band_rows, dtype=jnp.int32)[:, None]
        + jnp.zeros((1, image_width), jnp.int32)
    )
    pixel_col = jnp.arange(image_width, dtype=jnp.int32)[None, :]
    target_row = pixel_row + offsets[0]
    target_col = pixel_col // 8 + offsets[1]
    inside = (
        (target_row >= 0)
        & (target_row < total_rows)
        & (target_col >= 0)
        & (target_col < image_width // 8)
    )
    target_row = jnp.where(inside, target_row, -1)
    target_col = jnp.where(inside, target_col, -1)
    return (target_row, target_col, pixel_row, pixel_col)


def strip_step(
    state, feature_rows, strip_block, row_zero, total_rows, image_width, target_row, target_col
):
    block_rows, grid_cols, channels = strip_block.shape
    scores = jnp.dot(
        feature_rows,
        strip_block.reshape(block_rows * grid_cols, channels).T,
        preferred_element_type=jnp.float32,
    ) / math.sqrt(channels)
    running_max, denominator, acc_row, acc_col, lookup = state
    new_max = jnp.maximum(running_max, jnp.max(scores, axis=1))
    shrink = jnp.exp(running_max - new_max)
    exponent = jnp.exp(scores - new_max[:, None]).reshape(-1, block_rows, grid_cols)
    strip_row = row_zero + jnp.arange(block_rows, dtype=jnp.int32)
    column_ids = jnp.arange(grid_cols, dtype=jnp.int32)
    row_centre = strip_row.astype(jnp.float32) / total_rows
    col_centre = ((8 * column_ids).astype(jnp.float32) + 3.5) / image_width
    row_weight = jnp.sum(exponent, axis=2)
    col_weight = jnp.sum(exponent, axis=1)
    scores_grid = scores.reshape(-1, block_rows, grid_cols)
    hit = (strip_row[None, :, None] == target_row[:, None, None]) & (
        column_ids[None, None, :] == target_col[:, None, None]
    )
    found = jnp.sum(jnp.where(hit, scores_grid, 0.0), axis=(1, 2))
    return (
        new_max,
        denominator * shrink + jnp.sum(row_weight, axis=1),
        acc_row * shrink + jnp.sum(row_weight * row_centre[None, :], axis=1),
        acc_col * shrink + jnp.sum(col_weight * col_centre[None, :], axis=1),
        lookup + found,
    )


def conv_valid(source, weight, conv_axis):
    out_count = source.shape[conv_axis] - 4
    summed = None
    for kernel_tap in range(5):
        tap_slice = lax.slice_in_dim(source, kernel_tap, kernel_tap + out_count, axis=conv_axis)
        tap_term = jnp.dot(
            tap_slice.reshape(-1, tap_slice.shape[-1]),
            weight[kernel_tap],
            preferred_element_type=jnp.float32,
        )
        summed = tap_term if summed is None else summed + tap_term
    out_shape = tuple(tap_slice.shape[:-1]) + (weight.shape[-1],)
    return summed.reshape(out_shape)


def pad_columns(source):
    return jnp.pad(source, ((0, 0), (2, 2), (0, 0)))


def rows_around(source, depth, mover):
    above = [
        mover(source, offset)
        for offset in list(range(depth, 0, -1)) + list(range(-1, -depth - 1, -1))
    ]
    return jnp.concatenate(above[:depth] + [source] + above[depth:], axis=0)


def row_pass(hidden, from_inputs, weight):
    width_h = hidden.shape[-1]
    hidden_half = lax.optimization_barrier(hidden.astype(jnp.bfloat16))
    gate_pair = jax.nn.sigmoid(
        conv_valid(pad_columns(hidden_half), weight[:, :width_h, : 2 * width_h], 1)
        + from_inputs[..., : 2 * width_h]
    )
    update_gate = gate_pair[..., :width_h]
    reset_gate = gate_pair[..., width_h:]
    gated = (reset_gate * hidden_half.astype(jnp.float32)).astype(jnp.bfloat16)
    candidate = jnp.tanh(
        conv_valid(pad_columns(gated), weight[:, :width_h, 2 * width_h :], 1)
        + from_inputs[..., 2 * width_h :]
    )
    return (1.0 - update_gate) * hidden + update_gate * candidate


def column_pass_each(hidden, from_inputs, weight, inputs=None):
    width_h = hidden.shape[-1]
    hidden_half = lax.optimization_barrier(hidden.astype(jnp.bfloat16))
    mover = lambda source, offset: passed_along(source, "band", offset)
    if inputs is None:
        hidden_ext = rows_around(hidden_half, 2, mover)
    else:
        joined_ext = rows_around(jnp.concatenate([hidden_half, inputs], axis=-1), 2, mover)
        hidden_ext = joined_ext[..., :width_h]
        from_inputs = conv_valid(joined_ext[..., width_h:], weight[:, width_h:, :], 0)
    gate_pair = jax.nn.sigmoid(
        conv_valid(hidden_ext, weight[:, :width_h, : 2 * width_h], 0)
        + from_inputs[..., : 2 * width_h]
    )
    update_gate = gate_pair[..., :width_h]
    reset_gate = gate_pair[..., width_h:]
    gated = (reset_gate * hidden_half.astype(jnp.float32)).astype(jnp.bfloat16)
    gated_ext = rows_around(gated, 2, mover)
    candidate = jnp.tanh(
        conv_valid(gated_ext, weight[:, :width_h, 2 * width_h :], 0)
        + from_inputs[..., 2 * width_h :]
    )
    return ((1.0 - update_gate) * hidden + update_gate * candidate, from_inputs)


GATHER_BITS = (4, 3, 2, 7, 6, 5, 1, 0)


def match_kernel(f1_ref, s_ref, w_ref, m_in, a_in, m_out, a_out):
    @pl.when(pl.program_id(0) == 0)
    def _():
        m_out[...] = m_in[...]
        a_out[...] = a_in[...]

    scores = lax.dot_general(
        f1_ref[...], s_ref[...], (((1,), (1,)), ((), ())), preferred_element_type=jnp.float32
    )
    m_old = m_out[:, 0:1]
    m_new = jnp.maximum(m_old, jnp.max(scores, axis=1, keepdims=True))
    p = jnp.exp(scores - m_new)
    shrink = jnp.exp(m_old - m_new)
    p_hi = p.astype(jnp.bfloat16)
    p_lo = (p - p_hi.astype(jnp.float32)).astype(jnp.bfloat16)
    w = w_ref[...]
    part = jnp.dot(p_hi, w, preferred_element_type=jnp.float32) + jnp.dot(
        p_lo, w, preferred_element_type=jnp.float32
    )
    a_out[...] = a_out[...] * shrink + part
    m_out[...] = jnp.broadcast_to(m_new, m_out.shape)


def match_block(state, features, block, block_rows, grid_cols):
    count, channels = block.shape
    pixels = features.shape[0]
    tile = min(count, 3072)
    strip_row = jnp.repeat(block_rows, grid_cols).astype(jnp.float32)
    strip_col = (jnp.arange(count, dtype=jnp.int32) % grid_cols).astype(jnp.float32)
    weights = jnp.concatenate(
        [
            jnp.ones((count, 1), jnp.float32),
            strip_row[:, None],
            strip_col[:, None],
            jnp.zeros((count, 125), jnp.float32),
        ],
        axis=1,
    ).astype(jnp.bfloat16)
    running_max, acc = state
    return pl.pallas_call(
        match_kernel,
        grid=(count // tile,),
        in_specs=[
            pl.BlockSpec((pixels, channels), lambda i: (0, 0)),
            pl.BlockSpec((tile, channels), lambda i: (i, 0)),
            pl.BlockSpec((tile, 128), lambda i: (i, 0)),
            pl.BlockSpec((pixels, 128), lambda i: (0, 0)),
            pl.BlockSpec((pixels, 128), lambda i: (0, 0)),
        ],
        out_specs=[
            pl.BlockSpec((pixels, 128), lambda i: (0, 0)),
            pl.BlockSpec((pixels, 128), lambda i: (0, 0)),
        ],
        out_shape=[
            jax.ShapeDtypeStruct((pixels, 128), jnp.float32),
            jax.ShapeDtypeStruct((pixels, 128), jnp.float32),
        ],
        cost_estimate=pl.CostEstimate(
            flops=2 * pixels * count * (channels + 256),
            transcendentals=pixels * count,
            bytes_accessed=2 * count * (channels + 128) + 2 * pixels * channels + 16 * pixels * 128,
        ),
    )(features, block, weights, running_max, acc)


def gather_partner(device, step, where):
    bit = GATHER_BITS[step]
    if bit != 1:
        return device ^ (1 << bit)
    z = (device >> 1) & 15
    shifted = ((((z + 15) % 16) ^ 1) + 1) % 16
    partner_z = where((device & 1) == 0, z ^ 1, shifted)
    return device - (z << 1) + (partner_z << 1)


def gather_tables(bands):
    devices = np.arange(bands, dtype=np.int64)
    rows = devices[:, None]
    for step in range(len(GATHER_BITS)):
        rows = np.concatenate([rows, rows[gather_partner(devices, step, np.where)]], axis=1)
    places = np.zeros_like(rows)
    for device in range(bands):
        places[device, rows[device]] = np.arange(rows.shape[1])
    return rows.astype(np.int16), places.astype(np.int16)


def per_device(frame1, frame2, context, hidden_init, offsets, w_motion, w_row, w_col):
    band_rows, image_width, channels = frame1.shape
    bands = lax.axis_size("band")
    total_rows = band_rows * bands
    band = lax.axis_index("band")
    row_first = band * band_rows
    strips = scaled_strips(frame2, math.sqrt(channels))
    grid_cols = strips.shape[1]
    target_row, target_col, pixel_row, pixel_col = lookup_targets(
        offsets, row_first, total_rows, image_width
    )
    pixel_count = band_rows * image_width
    features = frame1.reshape(pixel_count, channels)
    row_table, place_table = gather_tables(bands)
    state = (
        jnp.full((pixel_count, 128), -jnp.inf, jnp.float32),
        jnp.zeros((pixel_count, 128), jnp.float32),
    )
    held = strips.reshape(band_rows * grid_cols, channels)
    merged = 7
    own_rows = lax.dynamic_index_in_dim(jnp.asarray(row_table), band, 0, keepdims=False)
    for step, bit in enumerate(GATHER_BITS):
        pairs = [(i, int(gather_partner(i, step, np.where))) for i in range(bands)]
        got = lax.ppermute(held, "band", pairs)
        if step < merged:
            held = jnp.concatenate([held, got], axis=0)
            if step == merged - 1:
                start_rows = own_rows[: 1 << merged].astype(jnp.int32)
                state = match_block(state, features, held, start_rows, grid_cols)
            continue
        partner = gather_partner(band, step, jnp.where)
        got_rows = lax.dynamic_index_in_dim(
            jnp.asarray(row_table[:, : 1 << step]), partner, 0, keepdims=False
        ).astype(jnp.int32)
        settled = state
        state = match_block(state, features, got, got_rows, grid_cols)
        if step + 1 < len(GATHER_BITS):
            held = jnp.concatenate([held, got], axis=0)
            held, settled = lax.optimization_barrier((held, settled))
    running_max, acc = state
    denominator = acc[:, 0]
    flow_row = (acc[:, 1] / denominator / total_rows).reshape(
        band_rows, image_width
    ) - pixel_row.astype(jnp.float32) / total_rows
    flow_col = (
        (8.0 * (acc[:, 2] / denominator) + 3.5) / image_width
    ).reshape(band_rows, image_width) - pixel_col.astype(jnp.float32) / image_width
    places = lax.dynamic_index_in_dim(jnp.asarray(place_table), band, 0, keepdims=False)
    t_row = target_row.reshape(pixel_count)
    t_col = target_col.reshape(pixel_count)
    valid = t_row >= 0
    place = places.astype(jnp.int32)[jnp.where(valid, t_row, 0)] * grid_cols + jnp.where(
        valid, t_col, 0
    )
    half = held.shape[0]
    picked = jnp.where(
        (place < half)[:, None],
        jnp.take(held, jnp.minimum(place, half - 1), axis=0),
        jnp.take(got, jnp.maximum(place - half, 0), axis=0),
    )
    found = jnp.sum(features.astype(jnp.float32) * picked.astype(jnp.float32), axis=1)
    lookup = jnp.where(valid, found, 0.0)
    lookup = lookup.reshape(band_rows, image_width)
    motion = jax.nn.relu(
        flow_row[..., None] * w_motion[0]
        + flow_col[..., None] * w_motion[1]
        + lookup[..., None] * w_motion[2]
    ).astype(jnp.bfloat16)
    inputs = jnp.concatenate([context, motion], axis=-1)
    width_h = hidden_init.shape[-1]
    from_row = conv_valid(pad_columns(inputs), w_row[:, width_h:, :], 1)
    hidden = hidden_init.astype(jnp.float32)
    from_col = None
    for iteration in range(ITERS):
        hidden = row_pass(hidden, from_row, w_row)
        hidden, from_col = column_pass_each(
            hidden, from_col, w_col, inputs if iteration == 0 else None
        )
    return (hidden, jnp.stack([flow_row, flow_col]))


def solution(mesh):
    return jax.shard_map(
        per_device,
        mesh=mesh,
        in_specs=(
            P("band", "pair", None),
            P("band", "pair", None),
            P("band", "pair", None),
            P("band", "pair", None),
            P(None, "band", "pair"),
            P(),
            P(),
            P(),
        ),
        out_specs=(P("band", "pair", None), P(None, "band", "pair")),
        check_vma=False,
    )
```

```python
import math

import numpy as np

import jax
import jax.numpy as jnp
from jax import lax
from jax.experimental import pallas as pl
from jax.sharding import PartitionSpec as P

ITERS = 2


def passed_along(array, axis, by):
    count = lax.axis_size(axis)
    pairs = [(i, i + by) for i in range(count) if 0 <= i + by < count]
    return lax.ppermute(array, axis, pairs)


def pool_strips(frame2):
    band_rows, image_width, channels = frame2.shape
    blocks = frame2.astype(jnp.float32).reshape(band_rows, image_width // 8, 8, channels)
    return (jnp.sum(blocks, axis=2) / 2.0).astype(jnp.bfloat16)


def scaled_strips(frame2, scale):
    band_rows, image_width, channels = frame2.shape
    blocks = frame2.astype(jnp.float32).reshape(band_rows, image_width // 8, 8, channels)
    return (jnp.sum(blocks, axis=2) / (2.0 * scale)).astype(jnp.bfloat16)


def lookup_targets(offsets, row_first, total_rows, image_width):
    band_rows = offsets.shape[1]
    pixel_row = (
        row_first
        + jnp.arange(band_rows, dtype=jnp.int32)[:, None]
        + jnp.zeros((1, image_width), jnp.int32)
    )
    pixel_col = jnp.arange(image_width, dtype=jnp.int32)[None, :]
    target_row = pixel_row + offsets[0]
    target_col = pixel_col // 8 + offsets[1]
    inside = (
        (target_row >= 0)
        & (target_row < total_rows)
        & (target_col >= 0)
        & (target_col < image_width // 8)
    )
    target_row = jnp.where(inside, target_row, -1)
    target_col = jnp.where(inside, target_col, -1)
    return (target_row, target_col, pixel_row, pixel_col)


def strip_step(
    state, feature_rows, strip_block, row_zero, total_rows, image_width, target_row, target_col
):
    block_rows, grid_cols, channels = strip_block.shape
    scores = jnp.dot(
        feature_rows,
        strip_block.reshape(block_rows * grid_cols, channels).T,
        preferred_element_type=jnp.float32,
    ) / math.sqrt(channels)
    running_max, denominator, acc_row, acc_col, lookup = state
    new_max = jnp.maximum(running_max, jnp.max(scores, axis=1))
    shrink = jnp.exp(running_max - new_max)
    exponent = jnp.exp(scores - new_max[:, None]).reshape(-1, block_rows, grid_cols)
    strip_row = row_zero + jnp.arange(block_rows, dtype=jnp.int32)
    column_ids = jnp.arange(grid_cols, dtype=jnp.int32)
    row_centre = strip_row.astype(jnp.float32) / total_rows
    col_centre = ((8 * column_ids).astype(jnp.float32) + 3.5) / image_width
    row_weight = jnp.sum(exponent, axis=2)
    col_weight = jnp.sum(exponent, axis=1)
    scores_grid = scores.reshape(-1, block_rows, grid_cols)
    hit = (strip_row[None, :, None] == target_row[:, None, None]) & (
        column_ids[None, None, :] == target_col[:, None, None]
    )
    found = jnp.sum(jnp.where(hit, scores_grid, 0.0), axis=(1, 2))
    return (
        new_max,
        denominator * shrink + jnp.sum(row_weight, axis=1),
        acc_row * shrink + jnp.sum(row_weight * row_centre[None, :], axis=1),
        acc_col * shrink + jnp.sum(col_weight * col_centre[None, :], axis=1),
        lookup + found,
    )


def conv_valid(source, weight, conv_axis):
    out_count = source.shape[conv_axis] - 4
    summed = None
    for kernel_tap in range(5):
        tap_slice = lax.slice_in_dim(source, kernel_tap, kernel_tap + out_count, axis=conv_axis)
        tap_term = jnp.dot(
            tap_slice.reshape(-1, tap_slice.shape[-1]),
            weight[kernel_tap],
            preferred_element_type=jnp.float32,
        )
        summed = tap_term if summed is None else summed + tap_term
    out_shape = tuple(tap_slice.shape[:-1]) + (weight.shape[-1],)
    return summed.reshape(out_shape)


def pad_columns(source):
    return jnp.pad(source, ((0, 0), (2, 2), (0, 0)))


def rows_around(source, depth, mover):
    above = [
        mover(source, offset)
        for offset in list(range(depth, 0, -1)) + list(range(-1, -depth - 1, -1))
    ]
    return jnp.concatenate(above[:depth] + [source] + above[depth:], axis=0)


def row_pass(hidden, from_inputs, weight):
    width_h = hidden.shape[-1]
    hidden_half = lax.optimization_barrier(hidden.astype(jnp.bfloat16))
    gate_pair = jax.nn.sigmoid(
        conv_valid(pad_columns(hidden_half), weight[:, :width_h, : 2 * width_h], 1)
        + from_inputs[..., : 2 * width_h]
    )
    update_gate = gate_pair[..., :width_h]
    reset_gate = gate_pair[..., width_h:]
    gated = (reset_gate * hidden_half.astype(jnp.float32)).astype(jnp.bfloat16)
    candidate = jnp.tanh(
        conv_valid(pad_columns(gated), weight[:, :width_h, 2 * width_h :], 1)
        + from_inputs[..., 2 * width_h :]
    )
    return (1.0 - update_gate) * hidden + update_gate * candidate


def column_pass_each(hidden, from_inputs, weight, inputs=None):
    width_h = hidden.shape[-1]
    hidden_half = lax.optimization_barrier(hidden.astype(jnp.bfloat16))
    mover = lambda source, offset: passed_along(source, "band", offset)
    if inputs is None:
        hidden_ext = rows_around(hidden_half, 2, mover)
    else:
        joined_ext = rows_around(jnp.concatenate([hidden_half, inputs], axis=-1), 2, mover)
        hidden_ext = joined_ext[..., :width_h]
        from_inputs = conv_valid(joined_ext[..., width_h:], weight[:, width_h:, :], 0)
    gate_pair = jax.nn.sigmoid(
        conv_valid(hidden_ext, weight[:, :width_h, : 2 * width_h], 0)
        + from_inputs[..., : 2 * width_h]
    )
    update_gate = gate_pair[..., :width_h]
    reset_gate = gate_pair[..., width_h:]
    gated = (reset_gate * hidden_half.astype(jnp.float32)).astype(jnp.bfloat16)
    gated_ext = rows_around(gated, 2, mover)
    candidate = jnp.tanh(
        conv_valid(gated_ext, weight[:, :width_h, 2 * width_h :], 0)
        + from_inputs[..., 2 * width_h :]
    )
    return ((1.0 - update_gate) * hidden + update_gate * candidate, from_inputs)


GATHER_BITS = (4, 3, 2, 7, 6, 5, 1, 0)


def match_kernel(f1_ref, s_ref, w_ref, m_in, a_in, m_out, a_out):
    @pl.when(pl.program_id(0) == 0)
    def _():
        m_out[...] = m_in[...]
        a_out[...] = a_in[...]

    scores = lax.dot_general(
        f1_ref[...], s_ref[...], (((1,), (1,)), ((), ())), preferred_element_type=jnp.float32
    )
    m_old = m_out[:, 0:1]
    m_new = jnp.maximum(m_old, jnp.max(scores, axis=1, keepdims=True))
    p = jnp.exp(scores - m_new)
    shrink = jnp.exp(m_old - m_new)
    p_hi = p.astype(jnp.bfloat16)
    p_lo = (p - p_hi.astype(jnp.float32)).astype(jnp.bfloat16)
    w = w_ref[...]
    part = jnp.dot(p_hi, w, preferred_element_type=jnp.float32) + jnp.dot(
        p_lo, w, preferred_element_type=jnp.float32
    )
    a_out[...] = a_out[...] * shrink + part
    m_out[...] = jnp.broadcast_to(m_new, m_out.shape)


def match_block(state, features, block, block_rows, grid_cols):
    count, channels = block.shape
    pixels = features.shape[0]
    tile = min(count, 6144)
    strip_row = jnp.repeat(block_rows, grid_cols).astype(jnp.float32)
    strip_col = (jnp.arange(count, dtype=jnp.int32) % grid_cols).astype(jnp.float32)
    weights = jnp.concatenate(
        [
            jnp.ones((count, 1), jnp.float32),
            strip_row[:, None],
            strip_col[:, None],
            jnp.zeros((count, 125), jnp.float32),
        ],
        axis=1,
    ).astype(jnp.bfloat16)
    running_max, acc = state
    return pl.pallas_call(
        match_kernel,
        grid=(count // tile,),
        in_specs=[
            pl.BlockSpec((pixels, channels), lambda i: (0, 0)),
            pl.BlockSpec((tile, channels), lambda i: (i, 0)),
            pl.BlockSpec((tile, 128), lambda i: (i, 0)),
            pl.BlockSpec((pixels, 128), lambda i: (0, 0)),
            pl.BlockSpec((pixels, 128), lambda i: (0, 0)),
        ],
        out_specs=[
            pl.BlockSpec((pixels, 128), lambda i: (0, 0)),
            pl.BlockSpec((pixels, 128), lambda i: (0, 0)),
        ],
        out_shape=[
            jax.ShapeDtypeStruct((pixels, 128), jnp.float32),
            jax.ShapeDtypeStruct((pixels, 128), jnp.float32),
        ],
        cost_estimate=pl.CostEstimate(
            flops=2 * pixels * count * (channels + 256),
            transcendentals=pixels * count,
            bytes_accessed=2 * count * (channels + 128) + 2 * pixels * channels + 16 * pixels * 128,
        ),
    )(features, block, weights, running_max, acc)


def gather_partner(device, step, where):
    bit = GATHER_BITS[step]
    if bit != 1:
        return device ^ (1 << bit)
    z = (device >> 1) & 15
    shifted = ((((z + 15) % 16) ^ 1) + 1) % 16
    partner_z = where((device & 1) == 0, z ^ 1, shifted)
    return device - (z << 1) + (partner_z << 1)


def gather_tables(bands):
    devices = np.arange(bands, dtype=np.int64)
    rows = devices[:, None]
    for step in range(len(GATHER_BITS)):
        rows = np.concatenate([rows, rows[gather_partner(devices, step, np.where)]], axis=1)
    places = np.zeros_like(rows)
    for device in range(bands):
        places[device, rows[device]] = np.arange(rows.shape[1])
    return rows.astype(np.int16), places.astype(np.int16)


def per_device(frame1, frame2, context, hidden_init, offsets, w_motion, w_row, w_col):
    band_rows, image_width, channels = frame1.shape
    bands = lax.axis_size("band")
    total_rows = band_rows * bands
    band = lax.axis_index("band")
    row_first = band * band_rows
    strips = scaled_strips(frame2, math.sqrt(channels))
    grid_cols = strips.shape[1]
    target_row, target_col, pixel_row, pixel_col = lookup_targets(
        offsets, row_first, total_rows, image_width
    )
    pixel_count = band_rows * image_width
    features = frame1.reshape(pixel_count, channels)
    row_table, place_table = gather_tables(bands)
    state = (
        jnp.full((pixel_count, 128), -jnp.inf, jnp.float32),
        jnp.zeros((pixel_count, 128), jnp.float32),
    )
    held = strips.reshape(band_rows * grid_cols, channels)
    merged = 6
    own_rows = lax.dynamic_index_in_dim(jnp.asarray(row_table), band, 0, keepdims=False)
    for step, bit in enumerate(GATHER_BITS):
        pairs = [(i, int(gather_partner(i, step, np.where))) for i in range(bands)]
        got = lax.ppermute(held, "band", pairs)
        if step < merged:
            held = jnp.concatenate([held, got], axis=0)
            if step == merged - 1:
                start_rows = own_rows[: 1 << merged].astype(jnp.int32)
                state = match_block(state, features, held, start_rows, grid_cols)
            continue
        partner = gather_partner(band, step, jnp.where)
        got_rows = lax.dynamic_index_in_dim(
            jnp.asarray(row_table[:, : 1 << step]), partner, 0, keepdims=False
        ).astype(jnp.int32)
        settled = state
        state = match_block(state, features, got, got_rows, grid_cols)
        if step + 1 < len(GATHER_BITS):
            held = jnp.concatenate([held, got], axis=0)
            held, settled = lax.optimization_barrier((held, settled))
    running_max, acc = state
    denominator = acc[:, 0]
    flow_row = (acc[:, 1] / denominator / total_rows).reshape(
        band_rows, image_width
    ) - pixel_row.astype(jnp.float32) / total_rows
    flow_col = (
        (8.0 * (acc[:, 2] / denominator) + 3.5) / image_width
    ).reshape(band_rows, image_width) - pixel_col.astype(jnp.float32) / image_width
    places = lax.dynamic_index_in_dim(jnp.asarray(place_table), band, 0, keepdims=False)
    t_row = target_row.reshape(pixel_count)
    t_col = target_col.reshape(pixel_count)
    valid = t_row >= 0
    place = places.astype(jnp.int32)[jnp.where(valid, t_row, 0)] * grid_cols + jnp.where(
        valid, t_col, 0
    )
    half = held.shape[0]
    picked = jnp.where(
        (place < half)[:, None],
        jnp.take(held, jnp.minimum(place, half - 1), axis=0),
        jnp.take(got, jnp.maximum(place - half, 0), axis=0),
    )
    found = jnp.sum(features.astype(jnp.float32) * picked.astype(jnp.float32), axis=1)
    lookup = jnp.where(valid, found, 0.0)
    lookup = lookup.reshape(band_rows, image_width)
    motion = jax.nn.relu(
        flow_row[..., None] * w_motion[0]
        + flow_col[..., None] * w_motion[1]
        + lookup[..., None] * w_motion[2]
    ).astype(jnp.bfloat16)
    inputs = jnp.concatenate([context, motion], axis=-1)
    width_h = hidden_init.shape[-1]
    from_row = conv_valid(pad_columns(inputs), w_row[:, width_h:, :], 1)
    hidden = hidden_init.astype(jnp.float32)
    from_col = None
    for iteration in range(ITERS):
        hidden = row_pass(hidden, from_row, w_row)
        hidden, from_col = column_pass_each(
            hidden, from_col, w_col, inputs if iteration == 0 else None
        )
    return (hidden, jnp.stack([flow_row, flow_col]))


def solution(mesh):
    return jax.shard_map(
        per_device,
        mesh=mesh,
        in_specs=(
            P("band", "pair", None),
            P("band", "pair", None),
            P("band", "pair", None),
            P("band", "pair", None),
            P(None, "band", "pair"),
            P(),
            P(),
            P(),
        ),
        out_specs=(P("band", "pair", None), P(None, "band", "pair")),
        check_vma=False,
    )
```

```python
import math

import numpy as np

import jax
import jax.numpy as jnp
from jax import lax
from jax.experimental import pallas as pl
from jax.sharding import PartitionSpec as P

ITERS = 2


def passed_along(array, axis, by):
    count = lax.axis_size(axis)
    pairs = [(i, i + by) for i in range(count) if 0 <= i + by < count]
    return lax.ppermute(array, axis, pairs)


def pool_strips(frame2):
    band_rows, image_width, channels = frame2.shape
    blocks = frame2.astype(jnp.float32).reshape(band_rows, image_width // 8, 8, channels)
    return (jnp.sum(blocks, axis=2) / 2.0).astype(jnp.bfloat16)


def scaled_strips(frame2, scale):
    band_rows, image_width, channels = frame2.shape
    blocks = frame2.astype(jnp.float32).reshape(band_rows, image_width // 8, 8, channels)
    return (jnp.sum(blocks, axis=2) / (2.0 * scale)).astype(jnp.bfloat16)


def lookup_targets(offsets, row_first, total_rows, image_width):
    band_rows = offsets.shape[1]
    pixel_row = (
        row_first
        + jnp.arange(band_rows, dtype=jnp.int32)[:, None]
        + jnp.zeros((1, image_width), jnp.int32)
    )
    pixel_col = jnp.arange(image_width, dtype=jnp.int32)[None, :]
    target_row = pixel_row + offsets[0]
    target_col = pixel_col // 8 + offsets[1]
    inside = (
        (target_row >= 0)
        & (target_row < total_rows)
        & (target_col >= 0)
        & (target_col < image_width // 8)
    )
    target_row = jnp.where(inside, target_row, -1)
    target_col = jnp.where(inside, target_col, -1)
    return (target_row, target_col, pixel_row, pixel_col)


def strip_step(
    state, feature_rows, strip_block, row_zero, total_rows, image_width, target_row, target_col
):
    block_rows, grid_cols, channels = strip_block.shape
    scores = jnp.dot(
        feature_rows,
        strip_block.reshape(block_rows * grid_cols, channels).T,
        preferred_element_type=jnp.float32,
    ) / math.sqrt(channels)
    running_max, denominator, acc_row, acc_col, lookup = state
    new_max = jnp.maximum(running_max, jnp.max(scores, axis=1))
    shrink = jnp.exp(running_max - new_max)
    exponent = jnp.exp(scores - new_max[:, None]).reshape(-1, block_rows, grid_cols)
    strip_row = row_zero + jnp.arange(block_rows, dtype=jnp.int32)
    column_ids = jnp.arange(grid_cols, dtype=jnp.int32)
    row_centre = strip_row.astype(jnp.float32) / total_rows
    col_centre = ((8 * column_ids).astype(jnp.float32) + 3.5) / image_width
    row_weight = jnp.sum(exponent, axis=2)
    col_weight = jnp.sum(exponent, axis=1)
    scores_grid = scores.reshape(-1, block_rows, grid_cols)
    hit = (strip_row[None, :, None] == target_row[:, None, None]) & (
        column_ids[None, None, :] == target_col[:, None, None]
    )
    found = jnp.sum(jnp.where(hit, scores_grid, 0.0), axis=(1, 2))
    return (
        new_max,
        denominator * shrink + jnp.sum(row_weight, axis=1),
        acc_row * shrink + jnp.sum(row_weight * row_centre[None, :], axis=1),
        acc_col * shrink + jnp.sum(col_weight * col_centre[None, :], axis=1),
        lookup + found,
    )


def conv_valid(source, weight, conv_axis):
    out_count = source.shape[conv_axis] - 4
    summed = None
    for kernel_tap in range(5):
        tap_slice = lax.slice_in_dim(source, kernel_tap, kernel_tap + out_count, axis=conv_axis)
        tap_term = jnp.dot(
            tap_slice.reshape(-1, tap_slice.shape[-1]),
            weight[kernel_tap],
            preferred_element_type=jnp.float32,
        )
        summed = tap_term if summed is None else summed + tap_term
    out_shape = tuple(tap_slice.shape[:-1]) + (weight.shape[-1],)
    return summed.reshape(out_shape)


def pad_columns(source):
    return jnp.pad(source, ((0, 0), (2, 2), (0, 0)))


def rows_around(source, depth, mover):
    above = [
        mover(source, offset)
        for offset in list(range(depth, 0, -1)) + list(range(-1, -depth - 1, -1))
    ]
    return jnp.concatenate(above[:depth] + [source] + above[depth:], axis=0)


def row_pass(hidden, from_inputs, weight):
    width_h = hidden.shape[-1]
    hidden_half = lax.optimization_barrier(hidden.astype(jnp.bfloat16))
    gate_pair = jax.nn.sigmoid(
        conv_valid(pad_columns(hidden_half), weight[:, :width_h, : 2 * width_h], 1)
        + from_inputs[..., : 2 * width_h]
    )
    update_gate = gate_pair[..., :width_h]
    reset_gate = gate_pair[..., width_h:]
    gated = (reset_gate * hidden_half.astype(jnp.float32)).astype(jnp.bfloat16)
    candidate = jnp.tanh(
        conv_valid(pad_columns(gated), weight[:, :width_h, 2 * width_h :], 1)
        + from_inputs[..., 2 * width_h :]
    )
    return (1.0 - update_gate) * hidden + update_gate * candidate


def column_pass_each(hidden, from_inputs, weight, inputs=None):
    width_h = hidden.shape[-1]
    hidden_half = lax.optimization_barrier(hidden.astype(jnp.bfloat16))
    mover = lambda source, offset: passed_along(source, "band", offset)
    if inputs is None:
        hidden_ext = rows_around(hidden_half, 2, mover)
    else:
        joined_ext = rows_around(jnp.concatenate([hidden_half, inputs], axis=-1), 2, mover)
        hidden_ext = joined_ext[..., :width_h]
        from_inputs = conv_valid(joined_ext[..., width_h:], weight[:, width_h:, :], 0)
    gate_pair = jax.nn.sigmoid(
        conv_valid(hidden_ext, weight[:, :width_h, : 2 * width_h], 0)
        + from_inputs[..., : 2 * width_h]
    )
    update_gate = gate_pair[..., :width_h]
    reset_gate = gate_pair[..., width_h:]
    gated = (reset_gate * hidden_half.astype(jnp.float32)).astype(jnp.bfloat16)
    gated_ext = rows_around(gated, 2, mover)
    candidate = jnp.tanh(
        conv_valid(gated_ext, weight[:, :width_h, 2 * width_h :], 0)
        + from_inputs[..., 2 * width_h :]
    )
    return ((1.0 - update_gate) * hidden + update_gate * candidate, from_inputs)


GATHER_BITS = (4, 3, 2, 6, 7, 5, 1, 0)


def match_kernel(f1_ref, s_ref, w_ref, m_in, a_in, m_out, a_out):
    @pl.when(pl.program_id(0) == 0)
    def _():
        m_out[...] = m_in[...]
        a_out[...] = a_in[...]

    scores = lax.dot_general(
        f1_ref[...], s_ref[...], (((1,), (1,)), ((), ())), preferred_element_type=jnp.float32
    )
    m_old = m_out[:, 0:1]
    m_new = jnp.maximum(m_old, jnp.max(scores, axis=1, keepdims=True))
    p = jnp.exp(scores - m_new)
    shrink = jnp.exp(m_old - m_new)
    p_hi = p.astype(jnp.bfloat16)
    p_lo = (p - p_hi.astype(jnp.float32)).astype(jnp.bfloat16)
    w = w_ref[...]
    part = jnp.dot(p_hi, w, preferred_element_type=jnp.float32) + jnp.dot(
        p_lo, w, preferred_element_type=jnp.float32
    )
    a_out[...] = a_out[...] * shrink + part
    m_out[...] = jnp.broadcast_to(m_new, m_out.shape)


def match_block(state, features, block, block_rows, grid_cols):
    count, channels = block.shape
    pixels = features.shape[0]
    tile = min(count, 6144)
    strip_row = jnp.repeat(block_rows, grid_cols).astype(jnp.float32)
    strip_col = (jnp.arange(count, dtype=jnp.int32) % grid_cols).astype(jnp.float32)
    weights = jnp.concatenate(
        [
            jnp.ones((count, 1), jnp.float32),
            strip_row[:, None],
            strip_col[:, None],
            jnp.zeros((count, 125), jnp.float32),
        ],
        axis=1,
    ).astype(jnp.bfloat16)
    running_max, acc = state
    return pl.pallas_call(
        match_kernel,
        grid=(count // tile,),
        in_specs=[
            pl.BlockSpec((pixels, channels), lambda i: (0, 0)),
            pl.BlockSpec((tile, channels), lambda i: (i, 0)),
            pl.BlockSpec((tile, 128), lambda i: (i, 0)),
            pl.BlockSpec((pixels, 128), lambda i: (0, 0)),
            pl.BlockSpec((pixels, 128), lambda i: (0, 0)),
        ],
        out_specs=[
            pl.BlockSpec((pixels, 128), lambda i: (0, 0)),
            pl.BlockSpec((pixels, 128), lambda i: (0, 0)),
        ],
        out_shape=[
            jax.ShapeDtypeStruct((pixels, 128), jnp.float32),
            jax.ShapeDtypeStruct((pixels, 128), jnp.float32),
        ],
        cost_estimate=pl.CostEstimate(
            flops=2 * pixels * count * (channels + 256),
            transcendentals=pixels * count,
            bytes_accessed=2 * count * (channels + 128) + 2 * pixels * channels + 16 * pixels * 128,
        ),
    )(features, block, weights, running_max, acc)


def gather_partner(device, step, where):
    bit = GATHER_BITS[step]
    if bit != 1:
        return device ^ (1 << bit)
    z = (device >> 1) & 15
    shifted = ((((z + 15) % 16) ^ 1) + 1) % 16
    partner_z = where((device & 1) == 0, z ^ 1, shifted)
    return device - (z << 1) + (partner_z << 1)


def gather_tables(bands):
    devices = np.arange(bands, dtype=np.int64)
    rows = devices[:, None]
    for step in range(len(GATHER_BITS)):
        rows = np.concatenate([rows, rows[gather_partner(devices, step, np.where)]], axis=1)
    places = np.zeros_like(rows)
    for device in range(bands):
        places[device, rows[device]] = np.arange(rows.shape[1])
    return rows.astype(np.int16), places.astype(np.int16)


def per_device(frame1, frame2, context, hidden_init, offsets, w_motion, w_row, w_col):
    band_rows, image_width, channels = frame1.shape
    bands = lax.axis_size("band")
    total_rows = band_rows * bands
    band = lax.axis_index("band")
    row_first = band * band_rows
    strips = scaled_strips(frame2, math.sqrt(channels))
    grid_cols = strips.shape[1]
    target_row, target_col, pixel_row, pixel_col = lookup_targets(
        offsets, row_first, total_rows, image_width
    )
    pixel_count = band_rows * image_width
    features = frame1.reshape(pixel_count, channels)
    row_table, place_table = gather_tables(bands)
    state = (
        jnp.full((pixel_count, 128), -jnp.inf, jnp.float32),
        jnp.zeros((pixel_count, 128), jnp.float32),
    )
    held = strips.reshape(band_rows * grid_cols, channels)
    merged = 6
    own_rows = lax.dynamic_index_in_dim(jnp.asarray(row_table), band, 0, keepdims=False)
    for step, bit in enumerate(GATHER_BITS):
        pairs = [(i, int(gather_partner(i, step, np.where))) for i in range(bands)]
        got = lax.ppermute(held, "band", pairs)
        if step < merged:
            held = jnp.concatenate([held, got], axis=0)
            if step == merged - 1:
                start_rows = own_rows[: 1 << merged].astype(jnp.int32)
                state = match_block(state, features, held, start_rows, grid_cols)
            continue
        partner = gather_partner(band, step, jnp.where)
        got_rows = lax.dynamic_index_in_dim(
            jnp.asarray(row_table[:, : 1 << step]), partner, 0, keepdims=False
        ).astype(jnp.int32)
        settled = state
        state = match_block(state, features, got, got_rows, grid_cols)
        if step + 1 < len(GATHER_BITS):
            held = jnp.concatenate([held, got], axis=0)
            held, settled = lax.optimization_barrier((held, settled))
    running_max, acc = state
    denominator = acc[:, 0]
    flow_row = (acc[:, 1] / denominator / total_rows).reshape(
        band_rows, image_width
    ) - pixel_row.astype(jnp.float32) / total_rows
    flow_col = (
        (8.0 * (acc[:, 2] / denominator) + 3.5) / image_width
    ).reshape(band_rows, image_width) - pixel_col.astype(jnp.float32) / image_width
    places = lax.dynamic_index_in_dim(jnp.asarray(place_table), band, 0, keepdims=False)
    t_row = target_row.reshape(pixel_count)
    t_col = target_col.reshape(pixel_count)
    valid = t_row >= 0
    place = places.astype(jnp.int32)[jnp.where(valid, t_row, 0)] * grid_cols + jnp.where(
        valid, t_col, 0
    )
    half = held.shape[0]
    picked = jnp.where(
        (place < half)[:, None],
        jnp.take(held, jnp.minimum(place, half - 1), axis=0),
        jnp.take(got, jnp.maximum(place - half, 0), axis=0),
    )
    found = jnp.sum(features.astype(jnp.float32) * picked.astype(jnp.float32), axis=1)
    lookup = jnp.where(valid, found, 0.0)
    lookup = lookup.reshape(band_rows, image_width)
    motion = jax.nn.relu(
        flow_row[..., None] * w_motion[0]
        + flow_col[..., None] * w_motion[1]
        + lookup[..., None] * w_motion[2]
    ).astype(jnp.bfloat16)
    inputs = jnp.concatenate([context, motion], axis=-1)
    width_h = hidden_init.shape[-1]
    from_row = conv_valid(pad_columns(inputs), w_row[:, width_h:, :], 1)
    hidden = hidden_init.astype(jnp.float32)
    from_col = None
    for iteration in range(ITERS):
        hidden = row_pass(hidden, from_row, w_row)
        hidden, from_col = column_pass_each(
            hidden, from_col, w_col, inputs if iteration == 0 else None
        )
    return (hidden, jnp.stack([flow_row, flow_col]))


def solution(mesh):
    return jax.shard_map(
        per_device,
        mesh=mesh,
        in_specs=(
            P("band", "pair", None),
            P("band", "pair", None),
            P("band", "pair", None),
            P("band", "pair", None),
            P(None, "band", "pair"),
            P(),
            P(),
            P(),
        ),
        out_specs=(P("band", "pair", None), P(None, "band", "pair")),
        check_vma=False,
    )
```
